32 devices in a mesh: win: 4 (over y, core), pair: 8 (over z, x).
Axes of the slice: x: 2, y: 2, z: 4, core: 2. Of those that a mesh axis runs over, the one named last changes fastest.
Arguments:
- strain: bfloat16 [4, 2048, 7680], P('win', 'pair'), may hold values from -40 to 40
- pair_list: int32 [32, 2], replicated, may hold values from 0 to 15, as said below
- tile_live: int32 [32], P('pair'), may hold values 0 or 1
Outputs:
- stack: float32 [128, 32, 16, 128], P('win', 'pair')
The draws below stay inside these ranges and needn't reach their ends.
Inputs may be any that keep to these rules, and one draw needn't show every extreme that they name: `pair_list`: rows q * 4 to (q + 1) * 4 - 1 are the tiles of owner q; the 8 block numbers in them fall into distinct groups of 2 consecutive blocks.
All inputs are finite; a program needn't handle non-finite values. No bound on the sum of `tile_live` on one device may be relied on, other than what follows from the above.
Results may differ from the reference program's by a relative error of at most 0.02.
Values may be sent and summed in bfloat16 or wider, within the bound.
No kernel may reach another device: no remote copies, remote signals or barrier semaphores. Data moves between devices by JAX's collectives and lax.ppermute only.
A program may use at most 64 MiB of HBM per device.

```python
import math
import jax
import jax.numpy as jnp
from jax import lax

C = 128
S = 7680
F = 384
LAGS = 16
DECIM = 32
B_DEV = 2
W_DEV = 1
TILE_SLOTS = 4
WINDOWS = 4
BLOCKS = 16
CHANNELS = 2048
TILES = 32


def draw_strain(key, part):

    def one_window(window_index):
        window_key = jax.random.fold_in(key, window_index)
        scale_draw = jax.random.uniform(jax.random.fold_in(window_key, 1), (CHANNELS, 1), jnp.float32, 0.0, 1.0)
        chan_scale = jnp.exp(math.log(10.0) * scale_draw)
        noise = jax.random.truncated_normal(jax.random.fold_in(window_key, 2), -5.0, 5.0, (CHANNELS, S), jnp.float32)
        signal = noise * chan_scale
        sample_index = lax.iota(jnp.int32, S)
        for line_index in range(6):
            line_key = jax.random.fold_in(window_key, 10 + line_index)
            line_bin = jax.random.randint(jax.random.fold_in(line_key, 1), (CHANNELS, 1), 1, F + 1)
            line_phase = jax.random.uniform(jax.random.fold_in(line_key, 2), (CHANNELS, 1), jnp.float32, 0.0, 2.0 * math.pi)
            line_amp = jnp.exp(jax.random.uniform(jax.random.fold_in(line_key, 3), (CHANNELS, 1), jnp.float32, math.log(0.03), math.log(0.3))) * chan_scale
            product = line_bin * sample_index[None, :] % S
            signal = signal + line_amp * jnp.cos(2.0 * math.pi / S * product.astype(jnp.float32) + line_phase)
        return jnp.clip(signal, -40.0, 40.0)
    return lax.map(one_window, jnp.arange(WINDOWS, dtype=jnp.int32)).astype(jnp.bfloat16)


def draw_pair_list(key, part):
    owner_count = TILES // TILE_SLOTS
    group_count = BLOCKS // B_DEV
    owner_keys = jax.random.split(jax.random.fold_in(key, 11), owner_count)
    chosen = jax.vmap(lambda owner_key: jax.random.permutation(owner_key, group_count)[:2 * TILE_SLOTS])(owner_keys)
    within = jax.random.randint(jax.random.fold_in(key, 12), (owner_count, 2 * TILE_SLOTS), 0, B_DEV)
    block_ids = chosen.astype(jnp.int32) * B_DEV + within.astype(jnp.int32)
    return block_ids.reshape(TILES, 2).astype(jnp.int32)


def touch_ends(array, key, least, high):
    longest = array.shape.index(max(array.shape))
    spots = []
    for shift in (0, 1):
        where = [jax.random.randint(jax.random.fold_in(key, axis), (), 0, length) for axis, length in enumerate(array.shape)]
        where[longest] = (where[longest] + shift) % array.shape[longest]
        spots.append(tuple(where))
    return array.at[spots[0]].set(least).at[spots[1]].set(high)


def setup_inputs(seed: int = 0) -> dict:
    splits = jax.random.split(jax.random.key(seed), 4)
    strain = draw_strain(jax.random.fold_in(splits[3], 71), 0)
    pair_list = draw_pair_list(jax.random.fold_in(splits[3], 71), 0)
    tile_live = touch_ends((jax.random.randint(splits[2], (TILES,), 0, 4) < 3).astype(jnp.int32), jax.random.fold_in(splits[2], 1), 0, 1)
    return {"strain": strain, "pair_list": pair_list, "tile_live": tile_live}


def dft_piece(first_row, row_count, sample_count, bin_count):
    sample_index = first_row + lax.iota(jnp.int32, row_count)
    bin_index = lax.iota(jnp.int32, bin_count) + 1
    product = sample_index[:, None] * bin_index[None, :] % sample_count
    angle = 2.0 * math.pi / sample_count * product.astype(jnp.float32)
    return jnp.concatenate([jnp.cos(angle), -jnp.sin(angle)], axis=1).astype(jnp.bfloat16)

def lag_tables(sample_count, bin_count, lag_count, stride):
    bin_index = lax.iota(jnp.int32, bin_count) + 1
    lag_shift = (lax.iota(jnp.int32, lag_count) - lag_count // 2) * stride
    product = bin_index[:, None] * lag_shift[None, :] % sample_count
    angle = 2.0 * math.pi / sample_count * product.astype(jnp.float32)
    return (jnp.cos(angle), jnp.sin(angle))

def whiten_spectrum(spectrum, bin_count):
    real_part = spectrum[:, :bin_count]
    imag_part = spectrum[:, bin_count:]
    amplitude = jnp.sqrt(real_part * real_part + imag_part * imag_part)
    level = 0.2 * lax.optimization_barrier(jnp.mean(amplitude, axis=1, keepdims=True)) + 1e-06
    divisor = jnp.maximum(amplitude, level)
    return jnp.concatenate([real_part / divisor, imag_part / divisor], axis=1).astype(jnp.bfloat16)

def shift_block(spectrum_block, cos_lag, sin_lag):
    bin_count = cos_lag.shape[0]
    real_part = spectrum_block[:, :bin_count].astype(jnp.float32).T
    imag_part = spectrum_block[:, bin_count:].astype(jnp.float32).T
    upper_half = real_part[:, None, :] * cos_lag[:, :, None] + imag_part[:, None, :] * sin_lag[:, :, None]
    lower_half = imag_part[:, None, :] * cos_lag[:, :, None] - real_part[:, None, :] * sin_lag[:, :, None]
    joined = jnp.concatenate([upper_half, lower_half], axis=0).astype(jnp.bfloat16)
    return joined.reshape(2 * bin_count, -1)

def reference(strain, pair_list, tile_live):
    cos_lag, sin_lag = lag_tables(S, F, LAGS, DECIM)
    dft_full = dft_piece(0, S, S, F).astype(jnp.float32)

    def whiten_window(window_rows):
        spectrum = jnp.dot(window_rows.astype(jnp.float32), dft_full, precision=lax.Precision.HIGHEST)
        return whiten_spectrum(spectrum, F)
    whitened = lax.map(whiten_window, strain)
    block_spectra = whitened.reshape(WINDOWS, BLOCKS, C, 2 * F)

    def one_tile(tile_index):
        first_block = pair_list[tile_index, 0]
        second_block = pair_list[tile_index, 1]
        left_all = jnp.take(block_spectra, first_block, axis=1)
        right_all = jnp.take(block_spectra, second_block, axis=1)

        def one_window(operands):
            left_rows, right_rows = operands
            shifted = shift_block(right_rows, cos_lag, sin_lag)
            return jnp.dot(left_rows.astype(jnp.float32), shifted.astype(jnp.float32), precision=lax.Precision.HIGHEST)
        correlation = lax.map(one_window, (left_all, right_all))
        grouped = lax.optimization_barrier(jnp.sum(correlation.reshape(WINDOWS // W_DEV, W_DEV, C, LAGS * C), axis=1))
        rounded = lax.optimization_barrier(grouped.astype(jnp.bfloat16)).astype(jnp.float32)
        summed = lax.optimization_barrier(jnp.sum(rounded, axis=0))
        return summed * tile_live[tile_index].astype(jnp.float32) / math.sqrt(F * WINDOWS)
    stacks = lax.map(one_tile, jnp.arange(TILES, dtype=jnp.int32))
    return jnp.transpose(stacks.reshape(TILES, C, LAGS, C), (1, 0, 2, 3))
```

```python
import math

import jax
import jax.numpy as jnp
from jax import lax
from jax.sharding import PartitionSpec as P

C = 128
F = 384
LAGS = 16
DECIM = 32
SPLIT = 128


def cos_sin(product, sample_count):
    angle = 2.0 * math.pi / sample_count * (product % sample_count).astype(jnp.float32)
    return jnp.cos(angle), jnp.sin(angle)


def dft_table(sample_count, bin_count):
    bin_index = lax.iota(jnp.int32, bin_count) + 1
    coarse = lax.iota(jnp.int32, sample_count // SPLIT) * SPLIT
    fine = lax.iota(jnp.int32, SPLIT)
    ca, sa = cos_sin(coarse[:, None] * bin_index[None, :], sample_count)
    cb, sb = cos_sin(fine[:, None] * bin_index[None, :], sample_count)
    cos_t = ca[:, None, :] * cb[None, :, :] - sa[:, None, :] * sb[None, :, :]
    sin_t = sa[:, None, :] * cb[None, :, :] + ca[:, None, :] * sb[None, :, :]
    table = jnp.concatenate([cos_t, -sin_t], axis=2).astype(jnp.bfloat16)
    return table.reshape(sample_count, 2 * bin_count)


def whiten_rows(strain_rows, bin_count):
    sample_count = strain_rows.shape[1]
    spectrum = jnp.dot(strain_rows, dft_table(sample_count, bin_count), preferred_element_type=jnp.float32)
    real_part = spectrum[:, :bin_count]
    imag_part = spectrum[:, bin_count:]
    amplitude = jnp.sqrt(real_part * real_part + imag_part * imag_part)
    level = 0.2 * jnp.mean(amplitude, axis=1, keepdims=True) + 1e-06
    divisor = jnp.maximum(amplitude, level)
    return jnp.concatenate([real_part / divisor, imag_part / divisor], axis=1).astype(jnp.bfloat16)


def rotate(block, cos_r, sin_r):
    re = block[..., :F].astype(jnp.float32)[None]
    im = block[..., F:].astype(jnp.float32)[None]
    shape = (cos_r.shape[0],) + (1,) * (block.ndim - 1) + (F,)
    c = cos_r.reshape(shape)
    s = sin_r.reshape(shape)
    return jnp.concatenate([re * c - im * s, re * s + im * c], axis=-1).astype(jnp.bfloat16)


def body(strain, pair_list, tile_live):
    window_count, local_rows, sample_count = strain.shape
    slot_count = tile_live.shape[0]
    n_pair = lax.axis_size("pair")
    n_win = lax.axis_size("win")
    pair_here = lax.axis_index("pair")
    win_here = lax.axis_index("win")
    b_dev = local_rows // C

    flat_rows = strain.reshape(window_count * local_rows, sample_count)
    whitened = whiten_rows(flat_rows, F).reshape(window_count, b_dev, C, 2 * F)

    lists = pair_list.reshape(n_pair, 2 * slot_count)
    mine = (lists // b_dev) == pair_here
    local_pick = jnp.sum(jnp.where(mine, lists % b_dev, 0), axis=1)
    outgoing = jnp.take(jnp.transpose(whitened, (1, 0, 2, 3)), local_pick, axis=0)
    incoming = lax.all_to_all(outgoing, "pair", 0, 0, tiled=True)
    wanted = lax.dynamic_slice_in_dim(pair_list, pair_here * slot_count, slot_count, 0)
    left = jnp.take(incoming, wanted[:, 0] // b_dev, axis=0)
    right = jnp.take(incoming, wanted[:, 1] // b_dev, axis=0)

    sub = 4
    bins = lax.iota(jnp.int32, F) + 1
    fine_lag = lax.iota(jnp.int32, sub) * DECIM
    coarse_lag = (lax.iota(jnp.int32, LAGS // sub) * sub - LAGS // 2) * DECIM
    cf, sf = cos_sin(fine_lag[:, None] * bins[None, :], sample_count)
    cc, sc = cos_sin(coarse_lag[:, None] * bins[None, :], sample_count)
    left_t = rotate(left, cc, sc)
    right_t = rotate(right, cf, -sf)
    corr = jnp.einsum("atwic,btwjc->tiawbj", left_t, right_t, preferred_element_type=jnp.float32)
    corr = jnp.sum(corr, axis=3)
    corr = corr.reshape(slot_count, C, LAGS * C).astype(jnp.bfloat16)

    own_rows = C // n_win
    n_y = n_win // 2
    core = win_here % 2
    y_here = win_here // 2
    parts = jnp.transpose(corr.reshape(slot_count, n_y, 2, own_rows, LAGS * C), (1, 2, 3, 0, 4))
    send = jnp.take(parts, 1 - core, axis=1)
    keep = jnp.take(parts, core, axis=1).astype(jnp.float32)
    got = lax.ppermute(send, "win", [(w, w ^ 1) for w in range(n_win)])
    half = keep + got.astype(jnp.float32)
    total = jnp.take(half, y_here, axis=0)
    for shift in range(1, n_y):
        dest = (y_here + shift) % n_y
        piece = jnp.take(half, dest, axis=0).astype(jnp.bfloat16)
        perm = [(w, ((w // 2 + shift) % n_y) * 2 + w % 2) for w in range(n_win)]
        total = total + lax.ppermute(piece, "win", perm).astype(jnp.float32)

    live_local = tile_live.astype(jnp.float32)
    output = total * live_local[None, :, None] / math.sqrt(F * window_count * n_win)
    return output.reshape(own_rows, slot_count, LAGS, C)


def solution(mesh):
    in_specs = (P("win", "pair", None), P(), P("pair"))
    out_specs = P("win", "pair", None, None)
    return jax.shard_map(body, mesh=mesh, in_specs=in_specs, out_specs=out_specs, check_vma=False)
```

```python
import functools
import math

import jax
import jax.numpy as jnp
from jax import lax
from jax.experimental import pallas as pl
from jax.experimental.pallas import tpu as pltpu
from jax.sharding import PartitionSpec as P

C = 128
F = 384
LAGS = 16
DECIM = 32
SPLIT = 128


def cos_sin(product, sample_count):
    angle = 2.0 * math.pi / sample_count * (product % sample_count).astype(jnp.float32)
    return jnp.cos(angle), jnp.sin(angle)


def dft_table(sample_count, bin_count):
    bin_index = lax.iota(jnp.int32, bin_count) + 1
    coarse = lax.iota(jnp.int32, sample_count // SPLIT) * SPLIT
    fine = lax.iota(jnp.int32, SPLIT)
    ca, sa = cos_sin(coarse[:, None] * bin_index[None, :], sample_count)
    cb, sb = cos_sin(fine[:, None] * bin_index[None, :], sample_count)
    cos_t = ca[:, None, :] * cb[None, :, :] - sa[:, None, :] * sb[None, :, :]
    sin_t = sa[:, None, :] * cb[None, :, :] + ca[:, None, :] * sb[None, :, :]
    table = jnp.concatenate([cos_t, -sin_t], axis=2).astype(jnp.bfloat16)
    return table.reshape(sample_count, 2 * bin_count)


def whiten_rows(strain_rows, bin_count):
    sample_count = strain_rows.shape[1]
    spectrum = jnp.dot(strain_rows, dft_table(sample_count, bin_count), preferred_element_type=jnp.float32)
    real_part = spectrum[:, :bin_count]
    imag_part = spectrum[:, bin_count:]
    amplitude = jnp.sqrt(real_part * real_part + imag_part * imag_part)
    level = 0.2 * jnp.mean(amplitude, axis=1, keepdims=True) + 1e-06
    divisor = jnp.maximum(amplitude, level)
    return jnp.concatenate([real_part / divisor, imag_part / divisor], axis=1).astype(jnp.bfloat16)


def correlation_kernel(sub, cc_ref, sc_ref, cf_ref, sf_ref, left_ref, right_ref, out_ref):
    window_count = left_ref.shape[1]
    acc = None
    for w in range(window_count):
        lre = left_ref[0, w, :, :F].astype(jnp.float32)
        lim = left_ref[0, w, :, F:].astype(jnp.float32)
        rre = right_ref[0, w, :, :F].astype(jnp.float32)
        rim = right_ref[0, w, :, F:].astype(jnp.float32)
        turned = []
        for l1 in range(sub):
            c = cf_ref[l1 : l1 + 1, :]
            s = sf_ref[l1 : l1 + 1, :]
            turned.append(jnp.concatenate([rre * c + rim * s, rim * c - rre * s], axis=1).astype(jnp.bfloat16))
        right_all = jnp.concatenate(turned, axis=0)
        parts = []
        for l2 in range(LAGS // sub):
            c = cc_ref[l2 : l2 + 1, :]
            s = sc_ref[l2 : l2 + 1, :]
            left_t = jnp.concatenate([lre * c - lim * s, lre * s + lim * c], axis=1).astype(jnp.bfloat16)
            parts.append(
                lax.dot_general(left_t, right_all, (((1,), (1,)), ((), ())), preferred_element_type=jnp.float32)
            )
        acc = parts if acc is None else [a + p for a, p in zip(acc, parts)]
    for l2, res in enumerate(acc):
        for l1 in range(sub):
            out_ref[:, 0, l2 * sub + l1, :] = res[:, l1 * C : (l1 + 1) * C].astype(out_ref.dtype)


def tile_correlation(cc, sc, cf, sf, left, right, sub):
    slot_count, window_count = left.shape[:2]
    table_spec = pl.BlockSpec(cc.shape, lambda t: (0, 0))
    block_spec = pl.BlockSpec((1, window_count, C, 2 * F), lambda t: (t, 0, 0, 0))
    flops = 2 * slot_count * window_count * C * 2 * F * LAGS * C
    return pl.pallas_call(
        functools.partial(correlation_kernel, sub),
        grid=(slot_count,),
        in_specs=[table_spec] * 4 + [block_spec] * 2,
        out_specs=pl.BlockSpec((C, 1, LAGS, C), lambda t: (0, t, 0, 0)),
        out_shape=jax.ShapeDtypeStruct((C, slot_count, LAGS, C), jnp.bfloat16),
        cost_estimate=pl.CostEstimate(
            flops=flops, transcendentals=0, bytes_accessed=slot_count * (4 * window_count * C * F * 2 + 2 * C * LAGS * C)
        ),
    )(cc, sc, cf, sf, left, right)


def body(strain, pair_list, tile_live):
    window_count, local_rows, sample_count = strain.shape
    slot_count = tile_live.shape[0]
    n_pair = lax.axis_size("pair")
    n_win = lax.axis_size("win")
    pair_here = lax.axis_index("pair")
    win_here = lax.axis_index("win")
    b_dev = local_rows // C

    flat_rows = strain.reshape(window_count * local_rows, sample_count)
    whitened = whiten_rows(flat_rows, F).reshape(window_count, b_dev, C, 2 * F)

    lists = pair_list.reshape(n_pair, 2 * slot_count)
    mine = (lists // b_dev) == pair_here
    local_pick = jnp.sum(jnp.where(mine, lists % b_dev, 0), axis=1)
    outgoing = jnp.take(jnp.transpose(whitened, (1, 0, 2, 3)), local_pick, axis=0)
    incoming = lax.all_to_all(outgoing, "pair", 0, 0, tiled=True)
    wanted = lax.dynamic_slice_in_dim(pair_list, pair_here * slot_count, slot_count, 0)
    left = jnp.take(incoming, wanted[:, 0] // b_dev, axis=0)
    right = jnp.take(incoming, wanted[:, 1] // b_dev, axis=0)

    sub = 4
    own_rows = C // n_win
    n_y = n_win // 2
    bins = lax.iota(jnp.int32, F) + 1
    fine_lag = lax.iota(jnp.int32, sub) * DECIM
    coarse_lag = (lax.iota(jnp.int32, LAGS // sub) * sub - LAGS // 2) * DECIM
    cf, sf = cos_sin(fine_lag[:, None] * bins[None, :], sample_count)
    cc, sc = cos_sin(coarse_lag[:, None] * bins[None, :], sample_count)
    left = left.reshape(slot_count, window_count, n_y, 2, own_rows, 2 * F)
    left = jnp.transpose(left, (0, 1, 3, 2, 4, 5)).reshape(slot_count, window_count, C, 2 * F)
    corr = tile_correlation(cc, sc, cf, sf, left, right, sub)

    core = win_here % 2
    y_here = win_here // 2
    parts = corr.reshape(2, n_y, own_rows, slot_count, LAGS, C)
    send = jnp.take(parts, 1 - core, axis=0)
    keep = jnp.take(parts, core, axis=0).astype(jnp.float32)
    got = lax.ppermute(send, "win", [(w, w ^ 1) for w in range(n_win)])
    half = keep + got.astype(jnp.float32)
    total = jnp.take(half, y_here, axis=0)
    for shift in range(1, n_y):
        dest = (y_here + shift) % n_y
        piece = jnp.take(half, dest, axis=0).astype(jnp.bfloat16)
        perm = [(w, ((w // 2 + shift) % n_y) * 2 + w % 2) for w in range(n_win)]
        total = total + lax.ppermute(piece, "win", perm).astype(jnp.float32)

    live_local = tile_live.astype(jnp.float32)
    return total * live_local[None, :, None, None] / math.sqrt(F * window_count * n_win)


def solution(mesh):
    in_specs = (P("win", "pair", None), P(), P("pair"))
    out_specs = P("win", "pair", None, None)
    return jax.shard_map(body, mesh=mesh, in_specs=in_specs, out_specs=out_specs, check_vma=False)
```

```python
import functools
import math

import jax
import jax.numpy as jnp
from jax import lax
from jax.experimental import pallas as pl
from jax.experimental.pallas import tpu as pltpu
from jax.sharding import PartitionSpec as P

C = 128
F = 384
LAGS = 16
DECIM = 32
SPLIT = 128


def cos_sin(product, sample_count):
    angle = 2.0 * math.pi / sample_count * (product % sample_count).astype(jnp.float32)
    return jnp.cos(angle), jnp.sin(angle)


def dft_table(sample_count, bin_count):
    bin_index = lax.iota(jnp.int32, bin_count) + 1
    coarse = lax.iota(jnp.int32, sample_count // SPLIT) * SPLIT
    fine = lax.iota(jnp.int32, SPLIT)
    ca, sa = cos_sin(coarse[:, None] * bin_index[None, :], sample_count)
    cb, sb = cos_sin(fine[:, None] * bin_index[None, :], sample_count)
    cos_t = ca[:, None, :] * cb[None, :, :] - sa[:, None, :] * sb[None, :, :]
    sin_t = sa[:, None, :] * cb[None, :, :] + ca[:, None, :] * sb[None, :, :]
    table = jnp.concatenate([cos_t, -sin_t], axis=2).astype(jnp.bfloat16)
    return table.reshape(sample_count, 2 * bin_count)


def whiten_rows(strain_rows, bin_count):
    sample_count = strain_rows.shape[1]
    spectrum = jnp.dot(strain_rows, dft_table(sample_count, bin_count), preferred_element_type=jnp.float32)
    real_part = spectrum[:, :bin_count]
    imag_part = spectrum[:, bin_count:]
    amplitude = jnp.sqrt(real_part * real_part + imag_part * imag_part)
    level = 0.2 * jnp.mean(amplitude, axis=1, keepdims=True) + 1e-06
    divisor = jnp.maximum(amplitude, level)
    return jnp.concatenate([real_part / divisor, imag_part / divisor], axis=1).astype(jnp.bfloat16)


def correlation_kernel(sub, cc_ref, sc_ref, cf_ref, sf_ref, left_ref, right_ref, out_ref):
    window_count = left_ref.shape[1]
    acc = None
    for w in range(window_count):
        lre = left_ref[0, w, :, :F].astype(jnp.float32)
        lim = left_ref[0, w, :, F:].astype(jnp.float32)
        rre = right_ref[0, w, :F, :].astype(jnp.float32)
        rim = right_ref[0, w, F:, :].astype(jnp.float32)
        turned = []
        for l1 in range(sub):
            c = cf_ref[:, l1 : l1 + 1]
            s = sf_ref[:, l1 : l1 + 1]
            turned.append(jnp.concatenate([rre * c + rim * s, rim * c - rre * s], axis=0).astype(jnp.bfloat16))
        right_all = jnp.concatenate(turned, axis=1)
        parts = []
        for l2 in range(LAGS // sub):
            c = cc_ref[l2 : l2 + 1, :]
            s = sc_ref[l2 : l2 + 1, :]
            left_t = jnp.concatenate([lre * c - lim * s, lre * s + lim * c], axis=1).astype(jnp.bfloat16)
            parts.append(
                jnp.dot(left_t, right_all, preferred_element_type=jnp.float32)
            )
        acc = parts if acc is None else [a + p for a, p in zip(acc, parts)]
    for l2, res in enumerate(acc):
        for l1 in range(sub):
            out_ref[:, 0, l2 * sub + l1, :] = res[:, l1 * C : (l1 + 1) * C].astype(out_ref.dtype)


def tile_correlation(cc, sc, cf, sf, left, right, sub):
    slot_count, window_count = left.shape[:2]
    table_spec = pl.BlockSpec(cc.shape, lambda t: (0, 0))
    column_spec = pl.BlockSpec(cf.shape, lambda t: (0, 0))
    block_spec = pl.BlockSpec((1, window_count, C, 2 * F), lambda t: (t, 0, 0, 0))
    right_spec = pl.BlockSpec((1, window_count, 2 * F, C), lambda t: (t, 0, 0, 0))
    flops = 2 * slot_count * window_count * C * 2 * F * LAGS * C
    return pl.pallas_call(
        functools.partial(correlation_kernel, sub),
        grid=(slot_count,),
        in_specs=[table_spec] * 2 + [column_spec] * 2 + [block_spec, right_spec],
        out_specs=pl.BlockSpec((C, 1, LAGS, C), lambda t: (0, t, 0, 0)),
        out_shape=jax.ShapeDtypeStruct((C, slot_count, LAGS, C), jnp.bfloat16),
        cost_estimate=pl.CostEstimate(
            flops=flops, transcendentals=0, bytes_accessed=slot_count * (4 * window_count * C * F * 2 + 2 * C * LAGS * C)
        ),
    )(cc, sc, cf, sf, left, right)


def body(strain, pair_list, tile_live):
    window_count, local_rows, sample_count = strain.shape
    slot_count = tile_live.shape[0]
    n_pair = lax.axis_size("pair")
    n_win = lax.axis_size("win")
    pair_here = lax.axis_index("pair")
    win_here = lax.axis_index("win")
    b_dev = local_rows // C

    flat_rows = strain.reshape(window_count * local_rows, sample_count)
    whitened = whiten_rows(flat_rows, F).reshape(window_count, b_dev, C, 2 * F)

    lists = pair_list.reshape(n_pair, 2 * slot_count)
    mine = (lists // b_dev) == pair_here
    local_pick = jnp.sum(jnp.where(mine, lists % b_dev, 0), axis=1)
    outgoing = jnp.take(jnp.transpose(whitened, (1, 0, 2, 3)), local_pick, axis=0, mode="clip")
    incoming = lax.all_to_all(outgoing, "pair", 0, 0, tiled=True)
    wanted = lax.dynamic_slice_in_dim(pair_list, pair_here * slot_count, slot_count, 0)
    left = jnp.take(incoming, wanted[:, 0] // b_dev, axis=0, mode="clip")
    right = jnp.take(incoming, wanted[:, 1] // b_dev, axis=0, mode="clip")

    sub = 4
    own_rows = C // n_win
    n_y = n_win // 2
    bins = lax.iota(jnp.int32, F) + 1
    fine_lag = lax.iota(jnp.int32, sub) * DECIM
    coarse_lag = (lax.iota(jnp.int32, LAGS // sub) * sub - LAGS // 2) * DECIM
    cf, sf = cos_sin(fine_lag[:, None] * bins[None, :], sample_count)
    cc, sc = cos_sin(coarse_lag[:, None] * bins[None, :], sample_count)
    left = left.reshape(slot_count, window_count, n_y, 2, own_rows, 2 * F)
    left = jnp.transpose(left, (0, 1, 3, 2, 4, 5)).reshape(slot_count, window_count, C, 2 * F)
    right = jnp.swapaxes(right, 2, 3)
    corr = tile_correlation(cc, sc, cf.T, sf.T, left, right, sub)

    core = win_here % 2
    y_here = win_here // 2
    parts = corr.reshape(2, n_y, own_rows, slot_count, LAGS, C)
    send = jnp.take(parts, 1 - core, axis=0, mode="clip")
    keep = jnp.take(parts, core, axis=0, mode="clip").astype(jnp.float32)
    got = lax.ppermute(send, "win", [(w, w ^ 1) for w in range(n_win)])
    half = keep + got.astype(jnp.float32)
    total = jnp.take(half, y_here, axis=0, mode="clip")
    for shift in range(1, n_y):
        dest = (y_here + shift) % n_y
        piece = jnp.take(half, dest, axis=0, mode="clip").astype(jnp.bfloat16)
        perm = [(w, ((w // 2 + shift) % n_y) * 2 + w % 2) for w in range(n_win)]
        total = total + lax.ppermute(piece, "win", perm).astype(jnp.float32)

    live_local = tile_live.astype(jnp.float32)
    return total * live_local[None, :, None, None] / math.sqrt(F * window_count * n_win)


def solution(mesh):
    in_specs = (P("win", "pair", None), P(), P("pair"))
    out_specs = P("win", "pair", None, None)
    return jax.shard_map(body, mesh=mesh, in_specs=in_specs, out_specs=out_specs, check_vma=False)
```

```python
import functools
import math

import jax
import jax.numpy as jnp
from jax import lax
from jax.experimental import pallas as pl
from jax.experimental.pallas import tpu as pltpu
from jax.sharding import PartitionSpec as P

C = 128
F = 384
LAGS = 16
DECIM = 32
SPLIT = 128


def cos_sin(product, sample_count):
    angle = 2.0 * math.pi / sample_count * (product % sample_count).astype(jnp.float32)
    return jnp.cos(angle), jnp.sin(angle)


def dft_table(sample_count, bin_count):
    bin_index = lax.iota(jnp.int32, bin_count) + 1
    coarse = lax.iota(jnp.int32, sample_count // SPLIT) * SPLIT
    fine = lax.iota(jnp.int32, SPLIT)
    ca, sa = cos_sin(coarse[:, None] * bin_index[None, :], sample_count)
    cb, sb = cos_sin(fine[:, None] * bin_index[None, :], sample_count)
    cos_t = ca[:, None, :] * cb[None, :, :] - sa[:, None, :] * sb[None, :, :]
    sin_t = sa[:, None, :] * cb[None, :, :] + ca[:, None, :] * sb[None, :, :]
    table = jnp.concatenate([cos_t, -sin_t], axis=2).astype(jnp.bfloat16)
    return table.reshape(sample_count, 2 * bin_count)


def whiten_rows(strain_rows, bin_count):
    sample_count = strain_rows.shape[1]
    spectrum = jnp.dot(strain_rows, dft_table(sample_count, bin_count), preferred_element_type=jnp.float32)
    real_part = spectrum[:, :bin_count]
    imag_part = spectrum[:, bin_count:]
    amplitude = jnp.sqrt(real_part * real_part + imag_part * imag_part)
    level = 0.2 * jnp.mean(amplitude, axis=1, keepdims=True) + 1e-06
    divisor = jnp.maximum(amplitude, level)
    return jnp.concatenate([real_part / divisor, imag_part / divisor], axis=1).astype(jnp.bfloat16)


def correlation_kernel(sub, cc_ref, sc_ref, cf_ref, sf_ref, left_ref, right_ref, out_ref):
    window_count = left_ref.shape[1]
    acc = None
    for w in range(window_count):
        lre = left_ref[0, w, :, :F].astype(jnp.float32)
        lim = left_ref[0, w, :, F:].astype(jnp.float32)
        rre = right_ref[0, w, :F, :].astype(jnp.float32)
        rim = right_ref[0, w, F:, :].astype(jnp.float32)
        turned = []
        for l1 in range(sub):
            if l1 == 0:
                turned.append(right_ref[0, w])
                continue
            c = cf_ref[:, l1 : l1 + 1]
            s = sf_ref[:, l1 : l1 + 1]
            turned.append(jnp.concatenate([rre * c + rim * s, rim * c - rre * s], axis=0).astype(jnp.bfloat16))
        right_all = jnp.concatenate(turned, axis=1)
        parts = []
        for l2 in range(LAGS // sub):
            if l2 * sub == LAGS // 2:
                left_t = left_ref[0, w]
            else:
                c = cc_ref[l2 : l2 + 1, :]
                s = sc_ref[l2 : l2 + 1, :]
                left_t = jnp.concatenate([lre * c - lim * s, lre * s + lim * c], axis=1).astype(jnp.bfloat16)
            parts.append(
                jnp.dot(left_t, right_all, preferred_element_type=jnp.float32)
            )
        acc = parts if acc is None else [a + p for a, p in zip(acc, parts)]
    for l2, res in enumerate(acc):
        for l1 in range(sub):
            out_ref[:, 0, l2 * sub + l1, :] = res[:, l1 * C : (l1 + 1) * C].astype(out_ref.dtype)


def tile_correlation(cc, sc, cf, sf, left, right, sub):
    slot_count, window_count = left.shape[:2]
    table_spec = pl.BlockSpec(cc.shape, lambda t: (0, 0))
    column_spec = pl.BlockSpec(cf.shape, lambda t: (0, 0))
    block_spec = pl.BlockSpec((1, window_count, C, 2 * F), lambda t: (t, 0, 0, 0))
    right_spec = pl.BlockSpec((1, window_count, 2 * F, C), lambda t: (t, 0, 0, 0))
    flops = 2 * slot_count * window_count * C * 2 * F * LAGS * C
    return pl.pallas_call(
        functools.partial(correlation_kernel, sub),
        grid=(slot_count,),
        in_specs=[table_spec] * 2 + [column_spec] * 2 + [block_spec, right_spec],
        out_specs=pl.BlockSpec((C, 1, LAGS, C), lambda t: (0, t, 0, 0)),
        out_shape=jax.ShapeDtypeStruct((C, slot_count, LAGS, C), jnp.bfloat16),
        cost_estimate=pl.CostEstimate(
            flops=flops, transcendentals=0, bytes_accessed=slot_count * (4 * window_count * C * F * 2 + 2 * C * LAGS * C)
        ),
    )(cc, sc, cf, sf, left, right)


def window_sum(corr, core, y_here, n_win, own_rows):
    n_y = n_win // 2
    parts = corr.reshape((2, n_y, own_rows) + corr.shape[1:])
    send = jnp.take(parts, 1 - core, axis=0, mode="clip")
    keep = jnp.take(parts, core, axis=0, mode="clip").astype(jnp.float32)
    got = lax.ppermute(send, "win", [(w, w ^ 1) for w in range(n_win)])
    half = keep + got.astype(jnp.float32)
    total = jnp.take(half, y_here, axis=0, mode="clip")
    for shift in range(1, n_y):
        dest = (y_here + shift) % n_y
        piece = jnp.take(half, dest, axis=0, mode="clip").astype(jnp.bfloat16)
        perm = [(w, ((w // 2 + shift) % n_y) * 2 + w % 2) for w in range(n_win)]
        total = total + lax.ppermute(piece, "win", perm).astype(jnp.float32)
    return total


def body(strain, pair_list, tile_live):
    window_count, local_rows, sample_count = strain.shape
    slot_count = tile_live.shape[0]
    n_pair = lax.axis_size("pair")
    n_win = lax.axis_size("win")
    pair_here = lax.axis_index("pair")
    win_here = lax.axis_index("win")
    b_dev = local_rows // C

    flat_rows = strain.reshape(window_count * local_rows, sample_count)
    whitened = whiten_rows(flat_rows, F).reshape(window_count, b_dev, C, 2 * F)

    lists = pair_list.reshape(n_pair, 2 * slot_count)
    mine = (lists // b_dev) == pair_here
    local_pick = jnp.sum(jnp.where(mine, lists % b_dev, 0), axis=1)
    outgoing = jnp.take(jnp.transpose(whitened, (1, 0, 2, 3)), local_pick, axis=0, mode="clip")
    incoming = lax.all_to_all(outgoing, "pair", 0, 0, tiled=True)
    wanted = lax.dynamic_slice_in_dim(pair_list, pair_here * slot_count, slot_count, 0)
    left = jnp.take(incoming, wanted[:, 0] // b_dev, axis=0, mode="clip")
    right = jnp.take(incoming, wanted[:, 1] // b_dev, axis=0, mode="clip")

    sub = 4
    own_rows = C // n_win
    n_y = n_win // 2
    bins = lax.iota(jnp.int32, F) + 1
    fine_lag = lax.iota(jnp.int32, sub) * DECIM
    coarse_lag = (lax.iota(jnp.int32, LAGS // sub) * sub - LAGS // 2) * DECIM
    cf, sf = cos_sin(fine_lag[:, None] * bins[None, :], sample_count)
    cc, sc = cos_sin(coarse_lag[:, None] * bins[None, :], sample_count)
    left = left.reshape(slot_count, window_count, n_y, 2, own_rows, 2 * F)
    left = jnp.transpose(left, (0, 1, 3, 2, 4, 5)).reshape(slot_count, window_count, C, 2 * F)
    right = jnp.swapaxes(right, 2, 3)
    core = win_here % 2
    y_here = win_here // 2
    totals = []
    for t in range(slot_count):
        corr = tile_correlation(cc, sc, cf.T, sf.T, left[t : t + 1], right[t : t + 1], sub)
        totals.append(window_sum(corr, core, y_here, n_win, own_rows))
    total = jnp.concatenate(totals, axis=1)

    live_local = tile_live.astype(jnp.float32)
    return total * live_local[None, :, None, None] / math.sqrt(F * window_count * n_win)


def solution(mesh):
    in_specs = (P("win", "pair", None), P(), P("pair"))
    out_specs = P("win", "pair", None, None)
    return jax.shard_map(body, mesh=mesh, in_specs=in_specs, out_specs=out_specs, check_vma=False)
```

```python
import functools
import math

import jax
import jax.numpy as jnp
from jax import lax
from jax.experimental import pallas as pl
from jax.experimental.pallas import tpu as pltpu
from jax.sharding import PartitionSpec as P

C = 128
F = 384
LAGS = 16
DECIM = 32
SPLIT = 128


def cos_sin(product, sample_count):
    angle = 2.0 * math.pi / sample_count * (product % sample_count).astype(jnp.float32)
    return jnp.cos(angle), jnp.sin(angle)


def dft_table(sample_count, bin_count):
    bin_index = lax.iota(jnp.int32, bin_count) + 1
    coarse = lax.iota(jnp.int32, sample_count // SPLIT) * SPLIT
    fine = lax.iota(jnp.int32, SPLIT)
    ca, sa = cos_sin(coarse[:, None] * bin_index[None, :], sample_count)
    cb, sb = cos_sin(fine[:, None] * bin_index[None, :], sample_count)
    cos_t = ca[:, None, :] * cb[None, :, :] - sa[:, None, :] * sb[None, :, :]
    sin_t = sa[:, None, :] * cb[None, :, :] + ca[:, None, :] * sb[None, :, :]
    table = jnp.concatenate([cos_t, -sin_t], axis=2).astype(jnp.bfloat16)
    return table.reshape(sample_count, 2 * bin_count)


def whiten_rows(strain_rows, bin_count):
    sample_count = strain_rows.shape[1]
    spectrum = jnp.dot(strain_rows, dft_table(sample_count, bin_count), preferred_element_type=jnp.float32)
    real_part = spectrum[:, :bin_count]
    imag_part = spectrum[:, bin_count:]
    amplitude = jnp.sqrt(real_part * real_part + imag_part * imag_part)
    level = 0.2 * jnp.mean(amplitude, axis=1, keepdims=True) + 1e-06
    divisor = jnp.maximum(amplitude, level)
    return jnp.concatenate([real_part / divisor, imag_part / divisor], axis=1).astype(jnp.bfloat16)


def correlation_kernel(sub, cc_ref, sc_ref, cf_ref, sf_ref, left_ref, right_ref, out_ref):
    window_count = left_ref.shape[1]
    acc = None
    for w in range(window_count):
        lre = left_ref[0, w, :, :F].astype(jnp.float32)
        lim = left_ref[0, w, :, F:].astype(jnp.float32)
        rre = right_ref[0, w, :F, :].astype(jnp.float32)
        rim = right_ref[0, w, F:, :].astype(jnp.float32)
        turned = []
        for l1 in range(sub):
            if l1 == 0:
                turned.append(right_ref[0, w])
                continue
            c = cf_ref[:, l1 : l1 + 1]
            s = sf_ref[:, l1 : l1 + 1]
            turned.append(jnp.concatenate([rre * c + rim * s, rim * c - rre * s], axis=0).astype(jnp.bfloat16))
        right_all = jnp.concatenate(turned, axis=1)
        parts = []
        for l2 in range(LAGS // sub):
            if l2 * sub == LAGS // 2:
                left_t = left_ref[0, w]
            else:
                c = cc_ref[l2 : l2 + 1, :]
                s = sc_ref[l2 : l2 + 1, :]
                left_t = jnp.concatenate([lre * c - lim * s, lre * s + lim * c], axis=1).astype(jnp.bfloat16)
            parts.append(
                jnp.dot(left_t, right_all, preferred_element_type=jnp.float32)
            )
        acc = parts if acc is None else [a + p for a, p in zip(acc, parts)]
    half_rows = C // 2
    for l2, res in enumerate(acc):
        for l1 in range(sub):
            for part in range(2):
                out_ref[part, l2 * sub + l1] = res[part * half_rows : (part + 1) * half_rows, l1 * C : (l1 + 1) * C].astype(
                    out_ref.dtype
                )


def tile_correlation(cc, sc, cf, sf, left, right, sub):
    slot_count, window_count = left.shape[:2]
    table_spec = pl.BlockSpec(cc.shape, lambda t: (0, 0))
    column_spec = pl.BlockSpec(cf.shape, lambda t: (0, 0))
    block_spec = pl.BlockSpec((1, window_count, C, 2 * F), lambda t: (t, 0, 0, 0))
    right_spec = pl.BlockSpec((1, window_count, 2 * F, C), lambda t: (t, 0, 0, 0))
    flops = 2 * slot_count * window_count * C * 2 * F * LAGS * C
    return pl.pallas_call(
        functools.partial(correlation_kernel, sub),
        grid=(slot_count,),
        in_specs=[table_spec] * 2 + [column_spec] * 2 + [block_spec, right_spec],
        out_specs=pl.BlockSpec((2, LAGS, C // 2, C), lambda t: (0, 0, 0, t)),
        out_shape=jax.ShapeDtypeStruct((2, LAGS, C // 2, slot_count * C), jnp.bfloat16),
        cost_estimate=pl.CostEstimate(
            flops=flops, transcendentals=0, bytes_accessed=slot_count * (4 * window_count * C * F * 2 + 2 * C * LAGS * C)
        ),
    )(cc, sc, cf, sf, left, right)


def body(strain, pair_list, tile_live):
    window_count, local_rows, sample_count = strain.shape
    slot_count = tile_live.shape[0]
    n_pair = lax.axis_size("pair")
    n_win = lax.axis_size("win")
    pair_here = lax.axis_index("pair")
    win_here = lax.axis_index("win")
    b_dev = local_rows // C

    flat_rows = strain.reshape(window_count * local_rows, sample_count)
    whitened = whiten_rows(flat_rows, F).reshape(window_count, b_dev, C, 2 * F)

    lists = pair_list.reshape(n_pair, 2 * slot_count)
    mine = (lists // b_dev) == pair_here
    local_pick = jnp.sum(jnp.where(mine, lists % b_dev, 0), axis=1)
    outgoing = jnp.take(jnp.transpose(whitened, (1, 0, 2, 3)), local_pick, axis=0, mode="clip")
    incoming = lax.all_to_all(outgoing, "pair", 0, 0, tiled=True)
    wanted = lax.dynamic_slice_in_dim(pair_list, pair_here * slot_count, slot_count, 0)
    left = jnp.take(incoming, wanted[:, 0] // b_dev, axis=0, mode="clip")
    right = jnp.take(incoming, wanted[:, 1] // b_dev, axis=0, mode="clip")

    sub = 4
    own_rows = C // n_win
    n_y = n_win // 2
    bins = lax.iota(jnp.int32, F) + 1
    fine_lag = lax.iota(jnp.int32, sub) * DECIM
    coarse_lag = (lax.iota(jnp.int32, LAGS // sub) * sub - LAGS // 2) * DECIM
    cf, sf = cos_sin(fine_lag[:, None] * bins[None, :], sample_count)
    cc, sc = cos_sin(coarse_lag[:, None] * bins[None, :], sample_count)
    left = left.reshape(slot_count, window_count, n_y, 2, own_rows, 2 * F)
    left = jnp.transpose(left, (0, 1, 3, 2, 4, 5)).reshape(slot_count, window_count, C, 2 * F)
    right = jnp.swapaxes(right, 2, 3)
    corr = tile_correlation(cc, sc, cf.T, sf.T, left, right, sub)

    core = win_here % 2
    y_here = win_here // 2
    send = jnp.take(corr, 1 - core, axis=0, mode="clip")
    keep = jnp.take(corr, core, axis=0, mode="clip").astype(jnp.float32)
    got = lax.ppermute(send, "win", [(w, w ^ 1) for w in range(n_win)])
    half = (keep + got.astype(jnp.float32)).reshape(LAGS, n_y, own_rows, slot_count * C)
    half = jnp.transpose(half, (1, 0, 2, 3))
    total = jnp.take(half, y_here, axis=0, mode="clip")
    for shift in range(1, n_y):
        dest = (y_here + shift) % n_y
        piece = jnp.take(half, dest, axis=0, mode="clip").astype(jnp.bfloat16)
        perm = [(w, ((w // 2 + shift) % n_y) * 2 + w % 2) for w in range(n_win)]
        total = total + lax.ppermute(piece, "win", perm).astype(jnp.float32)
    total = jnp.transpose(total.reshape(LAGS, own_rows, slot_count, C), (1, 2, 0, 3))

    live_local = tile_live.astype(jnp.float32)
    return total * live_local[None, :, None, None] / math.sqrt(F * window_count * n_win)


def solution(mesh):
    in_specs = (P("win", "pair", None), P(), P("pair"))
    out_specs = P("win", "pair", None, None)
    return jax.shard_map(body, mesh=mesh, in_specs=in_specs, out_specs=out_specs, check_vma=False)
```

```python
import functools
import math

import jax
import jax.numpy as jnp
from jax import lax
from jax.experimental import pallas as pl
from jax.experimental.pallas import tpu as pltpu
from jax.sharding import PartitionSpec as P

C = 128
F = 384
LAGS = 16
DECIM = 32
SPLIT = 256


def cos_sin(product, sample_count):
    angle = 2.0 * math.pi / sample_count * (product % sample_count).astype(jnp.float32)
    return jnp.cos(angle), jnp.sin(angle)


def dft_kernel(group, bin_count, ca_ref, sa_ref, cb_ref, sb_ref, x_ref, out_ref, acc_ref):
    k = pl.program_id(0)

    @pl.when(k == 0)
    def _():
        acc_ref[...] = jnp.zeros_like(acc_ref)

    cb = cb_ref[...]
    sb = sb_ref[...]
    for g in range(group):
        a = k * group + g
        ca = ca_ref[pl.ds(a, 1), :]
        sa = sa_ref[pl.ds(a, 1), :]
        table = jnp.concatenate([ca * cb - sa * sb, -(sa * cb + ca * sb)], axis=1).astype(jnp.bfloat16)
        acc_ref[...] += jnp.dot(x_ref[:, g * SPLIT : (g + 1) * SPLIT], table, preferred_element_type=jnp.float32)

    @pl.when(k == pl.num_programs(0) - 1)
    def _():
        spectrum = acc_ref[...]
        real_part = spectrum[:, :bin_count]
        imag_part = spectrum[:, bin_count:]
        amplitude = jnp.sqrt(real_part * real_part + imag_part * imag_part)
        level = 0.2 * jnp.mean(amplitude, axis=1, keepdims=True) + 1e-06
        divisor = jnp.maximum(amplitude, level)
        out_ref[...] = jnp.concatenate([real_part / divisor, imag_part / divisor], axis=1).astype(out_ref.dtype)


def whiten_rows(strain_rows, bin_count):
    row_count, sample_count = strain_rows.shape
    bin_index = lax.iota(jnp.int32, bin_count) + 1
    coarse_count = sample_count // SPLIT
    ca, sa = cos_sin((lax.iota(jnp.int32, coarse_count) * SPLIT)[:, None] * bin_index[None, :], sample_count)
    cb, sb = cos_sin(lax.iota(jnp.int32, SPLIT)[:, None] * bin_index[None, :], sample_count)
    group = max(g for g in range(1, 7) if coarse_count % g == 0)
    steps = coarse_count // group
    full = lambda shape: pl.BlockSpec(shape, lambda k: (0, 0))
    return pl.pallas_call(
        functools.partial(dft_kernel, group, bin_count),
        grid=(steps,),
        in_specs=[full(ca.shape), full(sa.shape), full(cb.shape), full(sb.shape)]
        + [pl.BlockSpec((row_count, group * SPLIT), lambda k: (0, k))],
        out_specs=pl.BlockSpec((row_count, 2 * bin_count), lambda k: (0, 0)),
        out_shape=jax.ShapeDtypeStruct((row_count, 2 * bin_count), jnp.bfloat16),
        scratch_shapes=[pltpu.VMEM((row_count, 2 * bin_count), jnp.float32)],
        cost_estimate=pl.CostEstimate(
            flops=2 * row_count * sample_count * 2 * bin_count,
            transcendentals=0,
            bytes_accessed=row_count * sample_count * 2 + row_count * 2 * bin_count * 2,
        ),
    )(ca, sa, cb, sb, strain_rows)


def correlation_kernel(sub, cc_ref, sc_ref, cf_ref, sf_ref, left_ref, right_ref, out_ref):
    window_count = left_ref.shape[1]
    acc = None
    for w in range(window_count):
        lre = left_ref[0, w, :, :F].astype(jnp.float32)
        lim = left_ref[0, w, :, F:].astype(jnp.float32)
        rre = right_ref[0, w, :F, :].astype(jnp.float32)
        rim = right_ref[0, w, F:, :].astype(jnp.float32)
        turned = []
        for l1 in range(sub):
            if l1 == 0:
                turned.append(right_ref[0, w])
                continue
            c = cf_ref[:, l1 : l1 + 1]
            s = sf_ref[:, l1 : l1 + 1]
            turned.append(jnp.concatenate([rre * c + rim * s, rim * c - rre * s], axis=0).astype(jnp.bfloat16))
        right_all = jnp.concatenate(turned, axis=1)
        parts = []
        for l2 in range(LAGS // sub):
            if l2 * sub == LAGS // 2:
                left_t = left_ref[0, w]
            else:
                c = cc_ref[l2 : l2 + 1, :]
                s = sc_ref[l2 : l2 + 1, :]
                left_t = jnp.concatenate([lre * c - lim * s, lre * s + lim * c], axis=1).astype(jnp.bfloat16)
            parts.append(
                jnp.dot(left_t, right_all, preferred_element_type=jnp.float32)
            )
        acc = parts if acc is None else [a + p for a, p in zip(acc, parts)]
    half_rows = C // 2
    for l2, res in enumerate(acc):
        for l1 in range(sub):
            for part in range(2):
                out_ref[part, l2 * sub + l1] = res[part * half_rows : (part + 1) * half_rows, l1 * C : (l1 + 1) * C].astype(
                    out_ref.dtype
                )


def tile_correlation(cc, sc, cf, sf, left, right, sub):
    slot_count, window_count = left.shape[:2]
    table_spec = pl.BlockSpec(cc.shape, lambda t: (0, 0))
    column_spec = pl.BlockSpec(cf.shape, lambda t: (0, 0))
    block_spec = pl.BlockSpec((1, window_count, C, 2 * F), lambda t: (t, 0, 0, 0))
    right_spec = pl.BlockSpec((1, window_count, 2 * F, C), lambda t: (t, 0, 0, 0))
    flops = 2 * slot_count * window_count * C * 2 * F * LAGS * C
    return pl.pallas_call(
        functools.partial(correlation_kernel, sub),
        grid=(slot_count,),
        in_specs=[table_spec] * 2 + [column_spec] * 2 + [block_spec, right_spec],
        out_specs=pl.BlockSpec((2, LAGS, C // 2, C), lambda t: (0, 0, 0, t)),
        out_shape=jax.ShapeDtypeStruct((2, LAGS, C // 2, slot_count * C), jnp.bfloat16),
        cost_estimate=pl.CostEstimate(
            flops=flops, transcendentals=0, bytes_accessed=slot_count * (4 * window_count * C * F * 2 + 2 * C * LAGS * C)
        ),
    )(cc, sc, cf, sf, left, right)


def body(strain, pair_list, tile_live):
    window_count, local_rows, sample_count = strain.shape
    slot_count = tile_live.shape[0]
    n_pair = lax.axis_size("pair")
    n_win = lax.axis_size("win")
    pair_here = lax.axis_index("pair")
    win_here = lax.axis_index("win")
    b_dev = local_rows // C

    flat_rows = strain.reshape(window_count * local_rows, sample_count)
    whitened = whiten_rows(flat_rows, F).reshape(window_count, b_dev, C, 2 * F)

    lists = pair_list.reshape(n_pair, 2 * slot_count)
    mine = (lists // b_dev) == pair_here
    local_pick = jnp.sum(jnp.where(mine, lists % b_dev, 0), axis=1)
    outgoing = jnp.take(jnp.transpose(whitened, (1, 0, 2, 3)), local_pick, axis=0, mode="clip")
    incoming = lax.all_to_all(outgoing, "pair", 0, 0, tiled=True)
    wanted = lax.dynamic_slice_in_dim(pair_list, pair_here * slot_count, slot_count, 0)
    left = jnp.take(incoming, wanted[:, 0] // b_dev, axis=0, mode="clip")
    right = jnp.take(incoming, wanted[:, 1] // b_dev, axis=0, mode="clip")

    sub = 4
    own_rows = C // n_win
    n_y = n_win // 2
    bins = lax.iota(jnp.int32, F) + 1
    fine_lag = lax.iota(jnp.int32, sub) * DECIM
    coarse_lag = (lax.iota(jnp.int32, LAGS // sub) * sub - LAGS // 2) * DECIM
    cf, sf = cos_sin(fine_lag[:, None] * bins[None, :], sample_count)
    cc, sc = cos_sin(coarse_lag[:, None] * bins[None, :], sample_count)
    left = left.reshape(slot_count, window_count, n_y, 2, own_rows, 2 * F)
    left = jnp.transpose(left, (0, 1, 3, 2, 4, 5)).reshape(slot_count, window_count, C, 2 * F)
    right = jnp.swapaxes(right, 2, 3)
    corr = tile_correlation(cc, sc, cf.T, sf.T, left, right, sub)

    core = win_here % 2
    y_here = win_here // 2
    send = jnp.take(corr, 1 - core, axis=0, mode="clip")
    keep = jnp.take(corr, core, axis=0, mode="clip").astype(jnp.float32)
    got = lax.ppermute(send, "win", [(w, w ^ 1) for w in range(n_win)])
    half = (keep + got.astype(jnp.float32)).reshape(LAGS, n_y, own_rows, slot_count * C)
    half = jnp.transpose(half, (1, 0, 2, 3))
    total = jnp.take(half, y_here, axis=0, mode="clip")
    for shift in range(1, n_y):
        dest = (y_here + shift) % n_y
        piece = jnp.take(half, dest, axis=0, mode="clip").astype(jnp.bfloat16)
        perm = [(w, ((w // 2 + shift) % n_y) * 2 + w % 2) for w in range(n_win)]
        total = total + lax.ppermute(piece, "win", perm).astype(jnp.float32)
    total = jnp.transpose(total.reshape(LAGS, own_rows, slot_count, C), (1, 2, 0, 3))

    live_local = tile_live.astype(jnp.float32)
    return total * live_local[None, :, None, None] / math.sqrt(F * window_count * n_win)


def solution(mesh):
    in_specs = (P("win", "pair", None), P(), P("pair"))
    out_specs = P("win", "pair", None, None)
    return jax.shard_map(body, mesh=mesh, in_specs=in_specs, out_specs=out_specs, check_vma=False)
```

```python
import functools
import math

import jax
import jax.numpy as jnp
from jax import lax
from jax.experimental import pallas as pl
from jax.experimental.pallas import tpu as pltpu
from jax.sharding import PartitionSpec as P

C = 128
F = 384
LAGS = 16
DECIM = 32
SPLIT = 128


def cos_sin(product, sample_count):
    angle = 2.0 * math.pi / sample_count * (product % sample_count).astype(jnp.float32)
    return jnp.cos(angle), jnp.sin(angle)


def dft_table(sample_count, bin_count):
    bin_index = lax.iota(jnp.int32, bin_count) + 1
    coarse = lax.iota(jnp.int32, sample_count // SPLIT) * SPLIT
    fine = lax.iota(jnp.int32, SPLIT)
    ca, sa = cos_sin(coarse[:, None] * bin_index[None, :], sample_count)
    cb, sb = cos_sin(fine[:, None] * bin_index[None, :], sample_count)
    cos_t = ca[:, None, :] * cb[None, :, :] - sa[:, None, :] * sb[None, :, :]
    sin_t = sa[:, None, :] * cb[None, :, :] + ca[:, None, :] * sb[None, :, :]
    table = jnp.concatenate([cos_t, -sin_t], axis=2).astype(jnp.bfloat16)
    return table.reshape(sample_count, 2 * bin_count)


def whiten_rows(strain_rows, bin_count):
    sample_count = strain_rows.shape[1]
    spectrum = jnp.dot(strain_rows, dft_table(sample_count, bin_count), preferred_element_type=jnp.float32)
    real_part = spectrum[:, :bin_count]
    imag_part = spectrum[:, bin_count:]
    amplitude = jnp.sqrt(real_part * real_part + imag_part * imag_part)
    level = 0.2 * jnp.mean(amplitude, axis=1, keepdims=True) + 1e-06
    divisor = jnp.maximum(amplitude, level)
    return jnp.concatenate([real_part / divisor, imag_part / divisor], axis=1).astype(jnp.bfloat16)


def correlation_kernel(sub, n_y, own_rows, index_ref, cc_ref, sc_ref, cf_ref, sf_ref, left_ref, right_ref, out_ref):
    window_count = left_ref.shape[1]
    order = [(y * 2 + c) * own_rows for c in range(2) for y in range(n_y)]
    acc = None
    for w in range(window_count):
        left = left_ref[0, w].astype(jnp.float32)
        left = jnp.concatenate([left[r : r + own_rows] for r in order], axis=0)
        lre = left[:, :F]
        lim = left[:, F:]
        rre = right_ref[0, w, :, :F].astype(jnp.float32)
        rim = right_ref[0, w, :, F:].astype(jnp.float32)
        turned = []
        for l1 in range(sub):
            if l1 == 0:
                turned.append(right_ref[0, w])
                continue
            c = cf_ref[l1 : l1 + 1, :]
            s = sf_ref[l1 : l1 + 1, :]
            turned.append(jnp.concatenate([rre * c + rim * s, rim * c - rre * s], axis=1).astype(jnp.bfloat16))
        right_all = jnp.concatenate(turned, axis=0)
        parts = []
        for l2 in range(LAGS // sub):
            if l2 * sub == LAGS // 2:
                left_t = left.astype(jnp.bfloat16)
            else:
                c = cc_ref[l2 : l2 + 1, :]
                s = sc_ref[l2 : l2 + 1, :]
                left_t = jnp.concatenate([lre * c - lim * s, lre * s + lim * c], axis=1).astype(jnp.bfloat16)
            parts.append(
                lax.dot_general(left_t, right_all, (((1,), (1,)), ((), ())), preferred_element_type=jnp.float32)
            )
        acc = parts if acc is None else [a + p for a, p in zip(acc, parts)]
    half_rows = C // 2
    for l2, res in enumerate(acc):
        for l1 in range(sub):
            for part in range(2):
                out_ref[part, l2 * sub + l1] = res[part * half_rows : (part + 1) * half_rows, l1 * C : (l1 + 1) * C].astype(
                    out_ref.dtype
                )


def tile_correlation(cc, sc, cf, sf, incoming, slots, sub, n_y, own_rows):
    window_count = incoming.shape[1]
    slot_count = slots.shape[0] // 2
    table_spec = pl.BlockSpec(cc.shape, lambda t, idx: (0, 0))
    left_spec = pl.BlockSpec((1, window_count, C, 2 * F), lambda t, idx: (idx[2 * t], 0, 0, 0))
    right_spec = pl.BlockSpec((1, window_count, C, 2 * F), lambda t, idx: (idx[2 * t + 1], 0, 0, 0))
    flops = 2 * slot_count * window_count * C * 2 * F * LAGS * C
    grid_spec = pltpu.PrefetchScalarGridSpec(
        num_scalar_prefetch=1,
        grid=(slot_count,),
        in_specs=[table_spec] * 4 + [left_spec, right_spec],
        out_specs=pl.BlockSpec((2, LAGS, C // 2, C), lambda t, idx: (0, 0, 0, t)),
    )
    return pl.pallas_call(
        functools.partial(correlation_kernel, sub, n_y, own_rows),
        grid_spec=grid_spec,
        out_shape=jax.ShapeDtypeStruct((2, LAGS, C // 2, slot_count * C), jnp.bfloat16),
        cost_estimate=pl.CostEstimate(
            flops=flops, transcendentals=0, bytes_accessed=slot_count * (4 * window_count * C * F * 2 + 2 * C * LAGS * C)
        ),
    )(slots, cc, sc, cf, sf, incoming, incoming)


def body(strain, pair_list, tile_live):
    window_count, local_rows, sample_count = strain.shape
    slot_count = tile_live.shape[0]
    n_pair = lax.axis_size("pair")
    n_win = lax.axis_size("win")
    pair_here = lax.axis_index("pair")
    win_here = lax.axis_index("win")
    b_dev = local_rows // C

    flat_rows = strain.reshape(window_count * local_rows, sample_count)
    whitened = whiten_rows(flat_rows, F).reshape(window_count, b_dev, C, 2 * F)

    lists = pair_list.reshape(n_pair, 2 * slot_count)
    mine = (lists // b_dev) == pair_here
    local_pick = jnp.sum(jnp.where(mine, lists % b_dev, 0), axis=1)
    pick = local_pick[:, None, None, None]
    outgoing = jnp.broadcast_to(whitened[:, 0][None], (n_pair,) + whitened[:, 0].shape)
    for k in range(1, b_dev):
        outgoing = jnp.where(pick == k, whitened[:, k][None], outgoing)
    incoming = lax.all_to_all(outgoing, "pair", 0, 0, tiled=True)
    wanted = lax.dynamic_slice_in_dim(pair_list, pair_here * slot_count, slot_count, 0)
    slots = jnp.clip(wanted.reshape(2 * slot_count) // b_dev, 0, n_pair - 1)

    sub = 4
    own_rows = C // n_win
    n_y = n_win // 2
    bins = lax.iota(jnp.int32, F) + 1
    fine_lag = lax.iota(jnp.int32, sub) * DECIM
    coarse_lag = (lax.iota(jnp.int32, LAGS // sub) * sub - LAGS // 2) * DECIM
    cf, sf = cos_sin(fine_lag[:, None] * bins[None, :], sample_count)
    cc, sc = cos_sin(coarse_lag[:, None] * bins[None, :], sample_count)
    corr = tile_correlation(cc, sc, cf, sf, incoming, slots, sub, n_y, own_rows)

    core = win_here % 2
    y_here = win_here // 2
    send = jnp.take(corr, 1 - core, axis=0, mode="clip")
    keep = jnp.take(corr, core, axis=0, mode="clip").astype(jnp.float32)
    got = lax.ppermute(send, "win", [(w, w ^ 1) for w in range(n_win)])
    half = (keep + got.astype(jnp.float32)).reshape(LAGS, n_y, own_rows, slot_count * C)
    half = jnp.transpose(half, (1, 0, 2, 3))
    total = jnp.take(half, y_here, axis=0, mode="clip")
    for shift in range(1, n_y):
        dest = (y_here + shift) % n_y
        piece = jnp.take(half, dest, axis=0, mode="clip").astype(jnp.bfloat16)
        perm = [(w, ((w // 2 + shift) % n_y) * 2 + w % 2) for w in range(n_win)]
        total = total + lax.ppermute(piece, "win", perm).astype(jnp.float32)
    total = jnp.transpose(total.reshape(LAGS, own_rows, slot_count, C), (1, 2, 0, 3))

    live_local = tile_live.astype(jnp.float32)
    return total * live_local[None, :, None, None] / math.sqrt(F * window_count * n_win)


def solution(mesh):
    in_specs = (P("win", "pair", None), P(), P("pair"))
    out_specs = P("win", "pair", None, None)
    return jax.shard_map(body, mesh=mesh, in_specs=in_specs, out_specs=out_specs, check_vma=False)
```

```python
import functools
import math

import jax
import jax.numpy as jnp
from jax import lax
from jax.experimental import pallas as pl
from jax.experimental.pallas import tpu as pltpu
from jax.sharding import PartitionSpec as P

C = 128
F = 384
LAGS = 16
DECIM = 32
SPLIT = 128


def cos_sin(product, sample_count):
    angle = 2.0 * math.pi / sample_count * (product % sample_count).astype(jnp.float32)
    return jnp.cos(angle), jnp.sin(angle)


def dft_table(sample_count, bin_count):
    bin_index = lax.iota(jnp.int32, bin_count) + 1
    coarse = lax.iota(jnp.int32, sample_count // SPLIT) * SPLIT
    fine = lax.iota(jnp.int32, SPLIT)
    ca, sa = cos_sin(coarse[:, None] * bin_index[None, :], sample_count)
    cb, sb = cos_sin(fine[:, None] * bin_index[None, :], sample_count)
    cos_t = ca[:, None, :] * cb[None, :, :] - sa[:, None, :] * sb[None, :, :]
    sin_t = sa[:, None, :] * cb[None, :, :] + ca[:, None, :] * sb[None, :, :]
    table = jnp.concatenate([cos_t, -sin_t], axis=2).astype(jnp.bfloat16)
    return table.reshape(sample_count, 2 * bin_count)


def whiten_rows(strain_rows, bin_count):
    sample_count = strain_rows.shape[1]
    spectrum = jnp.dot(strain_rows, dft_table(sample_count, bin_count), preferred_element_type=jnp.float32)
    real_part = spectrum[:, :bin_count]
    imag_part = spectrum[:, bin_count:]
    amplitude = jnp.sqrt(real_part * real_part + imag_part * imag_part)
    level = 0.2 * jnp.mean(amplitude, axis=1, keepdims=True) + 1e-06
    divisor = jnp.maximum(amplitude, level)
    return jnp.concatenate([real_part / divisor, imag_part / divisor], axis=1).astype(jnp.bfloat16)


def correlation_kernel(sub, n_y, own_rows, index_ref, cc_ref, sc_ref, cf_ref, sf_ref, left_ref, right_ref, out_ref):
    window_count = left_ref.shape[1]
    order = [(y * 2 + c) * own_rows for c in range(2) for y in range(n_y)]
    acc = None
    for w in range(window_count):
        left = left_ref[0, w].astype(jnp.float32)
        left = jnp.concatenate([left[r : r + own_rows] for r in order], axis=0)
        lre = left[:, :F]
        lim = left[:, F:]
        rre = right_ref[0, w, :, :F].astype(jnp.float32)
        rim = right_ref[0, w, :, F:].astype(jnp.float32)
        turned = []
        for l1 in range(sub):
            if l1 == 0:
                turned.append(right_ref[0, w])
                continue
            c = cf_ref[l1 : l1 + 1, :]
            s = sf_ref[l1 : l1 + 1, :]
            turned.append(jnp.concatenate([rre * c + rim * s, rim * c - rre * s], axis=1).astype(jnp.bfloat16))
        right_all = jnp.concatenate(turned, axis=0)
        parts = []
        for l2 in range(LAGS // sub):
            if l2 * sub == LAGS // 2:
                left_t = left.astype(jnp.bfloat16)
            else:
                c = cc_ref[l2 : l2 + 1, :]
                s = sc_ref[l2 : l2 + 1, :]
                left_t = jnp.concatenate([lre * c - lim * s, lre * s + lim * c], axis=1).astype(jnp.bfloat16)
            parts.append(
                lax.dot_general(left_t, right_all, (((1,), (1,)), ((), ())), preferred_element_type=jnp.float32)
            )
        acc = parts if acc is None else [a + p for a, p in zip(acc, parts)]
    half_rows = C // 2
    for l2, res in enumerate(acc):
        for l1 in range(sub):
            for part in range(2):
                out_ref[part, l2 * sub + l1] = res[part * half_rows : (part + 1) * half_rows, l1 * C : (l1 + 1) * C].astype(
                    out_ref.dtype
                )


def tile_correlation(cc, sc, cf, sf, incoming, slots, sub, n_y, own_rows):
    window_count = incoming.shape[1]
    slot_count = slots.shape[0] // 2
    table_spec = pl.BlockSpec(cc.shape, lambda t, idx: (0, 0))
    left_spec = pl.BlockSpec((1, window_count, C, 2 * F), lambda t, idx: (idx[2 * t], 0, 0, 0))
    right_spec = pl.BlockSpec((1, window_count, C, 2 * F), lambda t, idx: (idx[2 * t + 1], 0, 0, 0))
    flops = 2 * slot_count * window_count * C * 2 * F * LAGS * C
    grid_spec = pltpu.PrefetchScalarGridSpec(
        num_scalar_prefetch=1,
        grid=(slot_count,),
        in_specs=[table_spec] * 4 + [left_spec, right_spec],
        out_specs=pl.BlockSpec((2, LAGS, C // 2, C), lambda t, idx: (0, 0, 0, t)),
    )
    return pl.pallas_call(
        functools.partial(correlation_kernel, sub, n_y, own_rows),
        grid_spec=grid_spec,
        out_shape=jax.ShapeDtypeStruct((2, LAGS, C // 2, slot_count * C), jnp.bfloat16),
        cost_estimate=pl.CostEstimate(
            flops=flops, transcendentals=0, bytes_accessed=slot_count * (4 * window_count * C * F * 2 + 2 * C * LAGS * C)
        ),
    )(slots, cc, sc, cf, sf, incoming, incoming)


def block_choice(lists, group, b_dev):
    return jnp.sum(jnp.where((lists // b_dev) == group, lists % b_dev, 0), axis=1)


def pick_blocks(blocks, choice):
    pick = choice[:, None, None, None]
    out = jnp.broadcast_to(blocks[:, 0][None], choice.shape + blocks[:, 0].shape)
    for k in range(1, blocks.shape[1]):
        out = jnp.where(pick == k, blocks[:, k][None], out)
    return out


def exchange_by_halves(whitened, lists, groups, pair_here, b_dev):
    n_pair = lists.shape[0]
    half = n_pair // 2
    base = (pair_here // half) * half
    pos = pair_here % half
    mirror_blocks = lax.ppermute(whitened, "pair", [(p, p ^ half) for p in range(n_pair)])
    own_choice = block_choice(lists, pair_here, b_dev)
    mirror_choice = block_choice(lists, pair_here ^ half, b_dev)
    arrived_own = []
    arrived_relay = []
    for d in range(half):
        dest = base + (pos + d) % half
        own = pick_blocks(whitened, jnp.take(own_choice, dest[None], mode="clip"))[0]
        relay = pick_blocks(mirror_blocks, jnp.take(mirror_choice, dest[None], mode="clip"))[0]
        if d:
            perm = [(p, (p // half) * half + (p % half + d) % half) for p in range(n_pair)]
            own = lax.ppermute(own, "pair", perm)
            relay = lax.ppermute(relay, "pair", perm)
        arrived_own.append(own)
        arrived_relay.append(relay)
    incoming = jnp.stack(arrived_own + arrived_relay)
    step = (pos - groups % half) % half
    slots = jnp.where(groups // half == pair_here // half, step, half + step)
    return incoming, slots


def body(strain, pair_list, tile_live):
    window_count, local_rows, sample_count = strain.shape
    slot_count = tile_live.shape[0]
    n_pair = lax.axis_size("pair")
    n_win = lax.axis_size("win")
    pair_here = lax.axis_index("pair")
    win_here = lax.axis_index("win")
    b_dev = local_rows // C

    flat_rows = strain.reshape(window_count * local_rows, sample_count)
    whitened = whiten_rows(flat_rows, F).reshape(window_count, b_dev, C, 2 * F)

    lists = pair_list.reshape(n_pair, 2 * slot_count)
    wanted = lax.dynamic_slice_in_dim(pair_list, pair_here * slot_count, slot_count, 0)
    groups = wanted.reshape(2 * slot_count) // b_dev
    if n_pair == 8:
        incoming, slots = exchange_by_halves(whitened, lists, groups, pair_here, b_dev)
    else:
        outgoing = pick_blocks(whitened, block_choice(lists, pair_here, b_dev))
        incoming = lax.all_to_all(outgoing, "pair", 0, 0, tiled=True)
        slots = groups
    slots = jnp.clip(slots, 0, n_pair - 1)

    sub = 4
    own_rows = C // n_win
    n_y = n_win // 2
    bins = lax.iota(jnp.int32, F) + 1
    fine_lag = lax.iota(jnp.int32, sub) * DECIM
    coarse_lag = (lax.iota(jnp.int32, LAGS // sub) * sub - LAGS // 2) * DECIM
    cf, sf = cos_sin(fine_lag[:, None] * bins[None, :], sample_count)
    cc, sc = cos_sin(coarse_lag[:, None] * bins[None, :], sample_count)
    corr = tile_correlation(cc, sc, cf, sf, incoming, slots, sub, n_y, own_rows)

    core = win_here % 2
    y_here = win_here // 2
    send = jnp.take(corr, 1 - core, axis=0, mode="clip")
    keep = jnp.take(corr, core, axis=0, mode="clip").astype(jnp.float32)
    got = lax.ppermute(send, "win", [(w, w ^ 1) for w in range(n_win)])
    half = (keep + got.astype(jnp.float32)).reshape(LAGS, n_y, own_rows, slot_count * C)
    half = jnp.transpose(half, (1, 0, 2, 3))
    total = jnp.take(half, y_here, axis=0, mode="clip")
    for shift in range(1, n_y):
        dest = (y_here + shift) % n_y
        piece = jnp.take(half, dest, axis=0, mode="clip").astype(jnp.bfloat16)
        perm = [(w, ((w // 2 + shift) % n_y) * 2 + w % 2) for w in range(n_win)]
        total = total + lax.ppermute(piece, "win", perm).astype(jnp.float32)
    total = jnp.transpose(total.reshape(LAGS, own_rows, slot_count, C), (1, 2, 0, 3))

    live_local = tile_live.astype(jnp.float32)
    return total * live_local[None, :, None, None] / math.sqrt(F * window_count * n_win)


def solution(mesh):
    in_specs = (P("win", "pair", None), P(), P("pair"))
    out_specs = P("win", "pair", None, None)
    return jax.shard_map(body, mesh=mesh, in_specs=in_specs, out_specs=out_specs, check_vma=False)
```

```python
import functools
import math

import jax
import jax.numpy as jnp
from jax import lax
from jax.experimental import pallas as pl
from jax.experimental.pallas import tpu as pltpu
from jax.sharding import PartitionSpec as P

C = 128
F = 384
LAGS = 16
DECIM = 32
SPLIT = 128


def cos_sin(product, sample_count):
    angle = 2.0 * math.pi / sample_count * (product % sample_count).astype(jnp.float32)
    return jnp.cos(angle), jnp.sin(angle)


def dft_table(sample_count, bin_count):
    bin_index = lax.iota(jnp.int32, bin_count) + 1
    coarse = lax.iota(jnp.int32, sample_count // SPLIT) * SPLIT
    fine = lax.iota(jnp.int32, SPLIT)
    ca, sa = cos_sin(coarse[:, None] * bin_index[None, :], sample_count)
    cb, sb = cos_sin(fine[:, None] * bin_index[None, :], sample_count)
    cos_t = ca[:, None, :] * cb[None, :, :] - sa[:, None, :] * sb[None, :, :]
    sin_t = sa[:, None, :] * cb[None, :, :] + ca[:, None, :] * sb[None, :, :]
    table = jnp.concatenate([cos_t, -sin_t], axis=2).astype(jnp.bfloat16)
    return table.reshape(sample_count, 2 * bin_count)


def whiten_rows(strain_rows, bin_count):
    sample_count = strain_rows.shape[1]
    spectrum = jnp.dot(strain_rows, dft_table(sample_count, bin_count), preferred_element_type=jnp.float32)
    real_part = spectrum[:, :bin_count]
    imag_part = spectrum[:, bin_count:]
    amplitude = jnp.sqrt(real_part * real_part + imag_part * imag_part)
    level = 0.2 * jnp.mean(amplitude, axis=1, keepdims=True) + 1e-06
    divisor = jnp.maximum(amplitude, level)
    return jnp.concatenate([real_part / divisor, imag_part / divisor], axis=1).astype(jnp.bfloat16)


def correlation_kernel(sub, n_y, own_rows, index_ref, cc_ref, sc_ref, cf_ref, sf_ref, left_ref, right_ref, out_ref):
    window_count = left_ref.shape[1]
    partner = 1 - lax.axis_index("win") % 2
    orders = [[(y * 2 + c) * own_rows for c in (1 - first, first) for y in range(n_y)] for first in (1, 0)]
    acc = None
    for w in range(window_count):
        left = left_ref[0, w].astype(jnp.float32)
        by_order = [jnp.concatenate([left[r : r + own_rows] for r in order], axis=0) for order in orders]
        left = jnp.where(partner == 0, by_order[0], by_order[1])
        lre = left[:, :F]
        lim = left[:, F:]
        rre = right_ref[0, w, :, :F].astype(jnp.float32)
        rim = right_ref[0, w, :, F:].astype(jnp.float32)
        turned = []
        for l1 in range(sub):
            if l1 == 0:
                turned.append(right_ref[0, w])
                continue
            c = cf_ref[l1 : l1 + 1, :]
            s = sf_ref[l1 : l1 + 1, :]
            turned.append(jnp.concatenate([rre * c + rim * s, rim * c - rre * s], axis=1).astype(jnp.bfloat16))
        right_all = jnp.concatenate(turned, axis=0)
        parts = []
        for l2 in range(LAGS // sub):
            if l2 * sub == LAGS // 2:
                left_t = left.astype(jnp.bfloat16)
            else:
                c = cc_ref[l2 : l2 + 1, :]
                s = sc_ref[l2 : l2 + 1, :]
                left_t = jnp.concatenate([lre * c - lim * s, lre * s + lim * c], axis=1).astype(jnp.bfloat16)
            parts.append(
                lax.dot_general(left_t, right_all, (((1,), (1,)), ((), ())), preferred_element_type=jnp.float32)
            )
        acc = parts if acc is None else [a + p for a, p in zip(acc, parts)]
    half_rows = C // 2
    for l2, res in enumerate(acc):
        for l1 in range(sub):
            for part in range(2):
                out_ref[part, l2 * sub + l1] = res[part * half_rows : (part + 1) * half_rows, l1 * C : (l1 + 1) * C].astype(
                    out_ref.dtype
                )


def tile_correlation(cc, sc, cf, sf, incoming, slots, sub, n_y, own_rows):
    window_count = incoming.shape[1]
    slot_count = slots.shape[0] // 2
    table_spec = pl.BlockSpec(cc.shape, lambda t, idx: (0, 0))
    left_spec = pl.BlockSpec((1, window_count, C, 2 * F), lambda t, idx: (idx[2 * t], 0, 0, 0))
    right_spec = pl.BlockSpec((1, window_count, C, 2 * F), lambda t, idx: (idx[2 * t + 1], 0, 0, 0))
    flops = 2 * slot_count * window_count * C * 2 * F * LAGS * C
    grid_spec = pltpu.PrefetchScalarGridSpec(
        num_scalar_prefetch=1,
        grid=(slot_count,),
        in_specs=[table_spec] * 4 + [left_spec, right_spec],
        out_specs=pl.BlockSpec((2, LAGS, C // 2, C), lambda t, idx: (0, 0, 0, t)),
    )
    return pl.pallas_call(
        functools.partial(correlation_kernel, sub, n_y, own_rows),
        grid_spec=grid_spec,
        out_shape=jax.ShapeDtypeStruct((2, LAGS, C // 2, slot_count * C), jnp.bfloat16),
        cost_estimate=pl.CostEstimate(
            flops=flops, transcendentals=0, bytes_accessed=slot_count * (4 * window_count * C * F * 2 + 2 * C * LAGS * C)
        ),
    )(slots, cc, sc, cf, sf, incoming, incoming)


def block_choice(lists, group, b_dev):
    return jnp.sum(jnp.where((lists // b_dev) == group, lists % b_dev, 0), axis=1)


def pick_blocks(blocks, choice):
    pick = choice[:, None, None, None]
    out = jnp.broadcast_to(blocks[:, 0][None], choice.shape + blocks[:, 0].shape)
    for k in range(1, blocks.shape[1]):
        out = jnp.where(pick == k, blocks[:, k][None], out)
    return out


def exchange_by_halves(whitened, lists, groups, pair_here, b_dev):
    n_pair = lists.shape[0]
    half = n_pair // 2
    base = (pair_here // half) * half
    pos = pair_here % half
    mirror_blocks = lax.ppermute(whitened, "pair", [(p, p ^ half) for p in range(n_pair)])
    own_choice = block_choice(lists, pair_here, b_dev)
    mirror_choice = block_choice(lists, pair_here ^ half, b_dev)
    arrived_own = []
    arrived_relay = []
    for d in range(half):
        dest = base + (pos + d) % half
        own = pick_blocks(whitened, jnp.take(own_choice, dest[None], mode="clip"))[0]
        relay = pick_blocks(mirror_blocks, jnp.take(mirror_choice, dest[None], mode="clip"))[0]
        if d:
            perm = [(p, (p // half) * half + (p % half + d) % half) for p in range(n_pair)]
            own = lax.ppermute(own, "pair", perm)
            relay = lax.ppermute(relay, "pair", perm)
        arrived_own.append(own)
        arrived_relay.append(relay)
    incoming = jnp.stack(arrived_own + arrived_relay)
    step = (pos - groups % half) % half
    slots = jnp.where(groups // half == pair_here // half, step, half + step)
    return incoming, slots


def body(strain, pair_list, tile_live):
    window_count, local_rows, sample_count = strain.shape
    slot_count = tile_live.shape[0]
    n_pair = lax.axis_size("pair")
    n_win = lax.axis_size("win")
    pair_here = lax.axis_index("pair")
    win_here = lax.axis_index("win")
    b_dev = local_rows // C

    flat_rows = strain.reshape(window_count * local_rows, sample_count)
    whitened = whiten_rows(flat_rows, F).reshape(window_count, b_dev, C, 2 * F)

    lists = pair_list.reshape(n_pair, 2 * slot_count)
    wanted = lax.dynamic_slice_in_dim(pair_list, pair_here * slot_count, slot_count, 0)
    groups = wanted.reshape(2 * slot_count) // b_dev
    if n_pair == 8:
        incoming, slots = exchange_by_halves(whitened, lists, groups, pair_here, b_dev)
    else:
        outgoing = pick_blocks(whitened, block_choice(lists, pair_here, b_dev))
        incoming = lax.all_to_all(outgoing, "pair", 0, 0, tiled=True)
        slots = groups
    slots = jnp.clip(slots, 0, n_pair - 1)

    sub = 4
    own_rows = C // n_win
    n_y = n_win // 2
    bins = lax.iota(jnp.int32, F) + 1
    fine_lag = lax.iota(jnp.int32, sub) * DECIM
    coarse_lag = (lax.iota(jnp.int32, LAGS // sub) * sub - LAGS // 2) * DECIM
    cf, sf = cos_sin(fine_lag[:, None] * bins[None, :], sample_count)
    cc, sc = cos_sin(coarse_lag[:, None] * bins[None, :], sample_count)
    corr = tile_correlation(cc, sc, cf, sf, incoming, slots, sub, n_y, own_rows)

    core = win_here % 2
    y_here = win_here // 2
    send = corr[0]
    keep = corr[1].astype(jnp.float32)
    got = lax.ppermute(send, "win", [(w, w ^ 1) for w in range(n_win)])
    half = (keep + got.astype(jnp.float32)).reshape(LAGS, n_y, own_rows, slot_count * C)
    half = jnp.transpose(half, (1, 0, 2, 3))
    total = jnp.take(half, y_here, axis=0, mode="clip")
    for shift in range(1, n_y):
        dest = (y_here + shift) % n_y
        piece = jnp.take(half, dest, axis=0, mode="clip").astype(jnp.bfloat16)
        perm = [(w, ((w // 2 + shift) % n_y) * 2 + w % 2) for w in range(n_win)]
        total = total + lax.ppermute(piece, "win", perm).astype(jnp.float32)
    total = jnp.transpose(total.reshape(LAGS, own_rows, slot_count, C), (1, 2, 0, 3))

    live_local = tile_live.astype(jnp.float32)
    return total * live_local[None, :, None, None] / math.sqrt(F * window_count * n_win)


def solution(mesh):
    in_specs = (P("win", "pair", None), P(), P("pair"))
    out_specs = P("win", "pair", None, None)
    return jax.shard_map(body, mesh=mesh, in_specs=in_specs, out_specs=out_specs, check_vma=False)
```

```python
import functools
import math

import jax
import jax.numpy as jnp
from jax import lax
from jax.experimental import pallas as pl
from jax.experimental.pallas import tpu as pltpu
from jax.sharding import PartitionSpec as P

C = 128
F = 384
LAGS = 16
DECIM = 32
SPLIT = 128


def cos_sin(product, sample_count):
    angle = 2.0 * math.pi / sample_count * (product % sample_count).astype(jnp.float32)
    return jnp.cos(angle), jnp.sin(angle)


def dft_table(sample_count, bin_count):
    bin_index = lax.iota(jnp.int32, bin_count) + 1
    coarse = lax.iota(jnp.int32, sample_count // SPLIT) * SPLIT
    fine = lax.iota(jnp.int32, SPLIT)
    ca, sa = cos_sin(coarse[:, None] * bin_index[None, :], sample_count)
    cb, sb = cos_sin(fine[:, None] * bin_index[None, :], sample_count)
    cos_t = ca[:, None, :] * cb[None, :, :] - sa[:, None, :] * sb[None, :, :]
    sin_t = sa[:, None, :] * cb[None, :, :] + ca[:, None, :] * sb[None, :, :]
    table = jnp.concatenate([cos_t, -sin_t], axis=2).astype(jnp.bfloat16)
    return table.reshape(sample_count, 2 * bin_count)


def whiten_rows(strain_rows, table, bin_count):
    spectrum = jnp.dot(strain_rows, table, preferred_element_type=jnp.float32)
    real_part = spectrum[:, :bin_count]
    imag_part = spectrum[:, bin_count:]
    amplitude = jnp.sqrt(real_part * real_part + imag_part * imag_part)
    level = 0.2 * jnp.mean(amplitude, axis=1, keepdims=True) + 1e-06
    divisor = jnp.maximum(amplitude, level)
    return jnp.concatenate([real_part / divisor, imag_part / divisor], axis=1).astype(jnp.bfloat16)


def correlation_kernel(sub, n_y, own_rows, index_ref, cc_ref, sc_ref, cf_ref, sf_ref, left_ref, right_ref, out_ref):
    window_count = left_ref.shape[1]
    order = [(y * 2 + c) * own_rows for c in range(2) for y in range(n_y)]
    acc = None
    for w in range(window_count):
        left = left_ref[0, w].astype(jnp.float32)
        left = jnp.concatenate([left[r : r + own_rows] for r in order], axis=0)
        lre = left[:, :F]
        lim = left[:, F:]
        rre = right_ref[0, w, :, :F].astype(jnp.float32)
        rim = right_ref[0, w, :, F:].astype(jnp.float32)
        turned = []
        for l1 in range(sub):
            if l1 == 0:
                turned.append(right_ref[0, w])
                continue
            c = cf_ref[l1 : l1 + 1, :]
            s = sf_ref[l1 : l1 + 1, :]
            turned.append(jnp.concatenate([rre * c + rim * s, rim * c - rre * s], axis=1).astype(jnp.bfloat16))
        right_all = jnp.concatenate(turned, axis=0)
        parts = []
        for l2 in range(LAGS // sub):
            if l2 * sub == LAGS // 2:
                left_t = left.astype(jnp.bfloat16)
            else:
                c = cc_ref[l2 : l2 + 1, :]
                s = sc_ref[l2 : l2 + 1, :]
                left_t = jnp.concatenate([lre * c - lim * s, lre * s + lim * c], axis=1).astype(jnp.bfloat16)
            parts.append(
                lax.dot_general(left_t, right_all, (((1,), (1,)), ((), ())), preferred_element_type=jnp.float32)
            )
        acc = parts if acc is None else [a + p for a, p in zip(acc, parts)]
    half_rows = C // 2
    for l2, res in enumerate(acc):
        for l1 in range(sub):
            for part in range(2):
                out_ref[part, l2 * sub + l1] = res[part * half_rows : (part + 1) * half_rows, l1 * C : (l1 + 1) * C].astype(
                    out_ref.dtype
                )


def tile_correlation(cc, sc, cf, sf, incoming, slots, sub, n_y, own_rows):
    window_count = incoming.shape[1]
    slot_count = slots.shape[0] // 2
    table_spec = pl.BlockSpec(cc.shape, lambda t, idx: (0, 0))
    left_spec = pl.BlockSpec((1, window_count, C, 2 * F), lambda t, idx: (idx[2 * t], 0, 0, 0))
    right_spec = pl.BlockSpec((1, window_count, C, 2 * F), lambda t, idx: (idx[2 * t + 1], 0, 0, 0))
    flops = 2 * slot_count * window_count * C * 2 * F * LAGS * C
    grid_spec = pltpu.PrefetchScalarGridSpec(
        num_scalar_prefetch=1,
        grid=(slot_count,),
        in_specs=[table_spec] * 4 + [left_spec, right_spec],
        out_specs=pl.BlockSpec((2, LAGS, C // 2, C), lambda t, idx: (0, 0, 0, t)),
    )
    return pl.pallas_call(
        functools.partial(correlation_kernel, sub, n_y, own_rows),
        grid_spec=grid_spec,
        out_shape=jax.ShapeDtypeStruct((2, LAGS, C // 2, slot_count * C), jnp.bfloat16),
        cost_estimate=pl.CostEstimate(
            flops=flops, transcendentals=0, bytes_accessed=slot_count * (4 * window_count * C * F * 2 + 2 * C * LAGS * C)
        ),
    )(slots, cc, sc, cf, sf, incoming, incoming)


def block_choice(lists, group, b_dev):
    return jnp.sum(jnp.where((lists // b_dev) == group, lists % b_dev, 0), axis=1)


def pick_blocks(blocks, choice):
    pick = choice[:, None, None, None]
    out = jnp.broadcast_to(blocks[:, 0][None], choice.shape + blocks[:, 0].shape)
    for k in range(1, blocks.shape[1]):
        out = jnp.where(pick == k, blocks[:, k][None], out)
    return out


def exchange_by_halves(whitened, block_list, lists, groups, pair_here, b_dev):
    n_pair = lists.shape[0]
    half = n_pair // 2
    base = (pair_here // half) * half
    pos = pair_here % half
    across = [(p, p ^ half) for p in range(n_pair)]
    mirror_blocks = jnp.stack([lax.ppermute(block, "pair", across) for block in block_list], axis=1)
    own_choice = block_choice(lists, pair_here, b_dev)
    mirror_choice = block_choice(lists, pair_here ^ half, b_dev)
    arrived_own = []
    arrived_relay = []
    for d in range(half):
        dest = base + (pos + d) % half
        own = pick_blocks(whitened, jnp.take(own_choice, dest[None], mode="clip"))[0]
        relay = pick_blocks(mirror_blocks, jnp.take(mirror_choice, dest[None], mode="clip"))[0]
        if d:
            perm = [(p, (p // half) * half + (p % half + d) % half) for p in range(n_pair)]
            own = lax.ppermute(own, "pair", perm)
            relay = lax.ppermute(relay, "pair", perm)
        arrived_own.append(own)
        arrived_relay.append(relay)
    incoming = jnp.stack(arrived_own + arrived_relay)
    step = (pos - groups % half) % half
    slots = jnp.where(groups // half == pair_here // half, step, half + step)
    return incoming, slots


def body(strain, pair_list, tile_live):
    window_count, local_rows, sample_count = strain.shape
    slot_count = tile_live.shape[0]
    n_pair = lax.axis_size("pair")
    n_win = lax.axis_size("win")
    pair_here = lax.axis_index("pair")
    win_here = lax.axis_index("win")
    b_dev = local_rows // C

    table = dft_table(sample_count, F)
    block_list = [
        whiten_rows(strain[:, k * C : (k + 1) * C].reshape(window_count * C, sample_count), table, F).reshape(
            window_count, C, 2 * F
        )
        for k in range(b_dev)
    ]
    whitened = jnp.stack(block_list, axis=1)

    lists = pair_list.reshape(n_pair, 2 * slot_count)
    wanted = lax.dynamic_slice_in_dim(pair_list, pair_here * slot_count, slot_count, 0)
    groups = wanted.reshape(2 * slot_count) // b_dev
    if n_pair == 8:
        incoming, slots = exchange_by_halves(whitened, block_list, lists, groups, pair_here, b_dev)
    else:
        outgoing = pick_blocks(whitened, block_choice(lists, pair_here, b_dev))
        incoming = lax.all_to_all(outgoing, "pair", 0, 0, tiled=True)
        slots = groups
    slots = jnp.clip(slots, 0, n_pair - 1)

    sub = 4
    own_rows = C // n_win
    n_y = n_win // 2
    bins = lax.iota(jnp.int32, F) + 1
    fine_lag = lax.iota(jnp.int32, sub) * DECIM
    coarse_lag = (lax.iota(jnp.int32, LAGS // sub) * sub - LAGS // 2) * DECIM
    cf, sf = cos_sin(fine_lag[:, None] * bins[None, :], sample_count)
    cc, sc = cos_sin(coarse_lag[:, None] * bins[None, :], sample_count)
    corr = tile_correlation(cc, sc, cf, sf, incoming, slots, sub, n_y, own_rows)

    core = win_here % 2
    y_here = win_here // 2
    send = jnp.take(corr, 1 - core, axis=0, mode="clip")
    keep = jnp.take(corr, core, axis=0, mode="clip").astype(jnp.float32)
    got = lax.ppermute(send, "win", [(w, w ^ 1) for w in range(n_win)])
    half = (keep + got.astype(jnp.float32)).reshape(LAGS, n_y, own_rows, slot_count * C)
    half = jnp.transpose(half, (1, 0, 2, 3))
    total = jnp.take(half, y_here, axis=0, mode="clip")
    for shift in range(1, n_y):
        dest = (y_here + shift) % n_y
        piece = jnp.take(half, dest, axis=0, mode="clip").astype(jnp.bfloat16)
        perm = [(w, ((w // 2 + shift) % n_y) * 2 + w % 2) for w in range(n_win)]
        total = total + lax.ppermute(piece, "win", perm).astype(jnp.float32)
    total = jnp.transpose(total.reshape(LAGS, own_rows, slot_count, C), (1, 2, 0, 3))

    live_local = tile_live.astype(jnp.float32)
    return total * live_local[None, :, None, None] / math.sqrt(F * window_count * n_win)


def solution(mesh):
    in_specs = (P("win", "pair", None), P(), P("pair"))
    out_specs = P("win", "pair", None, None)
    return jax.shard_map(body, mesh=mesh, in_specs=in_specs, out_specs=out_specs, check_vma=False)
```

```python
import functools
import math

import jax
import jax.numpy as jnp
from jax import lax
from jax.experimental import pallas as pl
from jax.experimental.pallas import tpu as pltpu
from jax.sharding import PartitionSpec as P

C = 128
F = 384
LAGS = 16
DECIM = 32
SPLIT = 128


def cos_sin(product, sample_count):
    angle = 2.0 * math.pi / sample_count * (product % sample_count).astype(jnp.float32)
    return jnp.cos(angle), jnp.sin(angle)


def dft_table(sample_count, bin_count):
    bin_index = lax.iota(jnp.int32, bin_count) + 1
    coarse = lax.iota(jnp.int32, sample_count // SPLIT) * SPLIT
    fine = lax.iota(jnp.int32, SPLIT)
    ca, sa = cos_sin(coarse[:, None] * bin_index[None, :], sample_count)
    cb, sb = cos_sin(fine[:, None] * bin_index[None, :], sample_count)
    cos_t = ca[:, None, :] * cb[None, :, :] - sa[:, None, :] * sb[None, :, :]
    sin_t = sa[:, None, :] * cb[None, :, :] + ca[:, None, :] * sb[None, :, :]
    table = jnp.concatenate([cos_t, -sin_t], axis=2).astype(jnp.bfloat16)
    return table.reshape(sample_count, 2 * bin_count)


def whiten_rows(strain_rows, table, bin_count):
    spectrum = jnp.dot(strain_rows, table, preferred_element_type=jnp.float32)
    real_part = spectrum[:, :bin_count]
    imag_part = spectrum[:, bin_count:]
    amplitude = jnp.sqrt(real_part * real_part + imag_part * imag_part)
    level = 0.2 * jnp.mean(amplitude, axis=1, keepdims=True) + 1e-06
    divisor = jnp.maximum(amplitude, level)
    return jnp.concatenate([real_part / divisor, imag_part / divisor], axis=1).astype(jnp.bfloat16)


def correlation_kernel(sub, n_y, own_rows, target, index_ref, cc_ref, sc_ref, cf_ref, sf_ref, left_ref, right_ref, out_ref):
    window_count = left_ref.shape[1]
    win = lax.axis_index("win")
    core = win % 2
    if target is None:
        chips = list(range(n_y))
    else:
        chips = [(1 - win // 2) if target == 0 else win // 2]
    starts = [(y * 2 + cc) * own_rows for cc in (1 - core, core) for y in chips]
    part_rows = len(chips) * own_rows
    acc = None
    for w in range(window_count):
        left = jnp.concatenate(
            [left_ref[0, w, pl.ds(pl.multiple_of(r, own_rows), own_rows), :] for r in starts], axis=0
        ).astype(jnp.float32)
        lre = left[:, :F]
        lim = left[:, F:]
        rre = right_ref[0, w, :, :F].astype(jnp.float32)
        rim = right_ref[0, w, :, F:].astype(jnp.float32)
        turned = []
        for l1 in range(sub):
            if l1 == 0:
                turned.append(right_ref[0, w])
                continue
            c = cf_ref[l1 : l1 + 1, :]
            s = sf_ref[l1 : l1 + 1, :]
            turned.append(jnp.concatenate([rre * c + rim * s, rim * c - rre * s], axis=1).astype(jnp.bfloat16))
        right_all = jnp.concatenate(turned, axis=0)
        parts = []
        for l2 in range(LAGS // sub):
            if l2 * sub == LAGS // 2:
                left_t = left.astype(jnp.bfloat16)
            else:
                c = cc_ref[l2 : l2 + 1, :]
                s = sc_ref[l2 : l2 + 1, :]
                left_t = jnp.concatenate([lre * c - lim * s, lre * s + lim * c], axis=1).astype(jnp.bfloat16)
            parts.append(
                lax.dot_general(left_t, right_all, (((1,), (1,)), ((), ())), preferred_element_type=jnp.float32)
            )
        acc = parts if acc is None else [a + p for a, p in zip(acc, parts)]
    for l2, res in enumerate(acc):
        for l1 in range(sub):
            for part in range(2):
                out_ref[part, l2 * sub + l1] = res[part * part_rows : (part + 1) * part_rows, l1 * C : (l1 + 1) * C].astype(
                    out_ref.dtype
                )


def tile_correlation(cc, sc, cf, sf, incoming, slots, sub, n_y, own_rows, target=None, weight=1.0):
    window_count = incoming.shape[1]
    slot_count = slots.shape[0] // 2
    part_rows = own_rows * (n_y if target is None else 1)
    table_spec = pl.BlockSpec(cc.shape, lambda t, idx: (0, 0))
    left_spec = pl.BlockSpec((1, window_count, C, 2 * F), lambda t, idx: (idx[2 * t], 0, 0, 0))
    right_spec = pl.BlockSpec((1, window_count, C, 2 * F), lambda t, idx: (idx[2 * t + 1], 0, 0, 0))
    flops = int(weight * 2 * slot_count * window_count * 2 * part_rows * 2 * F * LAGS * C)
    grid_spec = pltpu.PrefetchScalarGridSpec(
        num_scalar_prefetch=1,
        grid=(slot_count,),
        in_specs=[table_spec] * 4 + [left_spec, right_spec],
        out_specs=pl.BlockSpec((2, LAGS, part_rows, C), lambda t, idx: (0, 0, 0, t)),
    )
    return pl.pallas_call(
        functools.partial(correlation_kernel, sub, n_y, own_rows, target),
        grid_spec=grid_spec,
        out_shape=jax.ShapeDtypeStruct((2, LAGS, part_rows, slot_count * C), jnp.bfloat16),
        cost_estimate=pl.CostEstimate(
            flops=max(flops, 1),
            transcendentals=0,
            bytes_accessed=int(weight * slot_count * (4 * window_count * C * F * 2 + 4 * part_rows * LAGS * C)),
        ),
    )(slots, cc, sc, cf, sf, incoming, incoming)


def block_choice(lists, group, b_dev):
    return jnp.sum(jnp.where((lists // b_dev) == group, lists % b_dev, 0), axis=1)


def pick_blocks(blocks, choice):
    pick = choice[:, None, None, None]
    out = jnp.broadcast_to(blocks[:, 0][None], choice.shape + blocks[:, 0].shape)
    for k in range(1, blocks.shape[1]):
        out = jnp.where(pick == k, blocks[:, k][None], out)
    return out


def exchange_by_halves(whitened, block_list, lists, groups, pair_here, b_dev):
    n_pair = lists.shape[0]
    half = n_pair // 2
    base = (pair_here // half) * half
    pos = pair_here % half
    across = [(p, p ^ half) for p in range(n_pair)]
    mirror_blocks = jnp.stack([lax.ppermute(block, "pair", across) for block in block_list], axis=1)
    own_choice = block_choice(lists, pair_here, b_dev)
    mirror_choice = block_choice(lists, pair_here ^ half, b_dev)
    arrived_own = []
    arrived_relay = []
    for d in range(half):
        dest = base + (pos + d) % half
        own = pick_blocks(whitened, jnp.take(own_choice, dest[None], mode="clip"))[0]
        relay = pick_blocks(mirror_blocks, jnp.take(mirror_choice, dest[None], mode="clip"))[0]
        if d:
            perm = [(p, (p // half) * half + (p % half + d) % half) for p in range(n_pair)]
            own = lax.ppermute(own, "pair", perm)
            relay = lax.ppermute(relay, "pair", perm)
        arrived_own.append(own)
        arrived_relay.append(relay)
    incoming = jnp.stack(arrived_own + arrived_relay)
    step = (pos - groups % half) % half
    slots = jnp.where(groups // half == pair_here // half, step, half + step)
    return incoming, slots


def window_sum(corr, win_here, n_win, own_rows, slot_count):
    n_y = n_win // 2
    y_here = win_here // 2
    got = lax.ppermute(corr[0], "win", [(w, w ^ 1) for w in range(n_win)])
    half = (corr[1].astype(jnp.float32) + got.astype(jnp.float32)).reshape(LAGS, n_y, own_rows, slot_count * C)
    half = jnp.transpose(half, (1, 0, 2, 3))
    total = jnp.take(half, y_here, axis=0, mode="clip")
    for shift in range(1, n_y):
        dest = (y_here + shift) % n_y
        piece = jnp.take(half, dest, axis=0, mode="clip").astype(jnp.bfloat16)
        perm = [(w, ((w // 2 + shift) % n_y) * 2 + w % 2) for w in range(n_win)]
        total = total + lax.ppermute(piece, "win", perm).astype(jnp.float32)
    return total


def body(strain, pair_list, tile_live):
    window_count, local_rows, sample_count = strain.shape
    slot_count = tile_live.shape[0]
    n_pair = lax.axis_size("pair")
    n_win = lax.axis_size("win")
    pair_here = lax.axis_index("pair")
    win_here = lax.axis_index("win")
    b_dev = local_rows // C

    table = dft_table(sample_count, F)
    block_list = [
        whiten_rows(strain[:, k * C : (k + 1) * C].reshape(window_count * C, sample_count), table, F).reshape(
            window_count, C, 2 * F
        )
        for k in range(b_dev)
    ]
    whitened = jnp.stack(block_list, axis=1)

    lists = pair_list.reshape(n_pair, 2 * slot_count)
    wanted = lax.dynamic_slice_in_dim(pair_list, pair_here * slot_count, slot_count, 0)
    groups = wanted.reshape(2 * slot_count) // b_dev
    if n_pair == 8:
        incoming, slots = exchange_by_halves(whitened, block_list, lists, groups, pair_here, b_dev)
    else:
        outgoing = pick_blocks(whitened, block_choice(lists, pair_here, b_dev))
        incoming = lax.all_to_all(outgoing, "pair", 0, 0, tiled=True)
        slots = groups
    slots = jnp.clip(slots, 0, n_pair - 1)

    sub = 4
    own_rows = C // n_win
    n_y = n_win // 2
    bins = lax.iota(jnp.int32, F) + 1
    fine_lag = lax.iota(jnp.int32, sub) * DECIM
    coarse_lag = (lax.iota(jnp.int32, LAGS // sub) * sub - LAGS // 2) * DECIM
    cf, sf = cos_sin(fine_lag[:, None] * bins[None, :], sample_count)
    cc, sc = cos_sin(coarse_lag[:, None] * bins[None, :], sample_count)
    core_pairs = [(w, w ^ 1) for w in range(n_win)]
    if n_y == 2 and own_rows % 16 == 0:
        far = tile_correlation(cc, sc, cf, sf, incoming, slots, sub, n_y, own_rows, target=0)
        got = lax.ppermute(far[0], "win", core_pairs)
        far_sum = (far[1].astype(jnp.float32) + got.astype(jnp.float32)).astype(jnp.bfloat16)
        later, far_sum = lax.optimization_barrier((incoming, far_sum))
        near = tile_correlation(cc, sc, cf, sf, later, slots, sub, n_y, own_rows, target=1, weight=0.01)
        across = lax.ppermute(far_sum, "win", [(w, w ^ 2) for w in range(n_win)])
        got = lax.ppermute(near[0], "win", core_pairs)
        total = near[1].astype(jnp.float32) + got.astype(jnp.float32) + across.astype(jnp.float32)
    else:
        corr = tile_correlation(cc, sc, cf, sf, incoming, slots, sub, n_y, own_rows)
        total = window_sum(corr, win_here, n_win, own_rows, slot_count)
    total = jnp.transpose(total.reshape(LAGS, own_rows, slot_count, C), (1, 2, 0, 3))

    live_local = tile_live.astype(jnp.float32)
    return total * live_local[None, :, None, None] / math.sqrt(F * window_count * n_win)


def solution(mesh):
    in_specs = (P("win", "pair", None), P(), P("pair"))
    out_specs = P("win", "pair", None, None)
    return jax.shard_map(body, mesh=mesh, in_specs=in_specs, out_specs=out_specs, check_vma=False)
```

```python
import functools
import math

import jax
import jax.numpy as jnp
from jax import lax
from jax.experimental import pallas as pl
from jax.experimental.pallas import tpu as pltpu
from jax.sharding import PartitionSpec as P

C = 128
F = 384
LAGS = 16
DECIM = 32
SPLIT = 128


def cos_sin(product, sample_count):
    angle = 2.0 * math.pi / sample_count * (product % sample_count).astype(jnp.float32)
    return jnp.cos(angle), jnp.sin(angle)


def dft_table(sample_count, bin_count):
    bin_index = lax.iota(jnp.int32, bin_count) + 1
    coarse = lax.iota(jnp.int32, sample_count // SPLIT) * SPLIT
    fine = lax.iota(jnp.int32, SPLIT)
    ca, sa = cos_sin(coarse[:, None] * bin_index[None, :], sample_count)
    cb, sb = cos_sin(fine[:, None] * bin_index[None, :], sample_count)
    cos_t = ca[:, None, :] * cb[None, :, :] - sa[:, None, :] * sb[None, :, :]
    sin_t = sa[:, None, :] * cb[None, :, :] + ca[:, None, :] * sb[None, :, :]
    table = jnp.concatenate([cos_t, -sin_t], axis=2).astype(jnp.bfloat16)
    return table.reshape(sample_count, 2 * bin_count)


def whiten_rows(strain_rows, table, bin_count):
    spectrum = jnp.dot(strain_rows, table, preferred_element_type=jnp.float32)
    real_part = spectrum[:, :bin_count]
    imag_part = spectrum[:, bin_count:]
    amplitude = jnp.sqrt(real_part * real_part + imag_part * imag_part)
    level = 0.2 * jnp.mean(amplitude, axis=1, keepdims=True) + 1e-06
    divisor = jnp.maximum(amplitude, level)
    return jnp.concatenate([real_part / divisor, imag_part / divisor], axis=1).astype(jnp.bfloat16)


def correlation_kernel(sub, n_y, own_rows, index_ref, cc_ref, sc_ref, cf_ref, sf_ref, left_ref, right_ref, out_ref):
    window_count = left_ref.shape[1]
    order = [(y * 2 + c) * own_rows for c in range(2) for y in range(n_y)]
    acc = None
    for w in range(window_count):
        left = left_ref[0, w].astype(jnp.float32)
        left = jnp.concatenate([left[r : r + own_rows] for r in order], axis=0)
        lre = left[:, :F]
        lim = left[:, F:]
        rre = right_ref[0, w, :, :F].astype(jnp.float32)
        rim = right_ref[0, w, :, F:].astype(jnp.float32)
        turned = []
        for l1 in range(sub):
            if l1 == 0:
                turned.append(right_ref[0, w])
                continue
            c = cf_ref[l1 : l1 + 1, :]
            s = sf_ref[l1 : l1 + 1, :]
            turned.append(jnp.concatenate([rre * c + rim * s, rim * c - rre * s], axis=1).astype(jnp.bfloat16))
        right_all = jnp.concatenate(turned, axis=0)
        lefts = []
        for l2 in range(LAGS // sub):
            if l2 * sub == LAGS // 2:
                lefts.append(left.astype(jnp.bfloat16))
            else:
                c = cc_ref[l2 : l2 + 1, :]
                s = sc_ref[l2 : l2 + 1, :]
                lefts.append(jnp.concatenate([lre * c - lim * s, lre * s + lim * c], axis=1).astype(jnp.bfloat16))
        res = lax.dot_general(
            jnp.concatenate(lefts, axis=0), right_all, (((1,), (1,)), ((), ())), preferred_element_type=jnp.float32
        )
        acc = res if acc is None else acc + res
    half_rows = C // 2
    for l2 in range(LAGS // sub):
        for l1 in range(sub):
            for part in range(2):
                rows = l2 * C + part * half_rows
                out_ref[part, l2 * sub + l1] = acc[rows : rows + half_rows, l1 * C : (l1 + 1) * C].astype(out_ref.dtype)


def tile_correlation(cc, sc, cf, sf, incoming, slots, sub, n_y, own_rows):
    window_count = incoming.shape[1]
    slot_count = slots.shape[0] // 2
    table_spec = pl.BlockSpec(cc.shape, lambda t, idx: (0, 0))
    left_spec = pl.BlockSpec((1, window_count, C, 2 * F), lambda t, idx: (idx[2 * t], 0, 0, 0))
    right_spec = pl.BlockSpec((1, window_count, C, 2 * F), lambda t, idx: (idx[2 * t + 1], 0, 0, 0))
    flops = 2 * slot_count * window_count * C * 2 * F * LAGS * C
    grid_spec = pltpu.PrefetchScalarGridSpec(
        num_scalar_prefetch=1,
        grid=(slot_count,),
        in_specs=[table_spec] * 4 + [left_spec, right_spec],
        out_specs=pl.BlockSpec((2, LAGS, C // 2, C), lambda t, idx: (0, 0, 0, t)),
    )
    return pl.pallas_call(
        functools.partial(correlation_kernel, sub, n_y, own_rows),
        grid_spec=grid_spec,
        out_shape=jax.ShapeDtypeStruct((2, LAGS, C // 2, slot_count * C), jnp.bfloat16),
        cost_estimate=pl.CostEstimate(
            flops=flops, transcendentals=0, bytes_accessed=slot_count * (4 * window_count * C * F * 2 + 2 * C * LAGS * C)
        ),
    )(slots, cc, sc, cf, sf, incoming, incoming)


def block_choice(lists, group, b_dev):
    return jnp.sum(jnp.where((lists // b_dev) == group, lists % b_dev, 0), axis=1)


def pick_blocks(blocks, choice):
    pick = choice[:, None, None, None]
    out = jnp.broadcast_to(blocks[:, 0][None], choice.shape + blocks[:, 0].shape)
    for k in range(1, blocks.shape[1]):
        out = jnp.where(pick == k, blocks[:, k][None], out)
    return out


def exchange_by_halves(whitened, block_list, lists, groups, pair_here, b_dev):
    n_pair = lists.shape[0]
    half = n_pair // 2
    base = (pair_here // half) * half
    pos = pair_here % half
    across = [(p, p ^ half) for p in range(n_pair)]
    mirror_blocks = jnp.stack([lax.ppermute(block, "pair", across) for block in block_list], axis=1)
    own_choice = block_choice(lists, pair_here, b_dev)
    mirror_choice = block_choice(lists, pair_here ^ half, b_dev)
    arrived_own = []
    arrived_relay = []
    for d in range(half):
        dest = base + (pos + d) % half
        own = pick_blocks(whitened, jnp.take(own_choice, dest[None], mode="clip"))[0]
        relay = pick_blocks(mirror_blocks, jnp.take(mirror_choice, dest[None], mode="clip"))[0]
        if d:
            perm = [(p, (p // half) * half + (p % half + d) % half) for p in range(n_pair)]
            own = lax.ppermute(own, "pair", perm)
            relay = lax.ppermute(relay, "pair", perm)
        arrived_own.append(own)
        arrived_relay.append(relay)
    incoming = jnp.stack(arrived_own + arrived_relay)
    step = (pos - groups % half) % half
    slots = jnp.where(groups // half == pair_here // half, step, half + step)
    return incoming, slots


def body(strain, pair_list, tile_live):
    window_count, local_rows, sample_count = strain.shape
    slot_count = tile_live.shape[0]
    n_pair = lax.axis_size("pair")
    n_win = lax.axis_size("win")
    pair_here = lax.axis_index("pair")
    win_here = lax.axis_index("win")
    b_dev = local_rows // C

    table = dft_table(sample_count, F)
    block_list = [
        whiten_rows(strain[:, k * C : (k + 1) * C].reshape(window_count * C, sample_count), table, F).reshape(
            window_count, C, 2 * F
        )
        for k in range(b_dev)
    ]
    whitened = jnp.stack(block_list, axis=1)

    lists = pair_list.reshape(n_pair, 2 * slot_count)
    wanted = lax.dynamic_slice_in_dim(pair_list, pair_here * slot_count, slot_count, 0)
    groups = wanted.reshape(2 * slot_count) // b_dev
    if n_pair == 8:
        incoming, slots = exchange_by_halves(whitened, block_list, lists, groups, pair_here, b_dev)
    else:
        outgoing = pick_blocks(whitened, block_choice(lists, pair_here, b_dev))
        incoming = lax.all_to_all(outgoing, "pair", 0, 0, tiled=True)
        slots = groups
    slots = jnp.clip(slots, 0, n_pair - 1)

    sub = 4
    own_rows = C // n_win
    n_y = n_win // 2
    bins = lax.iota(jnp.int32, F) + 1
    fine_lag = lax.iota(jnp.int32, sub) * DECIM
    coarse_lag = (lax.iota(jnp.int32, LAGS // sub) * sub - LAGS // 2) * DECIM
    cf, sf = cos_sin(fine_lag[:, None] * bins[None, :], sample_count)
    cc, sc = cos_sin(coarse_lag[:, None] * bins[None, :], sample_count)
    corr = tile_correlation(cc, sc, cf, sf, incoming, slots, sub, n_y, own_rows)

    core = win_here % 2
    y_here = win_here // 2
    send = jnp.take(corr, 1 - core, axis=0, mode="clip")
    keep = jnp.take(corr, core, axis=0, mode="clip").astype(jnp.float32)
    got = lax.ppermute(send, "win", [(w, w ^ 1) for w in range(n_win)])
    half = (keep + got.astype(jnp.float32)).reshape(LAGS, n_y, own_rows, slot_count * C)
    half = jnp.transpose(half, (1, 0, 2, 3))
    total = jnp.take(half, y_here, axis=0, mode="clip")
    for shift in range(1, n_y):
        dest = (y_here + shift) % n_y
        piece = jnp.take(half, dest, axis=0, mode="clip").astype(jnp.bfloat16)
        perm = [(w, ((w // 2 + shift) % n_y) * 2 + w % 2) for w in range(n_win)]
        total = total + lax.ppermute(piece, "win", perm).astype(jnp.float32)
    total = jnp.transpose(total.reshape(LAGS, own_rows, slot_count, C), (1, 2, 0, 3))

    live_local = tile_live.astype(jnp.float32)
    return total * live_local[None, :, None, None] / math.sqrt(F * window_count * n_win)


def solution(mesh):
    in_specs = (P("win", "pair", None), P(), P("pair"))
    out_specs = P("win", "pair", None, None)
    return jax.shard_map(body, mesh=mesh, in_specs=in_specs, out_specs=out_specs, check_vma=False)
```

```python
import functools
import math

import jax
import jax.numpy as jnp
from jax import lax
from jax.experimental import pallas as pl
from jax.experimental.pallas import tpu as pltpu
from jax.sharding import PartitionSpec as P

C = 128
F = 384
LAGS = 16
DECIM = 32
SPLIT = 128


def cos_sin(product, sample_count):
    angle = 2.0 * math.pi / sample_count * (product % sample_count).astype(jnp.float32)
    return jnp.cos(angle), jnp.sin(angle)


def dft_table(sample_count, bin_count):
    bin_index = lax.iota(jnp.int32, bin_count) + 1
    coarse = lax.iota(jnp.int32, sample_count // SPLIT) * SPLIT
    fine = lax.iota(jnp.int32, SPLIT)
    ca, sa = cos_sin(coarse[:, None] * bin_index[None, :], sample_count)
    cb, sb = cos_sin(fine[:, None] * bin_index[None, :], sample_count)
    cos_t = ca[:, None, :] * cb[None, :, :] - sa[:, None, :] * sb[None, :, :]
    sin_t = sa[:, None, :] * cb[None, :, :] + ca[:, None, :] * sb[None, :, :]
    table = jnp.concatenate([cos_t, -sin_t], axis=2).astype(jnp.bfloat16)
    return table.reshape(sample_count, 2 * bin_count)


def whiten_rows(strain_rows, table, bin_count):
    spectrum = jnp.dot(strain_rows, table, preferred_element_type=jnp.float32)
    real_part = spectrum[:, :bin_count]
    imag_part = spectrum[:, bin_count:]
    amplitude = jnp.sqrt(real_part * real_part + imag_part * imag_part)
    level = 0.2 * jnp.mean(amplitude, axis=1, keepdims=True) + 1e-06
    divisor = jnp.maximum(amplitude, level)
    return jnp.concatenate([real_part / divisor, imag_part / divisor], axis=1).astype(jnp.bfloat16)


def correlation_kernel(sub, n_y, own_rows, target, index_ref, cc_ref, sc_ref, cf_ref, sf_ref, left_ref, right_ref, out_ref):
    window_count = left_ref.shape[1]
    win = lax.axis_index("win")
    core = win % 2
    if target is None:
        chips = list(range(n_y))
    else:
        chips = [(1 - win // 2) if target == 0 else win // 2]
    starts = [(y * 2 + cc) * own_rows for cc in (1 - core, core) for y in chips]
    part_rows = len(chips) * own_rows
    acc = None
    for w in range(window_count):
        left = jnp.concatenate(
            [left_ref[0, w, pl.ds(pl.multiple_of(r, own_rows), own_rows), :] for r in starts], axis=0
        ).astype(jnp.float32)
        lre = left[:, :F]
        lim = left[:, F:]
        rre = right_ref[0, w, :, :F].astype(jnp.float32)
        rim = right_ref[0, w, :, F:].astype(jnp.float32)
        turned = []
        for l1 in range(sub):
            if l1 == 0:
                turned.append(right_ref[0, w])
                continue
            c = cf_ref[l1 : l1 + 1, :]
            s = sf_ref[l1 : l1 + 1, :]
            turned.append(jnp.concatenate([rre * c + rim * s, rim * c - rre * s], axis=1).astype(jnp.bfloat16))
        right_all = jnp.concatenate(turned, axis=0)
        lefts = []
        for l2 in range(LAGS // sub):
            if l2 * sub == LAGS // 2:
                lefts.append(left.astype(jnp.bfloat16))
            else:
                c = cc_ref[l2 : l2 + 1, :]
                s = sc_ref[l2 : l2 + 1, :]
                lefts.append(jnp.concatenate([lre * c - lim * s, lre * s + lim * c], axis=1).astype(jnp.bfloat16))
        res = lax.dot_general(
            jnp.concatenate(lefts, axis=0), right_all, (((1,), (1,)), ((), ())), preferred_element_type=jnp.float32
        )
        acc = res if acc is None else acc + res
    block_rows = 2 * part_rows
    for l2 in range(LAGS // sub):
        for l1 in range(sub):
            for part in range(2):
                rows = l2 * block_rows + part * part_rows
                out_ref[part, l2 * sub + l1] = acc[rows : rows + part_rows, l1 * C : (l1 + 1) * C].astype(out_ref.dtype)


def tile_correlation(cc, sc, cf, sf, incoming, slots, sub, n_y, own_rows, target=None, weight=1.0):
    window_count = incoming.shape[1]
    slot_count = slots.shape[0] // 2
    part_rows = own_rows * (n_y if target is None else 1)
    table_spec = pl.BlockSpec(cc.shape, lambda t, idx: (0, 0))
    left_spec = pl.BlockSpec((1, window_count, C, 2 * F), lambda t, idx: (idx[2 * t], 0, 0, 0))
    right_spec = pl.BlockSpec((1, window_count, C, 2 * F), lambda t, idx: (idx[2 * t + 1], 0, 0, 0))
    flops = int(weight * 2 * slot_count * window_count * 2 * part_rows * 2 * F * LAGS * C)
    grid_spec = pltpu.PrefetchScalarGridSpec(
        num_scalar_prefetch=1,
        grid=(slot_count,),
        in_specs=[table_spec] * 4 + [left_spec, right_spec],
        out_specs=pl.BlockSpec((2, LAGS, part_rows, C), lambda t, idx: (0, 0, 0, t)),
    )
    return pl.pallas_call(
        functools.partial(correlation_kernel, sub, n_y, own_rows, target),
        grid_spec=grid_spec,
        out_shape=jax.ShapeDtypeStruct((2, LAGS, part_rows, slot_count * C), jnp.bfloat16),
        cost_estimate=pl.CostEstimate(
            flops=max(flops, 1),
            transcendentals=0,
            bytes_accessed=int(weight * slot_count * (4 * window_count * C * F * 2 + 4 * part_rows * LAGS * C)),
        ),
    )(slots, cc, sc, cf, sf, incoming, incoming)


def block_choice(lists, group, b_dev):
    return jnp.sum(jnp.where((lists // b_dev) == group, lists % b_dev, 0), axis=1)


def pick_blocks(blocks, choice):
    pick = choice[:, None, None, None]
    out = jnp.broadcast_to(blocks[:, 0][None], choice.shape + blocks[:, 0].shape)
    for k in range(1, blocks.shape[1]):
        out = jnp.where(pick == k, blocks[:, k][None], out)
    return out


def exchange_by_halves(whitened, block_list, lists, groups, pair_here, b_dev):
    n_pair = lists.shape[0]
    half = n_pair // 2
    base = (pair_here // half) * half
    pos = pair_here % half
    across = [(p, p ^ half) for p in range(n_pair)]
    mirror_blocks = jnp.stack([lax.ppermute(block, "pair", across) for block in block_list], axis=1)
    own_choice = block_choice(lists, pair_here, b_dev)
    mirror_choice = block_choice(lists, pair_here ^ half, b_dev)
    arrived_own = []
    arrived_relay = []
    for d in range(half):
        dest = base + (pos + d) % half
        own = pick_blocks(whitened, jnp.take(own_choice, dest[None], mode="clip"))[0]
        relay = pick_blocks(mirror_blocks, jnp.take(mirror_choice, dest[None], mode="clip"))[0]
        if d:
            perm = [(p, (p // half) * half + (p % half + d) % half) for p in range(n_pair)]
            own = lax.ppermute(own, "pair", perm)
            relay = lax.ppermute(relay, "pair", perm)
        arrived_own.append(own)
        arrived_relay.append(relay)
    incoming = jnp.stack(arrived_own + arrived_relay)
    step = (pos - groups % half) % half
    slots = jnp.where(groups // half == pair_here // half, step, half + step)
    return incoming, slots


def window_sum(corr, win_here, n_win, own_rows, slot_count):
    n_y = n_win // 2
    y_here = win_here // 2
    got = lax.ppermute(corr[0], "win", [(w, w ^ 1) for w in range(n_win)])
    half = (corr[1].astype(jnp.float32) + got.astype(jnp.float32)).reshape(LAGS, n_y, own_rows, slot_count * C)
    half = jnp.transpose(half, (1, 0, 2, 3))
    total = jnp.take(half, y_here, axis=0, mode="clip")
    for shift in range(1, n_y):
        dest = (y_here + shift) % n_y
        piece = jnp.take(half, dest, axis=0, mode="clip").astype(jnp.bfloat16)
        perm = [(w, ((w // 2 + shift) % n_y) * 2 + w % 2) for w in range(n_win)]
        total = total + lax.ppermute(piece, "win", perm).astype(jnp.float32)
    return total


def body(strain, pair_list, tile_live):
    window_count, local_rows, sample_count = strain.shape
    slot_count = tile_live.shape[0]
    n_pair = lax.axis_size("pair")
    n_win = lax.axis_size("win")
    pair_here = lax.axis_index("pair")
    win_here = lax.axis_index("win")
    b_dev = local_rows // C

    table = dft_table(sample_count, F)
    block_list = [
        whiten_rows(strain[:, k * C : (k + 1) * C].reshape(window_count * C, sample_count), table, F).reshape(
            window_count, C, 2 * F
        )
        for k in range(b_dev)
    ]
    whitened = jnp.stack(block_list, axis=1)

    lists = pair_list.reshape(n_pair, 2 * slot_count)
    wanted = lax.dynamic_slice_in_dim(pair_list, pair_here * slot_count, slot_count, 0)
    groups = wanted.reshape(2 * slot_count) // b_dev
    if n_pair == 8:
        incoming, slots = exchange_by_halves(whitened, block_list, lists, groups, pair_here, b_dev)
    else:
        outgoing = pick_blocks(whitened, block_choice(lists, pair_here, b_dev))
        incoming = lax.all_to_all(outgoing, "pair", 0, 0, tiled=True)
        slots = groups
    slots = jnp.clip(slots, 0, n_pair - 1)

    sub = 4
    own_rows = C // n_win
    n_y = n_win // 2
    bins = lax.iota(jnp.int32, F) + 1
    fine_lag = lax.iota(jnp.int32, sub) * DECIM
    coarse_lag = (lax.iota(jnp.int32, LAGS // sub) * sub - LAGS // 2) * DECIM
    cf, sf = cos_sin(fine_lag[:, None] * bins[None, :], sample_count)
    cc, sc = cos_sin(coarse_lag[:, None] * bins[None, :], sample_count)
    core_pairs = [(w, w ^ 1) for w in range(n_win)]
    if n_y == 2 and own_rows % 16 == 0:
        far = tile_correlation(cc, sc, cf, sf, incoming, slots, sub, n_y, own_rows, target=0)
        got = lax.ppermute(far[0], "win", core_pairs)
        far_sum = (far[1].astype(jnp.float32) + got.astype(jnp.float32)).astype(jnp.bfloat16)
        later, far_sum = lax.optimization_barrier((incoming, far_sum))
        near = tile_correlation(cc, sc, cf, sf, later, slots, sub, n_y, own_rows, target=1, weight=0.01)
        across = lax.ppermute(far_sum, "win", [(w, w ^ 2) for w in range(n_win)])
        got = lax.ppermute(near[0], "win", core_pairs)
        total = near[1].astype(jnp.float32) + got.astype(jnp.float32) + across.astype(jnp.float32)
    else:
        corr = tile_correlation(cc, sc, cf, sf, incoming, slots, sub, n_y, own_rows)
        total = window_sum(corr, win_here, n_win, own_rows, slot_count)
    total = jnp.transpose(total.reshape(LAGS, own_rows, slot_count, C), (1, 2, 0, 3))

    live_local = tile_live.astype(jnp.float32)
    return total * live_local[None, :, None, None] / math.sqrt(F * window_count * n_win)


def solution(mesh):
    in_specs = (P("win", "pair", None), P(), P("pair"))
    out_specs = P("win", "pair", None, None)
    return jax.shard_map(body, mesh=mesh, in_specs=in_specs, out_specs=out_specs, check_vma=False)
```

```python
import functools
import math

import jax
import jax.numpy as jnp
from jax import lax
from jax.experimental import pallas as pl
from jax.experimental.pallas import tpu as pltpu
from jax.sharding import PartitionSpec as P

C = 128
F = 384
LAGS = 16
DECIM = 32
SPLIT = 128


def cos_sin(product, sample_count):
    angle = 2.0 * math.pi / sample_count * (product % sample_count).astype(jnp.float32)
    return jnp.cos(angle), jnp.sin(angle)


def dft_table(sample_count, bin_count):
    bin_index = lax.iota(jnp.int32, bin_count) + 1
    coarse = lax.iota(jnp.int32, sample_count // SPLIT) * SPLIT
    fine = lax.iota(jnp.int32, SPLIT)
    ca, sa = cos_sin(coarse[:, None] * bin_index[None, :], sample_count)
    cb, sb = cos_sin(fine[:, None] * bin_index[None, :], sample_count)
    cos_t = ca[:, None, :] * cb[None, :, :] - sa[:, None, :] * sb[None, :, :]
    sin_t = sa[:, None, :] * cb[None, :, :] + ca[:, None, :] * sb[None, :, :]
    table = jnp.concatenate([cos_t, -sin_t], axis=2).astype(jnp.bfloat16)
    return table.reshape(sample_count, 2 * bin_count)


def whiten_rows(strain_rows, table, bin_count):
    spectrum = jnp.dot(strain_rows, table, preferred_element_type=jnp.float32)
    real_part = spectrum[:, :bin_count]
    imag_part = spectrum[:, bin_count:]
    amplitude = jnp.sqrt(real_part * real_part + imag_part * imag_part)
    level = 0.2 * jnp.mean(amplitude, axis=1, keepdims=True) + 1e-06
    divisor = jnp.maximum(amplitude, level)
    return jnp.concatenate([real_part / divisor, imag_part / divisor], axis=1).astype(jnp.bfloat16)


def correlation_kernel(sub, n_y, own_rows, index_ref, cc_ref, sc_ref, cf_ref, sf_ref, left_ref, right_ref, out_ref):
    window_count = left_ref.shape[1]
    order = [(y * 2 + c) * own_rows for c in range(2) for y in range(n_y)]
    acc = None
    for w in range(window_count):
        left = left_ref[0, w].astype(jnp.float32)
        left = jnp.concatenate([left[r : r + own_rows] for r in order], axis=0)
        lre = left[:, :F].astype(jnp.bfloat16)
        lim = left[:, F:].astype(jnp.bfloat16)
        rre = right_ref[0, w, :, :F]
        rim = right_ref[0, w, :, F:]
        turned = []
        for l1 in range(sub):
            if l1 == 0:
                turned.append(right_ref[0, w])
                continue
            c = cf_ref[l1 : l1 + 1, :].astype(jnp.bfloat16)
            s = sf_ref[l1 : l1 + 1, :].astype(jnp.bfloat16)
            turned.append(jnp.concatenate([rre * c + rim * s, rim * c - rre * s], axis=1).astype(jnp.bfloat16))
        right_all = jnp.concatenate(turned, axis=0)
        lefts = []
        for l2 in range(LAGS // sub):
            if l2 * sub == LAGS // 2:
                lefts.append(left.astype(jnp.bfloat16))
            else:
                c = cc_ref[l2 : l2 + 1, :].astype(jnp.bfloat16)
                s = sc_ref[l2 : l2 + 1, :].astype(jnp.bfloat16)
                lefts.append(jnp.concatenate([lre * c - lim * s, lre * s + lim * c], axis=1).astype(jnp.bfloat16))
        res = lax.dot_general(
            jnp.concatenate(lefts, axis=0), right_all, (((1,), (1,)), ((), ())), preferred_element_type=jnp.float32
        )
        acc = res if acc is None else acc + res
    half_rows = C // 2
    for l2 in range(LAGS // sub):
        for l1 in range(sub):
            for part in range(2):
                rows = l2 * C + part * half_rows
                out_ref[part, l2 * sub + l1] = acc[rows : rows + half_rows, l1 * C : (l1 + 1) * C].astype(out_ref.dtype)


def tile_correlation(cc, sc, cf, sf, incoming, slots, sub, n_y, own_rows):
    window_count = incoming.shape[1]
    slot_count = slots.shape[0] // 2
    table_spec = pl.BlockSpec(cc.shape, lambda t, idx: (0, 0))
    left_spec = pl.BlockSpec((1, window_count, C, 2 * F), lambda t, idx: (idx[2 * t], 0, 0, 0))
    right_spec = pl.BlockSpec((1, window_count, C, 2 * F), lambda t, idx: (idx[2 * t + 1], 0, 0, 0))
    flops = 2 * slot_count * window_count * C * 2 * F * LAGS * C
    grid_spec = pltpu.PrefetchScalarGridSpec(
        num_scalar_prefetch=1,
        grid=(slot_count,),
        in_specs=[table_spec] * 4 + [left_spec, right_spec],
        out_specs=pl.BlockSpec((2, LAGS, C // 2, C), lambda t, idx: (0, 0, 0, t)),
    )
    return pl.pallas_call(
        functools.partial(correlation_kernel, sub, n_y, own_rows),
        grid_spec=grid_spec,
        out_shape=jax.ShapeDtypeStruct((2, LAGS, C // 2, slot_count * C), jnp.bfloat16),
        cost_estimate=pl.CostEstimate(
            flops=flops, transcendentals=0, bytes_accessed=slot_count * (4 * window_count * C * F * 2 + 2 * C * LAGS * C)
        ),
    )(slots, cc, sc, cf, sf, incoming, incoming)


def block_choice(lists, group, b_dev):
    return jnp.sum(jnp.where((lists // b_dev) == group, lists % b_dev, 0), axis=1)


def pick_blocks(blocks, choice):
    pick = choice[:, None, None, None]
    out = jnp.broadcast_to(blocks[:, 0][None], choice.shape + blocks[:, 0].shape)
    for k in range(1, blocks.shape[1]):
        out = jnp.where(pick == k, blocks[:, k][None], out)
    return out


def exchange_by_halves(whitened, block_list, lists, groups, pair_here, b_dev):
    n_pair = lists.shape[0]
    half = n_pair // 2
    base = (pair_here // half) * half
    pos = pair_here % half
    across = [(p, p ^ half) for p in range(n_pair)]
    mirror_blocks = jnp.stack([lax.ppermute(block, "pair", across) for block in block_list], axis=1)
    own_choice = block_choice(lists, pair_here, b_dev)
    mirror_choice = block_choice(lists, pair_here ^ half, b_dev)
    arrived_own = []
    arrived_relay = []
    for d in range(half):
        dest = base + (pos + d) % half
        own = pick_blocks(whitened, jnp.take(own_choice, dest[None], mode="clip"))[0]
        relay = pick_blocks(mirror_blocks, jnp.take(mirror_choice, dest[None], mode="clip"))[0]
        if d:
            perm = [(p, (p // half) * half + (p % half + d) % half) for p in range(n_pair)]
            own = lax.ppermute(own, "pair", perm)
            relay = lax.ppermute(relay, "pair", perm)
        arrived_own.append(own)
        arrived_relay.append(relay)
    incoming = jnp.stack(arrived_own + arrived_relay)
    step = (pos - groups % half) % half
    slots = jnp.where(groups // half == pair_here // half, step, half + step)
    return incoming, slots


def body(strain, pair_list, tile_live):
    window_count, local_rows, sample_count = strain.shape
    slot_count = tile_live.shape[0]
    n_pair = lax.axis_size("pair")
    n_win = lax.axis_size("win")
    pair_here = lax.axis_index("pair")
    win_here = lax.axis_index("win")
    b_dev = local_rows // C

    table = dft_table(sample_count, F)
    block_list = [
        whiten_rows(strain[:, k * C : (k + 1) * C].reshape(window_count * C, sample_count), table, F).reshape(
            window_count, C, 2 * F
        )
        for k in range(b_dev)
    ]
    whitened = jnp.stack(block_list, axis=1)

    lists = pair_list.reshape(n_pair, 2 * slot_count)
    wanted = lax.dynamic_slice_in_dim(pair_list, pair_here * slot_count, slot_count, 0)
    groups = wanted.reshape(2 * slot_count) // b_dev
    if n_pair == 8:
        incoming, slots = exchange_by_halves(whitened, block_list, lists, groups, pair_here, b_dev)
    else:
        outgoing = pick_blocks(whitened, block_choice(lists, pair_here, b_dev))
        incoming = lax.all_to_all(outgoing, "pair", 0, 0, tiled=True)
        slots = groups
    slots = jnp.clip(slots, 0, n_pair - 1)

    sub = 4
    own_rows = C // n_win
    n_y = n_win // 2
    bins = lax.iota(jnp.int32, F) + 1
    fine_lag = lax.iota(jnp.int32, sub) * DECIM
    coarse_lag = (lax.iota(jnp.int32, LAGS // sub) * sub - LAGS // 2) * DECIM
    cf, sf = cos_sin(fine_lag[:, None] * bins[None, :], sample_count)
    cc, sc = cos_sin(coarse_lag[:, None] * bins[None, :], sample_count)
    corr = tile_correlation(cc, sc, cf, sf, incoming, slots, sub, n_y, own_rows)

    core = win_here % 2
    y_here = win_here // 2
    send = jnp.take(corr, 1 - core, axis=0, mode="clip")
    keep = jnp.take(corr, core, axis=0, mode="clip").astype(jnp.float32)
    got = lax.ppermute(send, "win", [(w, w ^ 1) for w in range(n_win)])
    half = (keep + got.astype(jnp.float32)).reshape(LAGS, n_y, own_rows, slot_count * C)
    half = jnp.transpose(half, (1, 0, 2, 3))
    total = jnp.take(half, y_here, axis=0, mode="clip")
    for shift in range(1, n_y):
        dest = (y_here + shift) % n_y
        piece = jnp.take(half, dest, axis=0, mode="clip").astype(jnp.bfloat16)
        perm = [(w, ((w // 2 + shift) % n_y) * 2 + w % 2) for w in range(n_win)]
        total = total + lax.ppermute(piece, "win", perm).astype(jnp.float32)
    total = jnp.transpose(total.reshape(LAGS, own_rows, slot_count, C), (1, 2, 0, 3))

    live_local = tile_live.astype(jnp.float32)
    return total * live_local[None, :, None, None] / math.sqrt(F * window_count * n_win)


def solution(mesh):
    in_specs = (P("win", "pair", None), P(), P("pair"))
    out_specs = P("win", "pair", None, None)
    return jax.shard_map(body, mesh=mesh, in_specs=in_specs, out_specs=out_specs, check_vma=False)
```

```python
import functools
import math

import jax
import jax.numpy as jnp
from jax import lax
from jax.experimental import pallas as pl
from jax.experimental.pallas import tpu as pltpu
from jax.sharding import PartitionSpec as P

C = 128
F = 384
LAGS = 16
DECIM = 32
SPLIT = 128


def cos_sin(product, sample_count):
    angle = 2.0 * math.pi / sample_count * (product % sample_count).astype(jnp.float32)
    return jnp.cos(angle), jnp.sin(angle)


def dft_table(sample_count, bin_count):
    bin_index = lax.iota(jnp.int32, bin_count) + 1
    coarse = lax.iota(jnp.int32, sample_count // SPLIT) * SPLIT
    fine = lax.iota(jnp.int32, SPLIT)
    ca, sa = cos_sin(coarse[:, None] * bin_index[None, :], sample_count)
    cb, sb = cos_sin(fine[:, None] * bin_index[None, :], sample_count)
    cos_t = ca[:, None, :] * cb[None, :, :] - sa[:, None, :] * sb[None, :, :]
    sin_t = sa[:, None, :] * cb[None, :, :] + ca[:, None, :] * sb[None, :, :]
    table = jnp.concatenate([cos_t, -sin_t], axis=2).astype(jnp.bfloat16)
    return table.reshape(sample_count, 2 * bin_count)


def whiten_rows(strain_rows, table, bin_count):
    spectrum = jnp.dot(strain_rows, table, preferred_element_type=jnp.float32)
    real_part = spectrum[:, :bin_count]
    imag_part = spectrum[:, bin_count:]
    amplitude = jnp.sqrt(real_part * real_part + imag_part * imag_part)
    level = 0.2 * jnp.mean(amplitude, axis=1, keepdims=True) + 1e-06
    divisor = jnp.maximum(amplitude, level)
    return jnp.concatenate([real_part / divisor, imag_part / divisor], axis=1).astype(jnp.bfloat16)


def correlation_kernel(sub, n_y, own_rows, index_ref, cc_ref, sc_ref, cf_ref, sf_ref, left_ref, right_ref, out_ref):
    window_count = left_ref.shape[1]
    order = [(y * 2 + c) * own_rows for c in range(2) for y in range(n_y)]
    acc = None
    for w in range(window_count):
        left = left_ref[0, w].astype(jnp.float32)
        left = jnp.concatenate([left[r : r + own_rows] for r in order], axis=0)
        lre = left[:, :F]
        lim = left[:, F:]
        rre = right_ref[0, w, :, :F].astype(jnp.float32)
        rim = right_ref[0, w, :, F:].astype(jnp.float32)
        turned = []
        for l1 in range(sub):
            if l1 == 0:
                turned.append(right_ref[0, w])
                continue
            c = cf_ref[l1 : l1 + 1, :]
            s = sf_ref[l1 : l1 + 1, :]
            turned.append(jnp.concatenate([rre * c + rim * s, rim * c - rre * s], axis=1).astype(jnp.bfloat16))
        right_all = jnp.concatenate(turned, axis=0)
        lefts = []
        for l2 in range(LAGS // sub):
            if l2 * sub == LAGS // 2:
                lefts.append(left.astype(jnp.bfloat16))
            else:
                c = cc_ref[l2 : l2 + 1, :]
                s = sc_ref[l2 : l2 + 1, :]
                lefts.append(jnp.concatenate([lre * c - lim * s, lre * s + lim * c], axis=1).astype(jnp.bfloat16))
        res = lax.dot_general(
            jnp.concatenate(lefts, axis=0), right_all, (((1,), (1,)), ((), ())), preferred_element_type=jnp.float32
        )
        acc = res if acc is None else acc + res
    half_rows = C // 2
    for l2 in range(LAGS // sub):
        for l1 in range(sub):
            for part in range(2):
                rows = l2 * C + part * half_rows
                out_ref[part, l2 * sub + l1] = acc[rows : rows + half_rows, l1 * C : (l1 + 1) * C].astype(out_ref.dtype)


def tile_correlation(cc, sc, cf, sf, incoming, slots, sub, n_y, own_rows):
    window_count = incoming.shape[1]
    slot_count = slots.shape[0] // 2
    table_spec = pl.BlockSpec(cc.shape, lambda t, idx: (0, 0))
    left_spec = pl.BlockSpec((1, window_count, C, 2 * F), lambda t, idx: (idx[2 * t], 0, 0, 0))
    right_spec = pl.BlockSpec((1, window_count, C, 2 * F), lambda t, idx: (idx[2 * t + 1], 0, 0, 0))
    flops = 2 * slot_count * window_count * C * 2 * F * LAGS * C
    grid_spec = pltpu.PrefetchScalarGridSpec(
        num_scalar_prefetch=1,
        grid=(slot_count,),
        in_specs=[table_spec] * 4 + [left_spec, right_spec],
        out_specs=pl.BlockSpec((2, LAGS, C // 2, C), lambda t, idx: (0, 0, 0, t)),
    )
    return pl.pallas_call(
        functools.partial(correlation_kernel, sub, n_y, own_rows),
        grid_spec=grid_spec,
        out_shape=jax.ShapeDtypeStruct((2, LAGS, C // 2, slot_count * C), jnp.bfloat16),
        cost_estimate=pl.CostEstimate(
            flops=flops, transcendentals=0, bytes_accessed=slot_count * (4 * window_count * C * F * 2 + 2 * C * LAGS * C)
        ),
    )(slots, cc, sc, cf, sf, incoming, incoming)


def block_choice(lists, group, b_dev):
    return jnp.sum(jnp.where((lists // b_dev) == group, lists % b_dev, 0), axis=1)


def pick_blocks(blocks, choice):
    pick = choice[:, None, None, None]
    out = jnp.broadcast_to(blocks[:, 0][None], choice.shape + blocks[:, 0].shape)
    for k in range(1, blocks.shape[1]):
        out = jnp.where(pick == k, blocks[:, k][None], out)
    return out


def exchange_by_halves(whitened, block_list, lists, groups, pair_here, b_dev):
    n_pair = lists.shape[0]
    half = n_pair // 2
    base = (pair_here // half) * half
    pos = pair_here % half
    across = [(p, p ^ half) for p in range(n_pair)]
    mirror_blocks = jnp.stack([lax.ppermute(block, "pair", across) for block in block_list], axis=1)
    own_choice = block_choice(lists, pair_here, b_dev)
    mirror_choice = block_choice(lists, pair_here ^ half, b_dev)
    arrived_own = []
    arrived_relay = []
    for d in range(half):
        dest = base + (pos + d) % half
        own = pick_blocks(whitened, jnp.take(own_choice, dest[None], mode="clip"))[0]
        relay = pick_blocks(mirror_blocks, jnp.take(mirror_choice, dest[None], mode="clip"))[0]
        if d:
            perm = [(p, (p // half) * half + (p % half + d) % half) for p in range(n_pair)]
            own = lax.ppermute(own, "pair", perm)
            relay = lax.ppermute(relay, "pair", perm)
        arrived_own.append(own)
        arrived_relay.append(relay)
    incoming = jnp.stack(arrived_own + arrived_relay)
    step = (pos - groups % half) % half
    slots = jnp.where(groups // half == pair_here // half, step, half + step)
    return incoming, slots


def body(strain, pair_list, tile_live):
    window_count, local_rows, sample_count = strain.shape
    slot_count = tile_live.shape[0]
    n_pair = lax.axis_size("pair")
    n_win = lax.axis_size("win")
    pair_here = lax.axis_index("pair")
    win_here = lax.axis_index("win")
    b_dev = local_rows // C

    table = dft_table(sample_count, F)
    block_list = []
    for k in range(b_dev):
        rows = strain[:, k * C : (k + 1) * C].reshape(window_count * C, sample_count)
        if block_list:
            rows, _ = lax.optimization_barrier((rows, block_list[-1]))
        block_list.append(whiten_rows(rows, table, F).reshape(window_count, C, 2 * F))
    whitened = jnp.stack(block_list, axis=1)

    lists = pair_list.reshape(n_pair, 2 * slot_count)
    wanted = lax.dynamic_slice_in_dim(pair_list, pair_here * slot_count, slot_count, 0)
    groups = wanted.reshape(2 * slot_count) // b_dev
    if n_pair == 8:
        incoming, slots = exchange_by_halves(whitened, block_list, lists, groups, pair_here, b_dev)
    else:
        outgoing = pick_blocks(whitened, block_choice(lists, pair_here, b_dev))
        incoming = lax.all_to_all(outgoing, "pair", 0, 0, tiled=True)
        slots = groups
    slots = jnp.clip(slots, 0, n_pair - 1)

    sub = 4
    own_rows = C // n_win
    n_y = n_win // 2
    bins = lax.iota(jnp.int32, F) + 1
    fine_lag = lax.iota(jnp.int32, sub) * DECIM
    coarse_lag = (lax.iota(jnp.int32, LAGS // sub) * sub - LAGS // 2) * DECIM
    cf, sf = cos_sin(fine_lag[:, None] * bins[None, :], sample_count)
    cc, sc = cos_sin(coarse_lag[:, None] * bins[None, :], sample_count)
    corr = tile_correlation(cc, sc, cf, sf, incoming, slots, sub, n_y, own_rows)

    core = win_here % 2
    y_here = win_here // 2
    send = jnp.take(corr, 1 - core, axis=0, mode="clip")
    keep = jnp.take(corr, core, axis=0, mode="clip").astype(jnp.float32)
    got = lax.ppermute(send, "win", [(w, w ^ 1) for w in range(n_win)])
    half = (keep + got.astype(jnp.float32)).reshape(LAGS, n_y, own_rows, slot_count * C)
    half = jnp.transpose(half, (1, 0, 2, 3))
    total = jnp.take(half, y_here, axis=0, mode="clip")
    for shift in range(1, n_y):
        dest = (y_here + shift) % n_y
        piece = jnp.take(half, dest, axis=0, mode="clip").astype(jnp.bfloat16)
        perm = [(w, ((w // 2 + shift) % n_y) * 2 + w % 2) for w in range(n_win)]
        total = total + lax.ppermute(piece, "win", perm).astype(jnp.float32)
    total = jnp.transpose(total.reshape(LAGS, own_rows, slot_count, C), (1, 2, 0, 3))

    live_local = tile_live.astype(jnp.float32)
    return total * live_local[None, :, None, None] / math.sqrt(F * window_count * n_win)


def solution(mesh):
    in_specs = (P("win", "pair", None), P(), P("pair"))
    out_specs = P("win", "pair", None, None)
    return jax.shard_map(body, mesh=mesh, in_specs=in_specs, out_specs=out_specs, check_vma=False)
```

```python
import functools
import math

import jax
import jax.numpy as jnp
from jax import lax
from jax.experimental import pallas as pl
from jax.experimental.pallas import tpu as pltpu
from jax.sharding import PartitionSpec as P

C = 128
F = 384
LAGS = 16
DECIM = 32
SPLIT = 128


def cos_sin(product, sample_count):
    angle = 2.0 * math.pi / sample_count * (product % sample_count).astype(jnp.float32)
    return jnp.cos(angle), jnp.sin(angle)


def dft_table(sample_count, bin_count):
    bin_index = lax.iota(jnp.int32, bin_count) + 1
    coarse = lax.iota(jnp.int32, sample_count // SPLIT) * SPLIT
    fine = lax.iota(jnp.int32, SPLIT)
    ca, sa = cos_sin(coarse[:, None] * bin_index[None, :], sample_count)
    cb, sb = cos_sin(fine[:, None] * bin_index[None, :], sample_count)
    cos_t = ca[:, None, :] * cb[None, :, :] - sa[:, None, :] * sb[None, :, :]
    sin_t = sa[:, None, :] * cb[None, :, :] + ca[:, None, :] * sb[None, :, :]
    table = jnp.concatenate([cos_t, -sin_t], axis=2).astype(jnp.bfloat16)
    return table.reshape(sample_count, 2 * bin_count)


def whiten_rows(strain_rows, table, bin_count):
    spectrum = jnp.dot(strain_rows, table, preferred_element_type=jnp.float32)
    real_part = spectrum[:, :bin_count]
    imag_part = spectrum[:, bin_count:]
    amplitude = jnp.sqrt(real_part * real_part + imag_part * imag_part)
    level = 0.2 * jnp.mean(amplitude, axis=1, keepdims=True) + 1e-06
    divisor = jnp.maximum(amplitude, level)
    return jnp.concatenate([real_part / divisor, imag_part / divisor], axis=1).astype(jnp.bfloat16)


def correlation_kernel(sub, n_y, own_rows, index_ref, cc_ref, sc_ref, cf_ref, sf_ref, left_ref, right_ref, send_ref, keep_ref):
    window_count = left_ref.shape[1]
    partner = 1 - lax.axis_index("win") % 2
    orders = [[(y * 2 + c) * own_rows for c in (1 - first, first) for y in range(n_y)] for first in (1, 0)]
    acc = None
    for w in range(window_count):
        left = left_ref[0, w].astype(jnp.float32)
        by_order = [jnp.concatenate([left[r : r + own_rows] for r in order], axis=0) for order in orders]
        left = jnp.where(partner == 0, by_order[0], by_order[1])
        lre = left[:, :F]
        lim = left[:, F:]
        rre = right_ref[0, w, :, :F].astype(jnp.float32)
        rim = right_ref[0, w, :, F:].astype(jnp.float32)
        turned = []
        for l1 in range(sub):
            if l1 == 0:
                turned.append(right_ref[0, w])
                continue
            c = cf_ref[l1 : l1 + 1, :]
            s = sf_ref[l1 : l1 + 1, :]
            turned.append(jnp.concatenate([rre * c + rim * s, rim * c - rre * s], axis=1).astype(jnp.bfloat16))
        right_all = jnp.concatenate(turned, axis=0)
        lefts = []
        for l2 in range(LAGS // sub):
            if l2 * sub == LAGS // 2:
                lefts.append(left.astype(jnp.bfloat16))
            else:
                c = cc_ref[l2 : l2 + 1, :]
                s = sc_ref[l2 : l2 + 1, :]
                lefts.append(jnp.concatenate([lre * c - lim * s, lre * s + lim * c], axis=1).astype(jnp.bfloat16))
        res = lax.dot_general(
            jnp.concatenate(lefts, axis=0), right_all, (((1,), (1,)), ((), ())), preferred_element_type=jnp.float32
        )
        acc = res if acc is None else acc + res
    half_rows = C // 2
    for l2 in range(LAGS // sub):
        for l1 in range(sub):
            for part in range(2):
                rows = l2 * C + part * half_rows
                out_ref = (send_ref, keep_ref)[part]
                out_ref[l2 * sub + l1] = acc[rows : rows + half_rows, l1 * C : (l1 + 1) * C].astype(out_ref.dtype)


def tile_correlation(cc, sc, cf, sf, incoming, slots, sub, n_y, own_rows):
    window_count = incoming.shape[1]
    slot_count = slots.shape[0] // 2
    table_spec = pl.BlockSpec(cc.shape, lambda t, idx: (0, 0))
    left_spec = pl.BlockSpec((1, window_count, C, 2 * F), lambda t, idx: (idx[2 * t], 0, 0, 0))
    right_spec = pl.BlockSpec((1, window_count, C, 2 * F), lambda t, idx: (idx[2 * t + 1], 0, 0, 0))
    flops = 2 * slot_count * window_count * C * 2 * F * LAGS * C
    grid_spec = pltpu.PrefetchScalarGridSpec(
        num_scalar_prefetch=1,
        grid=(slot_count,),
        in_specs=[table_spec] * 4 + [left_spec, right_spec],
        out_specs=[pl.BlockSpec((LAGS, C // 2, C), lambda t, idx: (0, 0, t))] * 2,
    )
    return pl.pallas_call(
        functools.partial(correlation_kernel, sub, n_y, own_rows),
        grid_spec=grid_spec,
        out_shape=[jax.ShapeDtypeStruct((LAGS, C // 2, slot_count * C), jnp.bfloat16)] * 2,
        cost_estimate=pl.CostEstimate(
            flops=flops, transcendentals=0, bytes_accessed=slot_count * (4 * window_count * C * F * 2 + 2 * C * LAGS * C)
        ),
    )(slots, cc, sc, cf, sf, incoming, incoming)


def block_choice(lists, group, b_dev):
    return jnp.sum(jnp.where((lists // b_dev) == group, lists % b_dev, 0), axis=1)


def pick_blocks(blocks, choice):
    pick = choice[:, None, None, None]
    out = jnp.broadcast_to(blocks[:, 0][None], choice.shape + blocks[:, 0].shape)
    for k in range(1, blocks.shape[1]):
        out = jnp.where(pick == k, blocks[:, k][None], out)
    return out


def exchange_by_halves(whitened, block_list, lists, groups, pair_here, b_dev):
    n_pair = lists.shape[0]
    half = n_pair // 2
    base = (pair_here // half) * half
    pos = pair_here % half
    across = [(p, p ^ half) for p in range(n_pair)]
    mirror_blocks = jnp.stack([lax.ppermute(block, "pair", across) for block in block_list], axis=1)
    own_choice = block_choice(lists, pair_here, b_dev)
    mirror_choice = block_choice(lists, pair_here ^ half, b_dev)
    arrived_own = []
    arrived_relay = []
    for d in range(half):
        dest = base + (pos + d) % half
        own = pick_blocks(whitened, jnp.take(own_choice, dest[None], mode="clip"))[0]
        relay = pick_blocks(mirror_blocks, jnp.take(mirror_choice, dest[None], mode="clip"))[0]
        if d:
            perm = [(p, (p // half) * half + (p % half + d) % half) for p in range(n_pair)]
            own = lax.ppermute(own, "pair", perm)
            relay = lax.ppermute(relay, "pair", perm)
        arrived_own.append(own)
        arrived_relay.append(relay)
    incoming = jnp.stack(arrived_own + arrived_relay)
    step = (pos - groups % half) % half
    slots = jnp.where(groups // half == pair_here // half, step, half + step)
    return incoming, slots


def body(strain, pair_list, tile_live):
    window_count, local_rows, sample_count = strain.shape
    slot_count = tile_live.shape[0]
    n_pair = lax.axis_size("pair")
    n_win = lax.axis_size("win")
    pair_here = lax.axis_index("pair")
    win_here = lax.axis_index("win")
    b_dev = local_rows // C

    table = dft_table(sample_count, F)
    block_list = [
        whiten_rows(strain[:, k * C : (k + 1) * C].reshape(window_count * C, sample_count), table, F).reshape(
            window_count, C, 2 * F
        )
        for k in range(b_dev)
    ]
    whitened = jnp.stack(block_list, axis=1)

    lists = pair_list.reshape(n_pair, 2 * slot_count)
    wanted = lax.dynamic_slice_in_dim(pair_list, pair_here * slot_count, slot_count, 0)
    groups = wanted.reshape(2 * slot_count) // b_dev
    if n_pair == 8:
        incoming, slots = exchange_by_halves(whitened, block_list, lists, groups, pair_here, b_dev)
    else:
        outgoing = pick_blocks(whitened, block_choice(lists, pair_here, b_dev))
        incoming = lax.all_to_all(outgoing, "pair", 0, 0, tiled=True)
        slots = groups
    slots = jnp.clip(slots, 0, n_pair - 1)

    sub = 4
    own_rows = C // n_win
    n_y = n_win // 2
    bins = lax.iota(jnp.int32, F) + 1
    fine_lag = lax.iota(jnp.int32, sub) * DECIM
    coarse_lag = (lax.iota(jnp.int32, LAGS // sub) * sub - LAGS // 2) * DECIM
    cf, sf = cos_sin(fine_lag[:, None] * bins[None, :], sample_count)
    cc, sc = cos_sin(coarse_lag[:, None] * bins[None, :], sample_count)
    corr = tile_correlation(cc, sc, cf, sf, incoming, slots, sub, n_y, own_rows)

    core = win_here % 2
    y_here = win_here // 2
    send, keep = corr
    keep = keep.astype(jnp.float32)
    got = lax.ppermute(send, "win", [(w, w ^ 1) for w in range(n_win)])
    half = (keep + got.astype(jnp.float32)).reshape(LAGS, n_y, own_rows, slot_count * C)
    half = jnp.transpose(half, (1, 0, 2, 3))
    total = jnp.take(half, y_here, axis=0, mode="clip")
    for shift in range(1, n_y):
        dest = (y_here + shift) % n_y
        piece = jnp.take(half, dest, axis=0, mode="clip").astype(jnp.bfloat16)
        perm = [(w, ((w // 2 + shift) % n_y) * 2 + w % 2) for w in range(n_win)]
        total = total + lax.ppermute(piece, "win", perm).astype(jnp.float32)
    total = jnp.transpose(total.reshape(LAGS, own_rows, slot_count, C), (1, 2, 0, 3))

    live_local = tile_live.astype(jnp.float32)
    return total * live_local[None, :, None, None] / math.sqrt(F * window_count * n_win)


def solution(mesh):
    in_specs = (P("win", "pair", None), P(), P("pair"))
    out_specs = P("win", "pair", None, None)
    return jax.shard_map(body, mesh=mesh, in_specs=in_specs, out_specs=out_specs, check_vma=False)
```

```python
import functools
import math

import jax
import jax.numpy as jnp
from jax import lax
from jax.experimental import pallas as pl
from jax.experimental.pallas import tpu as pltpu
from jax.sharding import PartitionSpec as P

C = 128
F = 384
LAGS = 16
DECIM = 32
SPLIT = 128


def cos_sin(product, sample_count):
    angle = 2.0 * math.pi / sample_count * (product % sample_count).astype(jnp.float32)
    return jnp.cos(angle), jnp.sin(angle)


def dft_table(sample_count, bin_count):
    bin_index = lax.iota(jnp.int32, bin_count) + 1
    coarse = lax.iota(jnp.int32, sample_count // SPLIT) * SPLIT
    fine = lax.iota(jnp.int32, SPLIT)
    ca, sa = cos_sin(coarse[:, None] * bin_index[None, :], sample_count)
    cb, sb = cos_sin(fine[:, None] * bin_index[None, :], sample_count)
    cos_t = ca[:, None, :] * cb[None, :, :] - sa[:, None, :] * sb[None, :, :]
    sin_t = sa[:, None, :] * cb[None, :, :] + ca[:, None, :] * sb[None, :, :]
    table = jnp.concatenate([cos_t, -sin_t], axis=2).astype(jnp.bfloat16)
    return table.reshape(sample_count, 2 * bin_count)


def whiten_rows(strain_rows, table, bin_count):
    spectrum = jnp.dot(strain_rows, table, preferred_element_type=jnp.float32)
    real_part = spectrum[:, :bin_count]
    imag_part = spectrum[:, bin_count:]
    amplitude = jnp.sqrt(real_part * real_part + imag_part * imag_part)
    level = 0.2 * jnp.mean(amplitude, axis=1, keepdims=True) + 1e-06
    divisor = jnp.maximum(amplitude, level)
    return jnp.concatenate([real_part / divisor, imag_part / divisor], axis=1).astype(jnp.bfloat16)


def correlation_kernel(sub, n_y, own_rows, index_ref, cc_ref, sc_ref, cf_ref, sf_ref, left_ref, right_ref, send_ref, keep_ref):
    window_count = left_ref.shape[1]
    partner = 1 - lax.axis_index("win") % 2
    orders = [[(y * 2 + c) * own_rows for c in (1 - first, first) for y in range(n_y)] for first in (1, 0)]
    acc = None
    for w in range(window_count):
        left = left_ref[0, w].astype(jnp.float32)
        by_order = [jnp.concatenate([left[r : r + own_rows] for r in order], axis=0) for order in orders]
        left = jnp.where(partner == 0, by_order[0], by_order[1])
        lre = left[:, :F]
        lim = left[:, F:]
        rre = right_ref[0, w, :, :F].astype(jnp.float32)
        rim = right_ref[0, w, :, F:].astype(jnp.float32)
        turned = []
        for l1 in range(sub):
            if l1 == 0:
                turned.append(right_ref[0, w])
                continue
            c = cf_ref[l1 : l1 + 1, :]
            s = sf_ref[l1 : l1 + 1, :]
            turned.append(jnp.concatenate([rre * c + rim * s, rim * c - rre * s], axis=1).astype(jnp.bfloat16))
        right_all = jnp.concatenate(turned, axis=0)
        lefts = []
        for l2 in range(LAGS // sub):
            if l2 * sub == LAGS // 2:
                lefts.append(left.astype(jnp.bfloat16))
            else:
                c = cc_ref[l2 : l2 + 1, :]
                s = sc_ref[l2 : l2 + 1, :]
                lefts.append(jnp.concatenate([lre * c - lim * s, lre * s + lim * c], axis=1).astype(jnp.bfloat16))
        res = lax.dot_general(
            jnp.concatenate(lefts, axis=0), right_all, (((1,), (1,)), ((), ())), preferred_element_type=jnp.float32
        )
        acc = res if acc is None else acc + res
    half_rows = C // 2
    for l2 in range(LAGS // sub):
        for l1 in range(sub):
            for part in range(2):
                rows = l2 * C + part * half_rows
                out_ref = (send_ref, keep_ref)[part]
                out_ref[l2 * sub + l1] = acc[rows : rows + half_rows, l1 * C : (l1 + 1) * C].astype(out_ref.dtype)


def tile_correlation(cc, sc, cf, sf, incoming, slots, sub, n_y, own_rows):
    window_count = incoming.shape[1]
    slot_count = slots.shape[0] // 2
    table_spec = pl.BlockSpec(cc.shape, lambda t, idx: (0, 0))
    left_spec = pl.BlockSpec((1, window_count, C, 2 * F), lambda t, idx: (idx[2 * t], 0, 0, 0))
    right_spec = pl.BlockSpec((1, window_count, C, 2 * F), lambda t, idx: (idx[2 * t + 1], 0, 0, 0))
    flops = 2 * slot_count * window_count * C * 2 * F * LAGS * C
    grid_spec = pltpu.PrefetchScalarGridSpec(
        num_scalar_prefetch=1,
        grid=(slot_count,),
        in_specs=[table_spec] * 4 + [left_spec, right_spec],
        out_specs=[pl.BlockSpec((LAGS, C // 2, C), lambda t, idx: (0, 0, t))] * 2,
    )
    return pl.pallas_call(
        functools.partial(correlation_kernel, sub, n_y, own_rows),
        grid_spec=grid_spec,
        out_shape=[jax.ShapeDtypeStruct((LAGS, C // 2, slot_count * C), jnp.bfloat16)] * 2,
        cost_estimate=pl.CostEstimate(
            flops=flops, transcendentals=0, bytes_accessed=slot_count * (4 * window_count * C * F * 2 + 2 * C * LAGS * C)
        ),
    )(slots, cc, sc, cf, sf, incoming, incoming)


def block_choice(lists, group, b_dev):
    return jnp.sum(jnp.where((lists // b_dev) == group, lists % b_dev, 0), axis=1)


def pick_blocks(blocks, choice):
    pick = choice[:, None, None, None]
    out = jnp.broadcast_to(blocks[:, 0][None], choice.shape + blocks[:, 0].shape)
    for k in range(1, blocks.shape[1]):
        out = jnp.where(pick == k, blocks[:, k][None], out)
    return out


def exchange_by_halves(whitened, block_list, lists, groups, pair_here, b_dev):
    n_pair = lists.shape[0]
    half = n_pair // 2
    base = (pair_here // half) * half
    pos = pair_here % half
    across = [(p, p ^ half) for p in range(n_pair)]
    mirror_blocks = jnp.stack([lax.ppermute(block, "pair", across) for block in block_list], axis=1)
    own_choice = block_choice(lists, pair_here, b_dev)
    mirror_choice = block_choice(lists, pair_here ^ half, b_dev)
    arrived_own = []
    arrived_relay = []
    for d in range(half):
        dest = base + (pos + d) % half
        own = pick_blocks(whitened, jnp.take(own_choice, dest[None], mode="clip"))[0]
        relay = pick_blocks(mirror_blocks, jnp.take(mirror_choice, dest[None], mode="clip"))[0]
        if d:
            perm = [(p, (p // half) * half + (p % half + d) % half) for p in range(n_pair)]
            own = lax.ppermute(own, "pair", perm)
            relay = lax.ppermute(relay, "pair", perm)
        arrived_own.append(own)
        arrived_relay.append(relay)
    incoming = jnp.stack(arrived_own + arrived_relay)
    step = (pos - groups % half) % half
    slots = jnp.where(groups // half == pair_here // half, step, half + step)
    return incoming, slots


def body(strain, pair_list, tile_live):
    window_count, local_rows, sample_count = strain.shape
    slot_count = tile_live.shape[0]
    n_pair = lax.axis_size("pair")
    n_win = lax.axis_size("win")
    pair_here = lax.axis_index("pair")
    win_here = lax.axis_index("win")
    b_dev = local_rows // C

    table = dft_table(sample_count, F)
    block_list = [
        whiten_rows(strain[:, k * C : (k + 1) * C].reshape(window_count * C, sample_count), table, F).reshape(
            window_count, C, 2 * F
        )
        for k in range(b_dev)
    ]
    whitened = jnp.stack(block_list, axis=1)

    lists = pair_list.reshape(n_pair, 2 * slot_count)
    wanted = lax.dynamic_slice_in_dim(pair_list, pair_here * slot_count, slot_count, 0)
    groups = wanted.reshape(2 * slot_count) // b_dev
    if n_pair == 8:
        incoming, slots = exchange_by_halves(whitened, block_list, lists, groups, pair_here, b_dev)
    else:
        outgoing = pick_blocks(whitened, block_choice(lists, pair_here, b_dev))
        incoming = lax.all_to_all(outgoing, "pair", 0, 0, tiled=True)
        slots = groups
    slots = jnp.clip(slots, 0, n_pair - 1)

    sub = 4
    own_rows = C // n_win
    n_y = n_win // 2
    bins = lax.iota(jnp.int32, F) + 1
    fine_lag = lax.iota(jnp.int32, sub) * DECIM
    coarse_lag = (lax.iota(jnp.int32, LAGS // sub) * sub - LAGS // 2) * DECIM
    cf, sf = cos_sin(fine_lag[:, None] * bins[None, :], sample_count)
    cc, sc = cos_sin(coarse_lag[:, None] * bins[None, :], sample_count)
    corr = tile_correlation(cc, sc, cf, sf, incoming, slots, sub, n_y, own_rows)

    core = win_here % 2
    y_here = win_here // 2
    send, keep = corr
    keep = keep.astype(jnp.float32)
    got = lax.ppermute(send, "win", [(w, w ^ 1) for w in range(n_win)])
    keep = keep.reshape(LAGS, n_y, own_rows, slot_count * C)
    got = got.reshape(LAGS, n_y, own_rows, slot_count * C)

    def chip_sum(y):
        pick = lambda a: jnp.take(a, y, axis=1, mode="clip")
        return pick(keep) + pick(got).astype(jnp.float32)

    pieces = []
    for shift in range(1, n_y):
        dest = (y_here + shift) % n_y
        perm = [(w, ((w // 2 + shift) % n_y) * 2 + w % 2) for w in range(n_win)]
        pieces.append(lax.ppermute(chip_sum(dest).astype(jnp.bfloat16), "win", perm))
    total = chip_sum(y_here)
    for piece in pieces:
        total = total + piece.astype(jnp.float32)
    total = jnp.transpose(total.reshape(LAGS, own_rows, slot_count, C), (1, 2, 0, 3))

    live_local = tile_live.astype(jnp.float32)
    return total * live_local[None, :, None, None] / math.sqrt(F * window_count * n_win)


def solution(mesh):
    in_specs = (P("win", "pair", None), P(), P("pair"))
    out_specs = P("win", "pair", None, None)
    return jax.shard_map(body, mesh=mesh, in_specs=in_specs, out_specs=out_specs, check_vma=False)
```

```python
import functools
import math

import jax
import jax.numpy as jnp
from jax import lax
from jax.experimental import pallas as pl
from jax.experimental.pallas import tpu as pltpu
from jax.sharding import PartitionSpec as P

C = 128
F = 384
LAGS = 16
DECIM = 32
SPLIT = 128


def cos_sin(product, sample_count):
    angle = 2.0 * math.pi / sample_count * (product % sample_count).astype(jnp.float32)
    return jnp.cos(angle), jnp.sin(angle)


def dft_table(sample_count, bin_count):
    bin_index = lax.iota(jnp.int32, bin_count) + 1
    coarse = lax.iota(jnp.int32, sample_count // SPLIT) * SPLIT
    fine = lax.iota(jnp.int32, SPLIT)
    ca, sa = cos_sin(coarse[:, None] * bin_index[None, :], sample_count)
    cb, sb = cos_sin(fine[:, None] * bin_index[None, :], sample_count)
    cos_t = ca[:, None, :] * cb[None, :, :] - sa[:, None, :] * sb[None, :, :]
    sin_t = sa[:, None, :] * cb[None, :, :] + ca[:, None, :] * sb[None, :, :]
    table = jnp.concatenate([cos_t, -sin_t], axis=2).astype(jnp.bfloat16)
    return table.reshape(sample_count, 2 * bin_count)


def whiten_rows(strain_rows, table, bin_count):
    spectrum = jnp.dot(strain_rows, table, preferred_element_type=jnp.float32)
    real_part = spectrum[:, :bin_count]
    imag_part = spectrum[:, bin_count:]
    amplitude = jnp.sqrt(real_part * real_part + imag_part * imag_part)
    level = 0.2 * jnp.mean(amplitude, axis=1, keepdims=True) + 1e-06
    divisor = jnp.maximum(amplitude, level)
    return jnp.concatenate([real_part / divisor, imag_part / divisor], axis=1).astype(jnp.bfloat16)


def correlation_kernel(sub, n_y, own_rows, index_ref, cc_ref, sc_ref, cf_ref, sf_ref, left_ref, right_ref, send_ref, keep_ref):
    window_count = left_ref.shape[1]
    partner = 1 - lax.axis_index("win") % 2
    orders = [[(y * 2 + c) * own_rows for c in (1 - first, first) for y in range(n_y)] for first in (1, 0)]
    acc = None
    for w in range(window_count):
        left = left_ref[0, w].astype(jnp.float32)
        by_order = [jnp.concatenate([left[r : r + own_rows] for r in order], axis=0) for order in orders]
        left = jnp.where(partner == 0, by_order[0], by_order[1])
        lre = left[:, :F]
        lim = left[:, F:]
        rre = right_ref[0, w, :, :F].astype(jnp.float32)
        rim = right_ref[0, w, :, F:].astype(jnp.float32)
        turned = []
        for l1 in range(sub):
            if l1 == 0:
                turned.append(right_ref[0, w])
                continue
            c = cf_ref[l1 : l1 + 1, :]
            s = sf_ref[l1 : l1 + 1, :]
            turned.append(jnp.concatenate([rre * c + rim * s, rim * c - rre * s], axis=1).astype(jnp.bfloat16))
        right_all = jnp.concatenate(turned, axis=0)
        lefts = []
        for l2 in range(LAGS // sub):
            if l2 * sub == LAGS // 2:
                lefts.append(left.astype(jnp.bfloat16))
            else:
                c = cc_ref[l2 : l2 + 1, :]
                s = sc_ref[l2 : l2 + 1, :]
                lefts.append(jnp.concatenate([lre * c - lim * s, lre * s + lim * c], axis=1).astype(jnp.bfloat16))
        res = lax.dot_general(
            jnp.concatenate(lefts, axis=0), right_all, (((1,), (1,)), ((), ())), preferred_element_type=jnp.float32
        )
        acc = res if acc is None else acc + res
    half_rows = C // 2
    for l2 in range(LAGS // sub):
        for l1 in range(sub):
            for part in range(2):
                rows = l2 * C + part * half_rows
                out_ref = (send_ref, keep_ref)[part]
                out_ref[l2 * sub + l1, 0] = acc[rows : rows + half_rows, l1 * C : (l1 + 1) * C].astype(out_ref.dtype)


def tile_correlation(cc, sc, cf, sf, incoming, slots, sub, n_y, own_rows):
    window_count = incoming.shape[1]
    slot_count = slots.shape[0] // 2
    table_spec = pl.BlockSpec(cc.shape, lambda t, idx: (0, 0))
    left_spec = pl.BlockSpec((1, window_count, C, 2 * F), lambda t, idx: (idx[2 * t], 0, 0, 0))
    right_spec = pl.BlockSpec((1, window_count, C, 2 * F), lambda t, idx: (idx[2 * t + 1], 0, 0, 0))
    flops = 2 * slot_count * window_count * C * 2 * F * LAGS * C
    grid_spec = pltpu.PrefetchScalarGridSpec(
        num_scalar_prefetch=1,
        grid=(slot_count,),
        in_specs=[table_spec] * 4 + [left_spec, right_spec],
        out_specs=[pl.BlockSpec((LAGS, 1, C // 2, C), lambda t, idx: (0, t, 0, 0))] * 2,
    )
    return pl.pallas_call(
        functools.partial(correlation_kernel, sub, n_y, own_rows),
        grid_spec=grid_spec,
        out_shape=[jax.ShapeDtypeStruct((LAGS, slot_count, C // 2, C), jnp.bfloat16)] * 2,
        cost_estimate=pl.CostEstimate(
            flops=flops, transcendentals=0, bytes_accessed=slot_count * (4 * window_count * C * F * 2 + 2 * C * LAGS * C)
        ),
    )(slots, cc, sc, cf, sf, incoming, incoming)


def block_choice(lists, group, b_dev):
    return jnp.sum(jnp.where((lists // b_dev) == group, lists % b_dev, 0), axis=1)


def pick_blocks(blocks, choice):
    pick = choice[:, None, None, None]
    out = jnp.broadcast_to(blocks[:, 0][None], choice.shape + blocks[:, 0].shape)
    for k in range(1, blocks.shape[1]):
        out = jnp.where(pick == k, blocks[:, k][None], out)
    return out


def exchange_by_halves(whitened, block_list, lists, groups, pair_here, b_dev):
    n_pair = lists.shape[0]
    half = n_pair // 2
    base = (pair_here // half) * half
    pos = pair_here % half
    across = [(p, p ^ half) for p in range(n_pair)]
    mirror_blocks = jnp.stack([lax.ppermute(block, "pair", across) for block in block_list], axis=1)
    own_choice = block_choice(lists, pair_here, b_dev)
    mirror_choice = block_choice(lists, pair_here ^ half, b_dev)
    arrived_own = []
    arrived_relay = []
    for d in range(half):
        dest = base + (pos + d) % half
        own = pick_blocks(whitened, jnp.take(own_choice, dest[None], mode="clip"))[0]
        relay = pick_blocks(mirror_blocks, jnp.take(mirror_choice, dest[None], mode="clip"))[0]
        if d:
            perm = [(p, (p // half) * half + (p % half + d) % half) for p in range(n_pair)]
            own = lax.ppermute(own, "pair", perm)
            relay = lax.ppermute(relay, "pair", perm)
        arrived_own.append(own)
        arrived_relay.append(relay)
    incoming = jnp.stack(arrived_own + arrived_relay)
    step = (pos - groups % half) % half
    slots = jnp.where(groups // half == pair_here // half, step, half + step)
    return incoming, slots


def body(strain, pair_list, tile_live):
    window_count, local_rows, sample_count = strain.shape
    slot_count = tile_live.shape[0]
    n_pair = lax.axis_size("pair")
    n_win = lax.axis_size("win")
    pair_here = lax.axis_index("pair")
    win_here = lax.axis_index("win")
    b_dev = local_rows // C

    table = dft_table(sample_count, F)
    block_list = [
        whiten_rows(strain[:, k * C : (k + 1) * C].reshape(window_count * C, sample_count), table, F).reshape(
            window_count, C, 2 * F
        )
        for k in range(b_dev)
    ]
    whitened = jnp.stack(block_list, axis=1)

    lists = pair_list.reshape(n_pair, 2 * slot_count)
    wanted = lax.dynamic_slice_in_dim(pair_list, pair_here * slot_count, slot_count, 0)
    groups = wanted.reshape(2 * slot_count) // b_dev
    if n_pair == 8:
        incoming, slots = exchange_by_halves(whitened, block_list, lists, groups, pair_here, b_dev)
    else:
        outgoing = pick_blocks(whitened, block_choice(lists, pair_here, b_dev))
        incoming = lax.all_to_all(outgoing, "pair", 0, 0, tiled=True)
        slots = groups
    slots = jnp.clip(slots, 0, n_pair - 1)

    sub = 4
    own_rows = C // n_win
    n_y = n_win // 2
    bins = lax.iota(jnp.int32, F) + 1
    fine_lag = lax.iota(jnp.int32, sub) * DECIM
    coarse_lag = (lax.iota(jnp.int32, LAGS // sub) * sub - LAGS // 2) * DECIM
    cf, sf = cos_sin(fine_lag[:, None] * bins[None, :], sample_count)
    cc, sc = cos_sin(coarse_lag[:, None] * bins[None, :], sample_count)
    corr = tile_correlation(cc, sc, cf, sf, incoming, slots, sub, n_y, own_rows)

    core = win_here % 2
    y_here = win_here // 2
    send, keep = corr
    keep = keep.astype(jnp.float32)
    got = lax.ppermute(send, "win", [(w, w ^ 1) for w in range(n_win)])
    keep = keep.reshape(LAGS, slot_count, n_y, own_rows, C)
    got = got.reshape(LAGS, slot_count, n_y, own_rows, C)

    def chip_sum(y):
        pick = lambda a: jnp.take(a, y, axis=2, mode="clip")
        return pick(keep) + pick(got).astype(jnp.float32)

    pieces = []
    for shift in range(1, n_y):
        dest = (y_here + shift) % n_y
        perm = [(w, ((w // 2 + shift) % n_y) * 2 + w % 2) for w in range(n_win)]
        pieces.append(lax.ppermute(chip_sum(dest).astype(jnp.bfloat16), "win", perm))
    total = chip_sum(y_here)
    for piece in pieces:
        total = total + piece.astype(jnp.float32)
    total = jnp.transpose(total, (2, 1, 0, 3))

    live_local = tile_live.astype(jnp.float32)
    return total * live_local[None, :, None, None] / math.sqrt(F * window_count * n_win)


def solution(mesh):
    in_specs = (P("win", "pair", None), P(), P("pair"))
    out_specs = P("win", "pair", None, None)
    return jax.shard_map(body, mesh=mesh, in_specs=in_specs, out_specs=out_specs, check_vma=False)
```

```python
import functools
import math

import jax
import jax.numpy as jnp
from jax import lax
from jax.experimental import pallas as pl
from jax.experimental.pallas import tpu as pltpu
from jax.sharding import PartitionSpec as P

C = 128
F = 384
LAGS = 16
DECIM = 32
SPLIT = 128


def cos_sin(product, sample_count):
    angle = 2.0 * math.pi / sample_count * (product % sample_count).astype(jnp.float32)
    return jnp.cos(angle), jnp.sin(angle)


def dft_table(sample_count, bin_count):
    bin_index = lax.iota(jnp.int32, bin_count) + 1
    coarse = lax.iota(jnp.int32, sample_count // SPLIT) * SPLIT
    fine = lax.iota(jnp.int32, SPLIT)
    ca, sa = cos_sin(coarse[:, None] * bin_index[None, :], sample_count)
    cb, sb = cos_sin(fine[:, None] * bin_index[None, :], sample_count)
    cos_t = ca[:, None, :] * cb[None, :, :] - sa[:, None, :] * sb[None, :, :]
    sin_t = sa[:, None, :] * cb[None, :, :] + ca[:, None, :] * sb[None, :, :]
    table = jnp.concatenate([cos_t, -sin_t], axis=2).astype(jnp.bfloat16)
    return table.reshape(sample_count, 2 * bin_count)


def whiten_rows(strain_rows, table, bin_count):
    spectrum = jnp.dot(strain_rows, table, preferred_element_type=jnp.float32)
    real_part = spectrum[:, :bin_count]
    imag_part = spectrum[:, bin_count:]
    amplitude = jnp.sqrt(real_part * real_part + imag_part * imag_part)
    level = 0.2 * jnp.mean(amplitude, axis=1, keepdims=True) + 1e-06
    divisor = jnp.maximum(amplitude, level)
    return jnp.concatenate([real_part / divisor, imag_part / divisor], axis=1).astype(jnp.bfloat16)


def correlation_kernel(sub, n_y, own_rows, index_ref, cc_ref, sc_ref, cf_ref, sf_ref, left_ref, right_ref, far_ref, near_ref, keep_ref):
    window_count = left_ref.shape[1]
    win = lax.axis_index("win")
    variants = [(c, y) for c in range(2) for y in range(n_y)]
    acc = None
    for w in range(window_count):
        left = left_ref[0, w].astype(jnp.float32)
        picked = None
        for c, y in variants:
            chips = [(y + shift) % n_y for shift in range(1, n_y)] + [y]
            order = [(yy * 2 + cc) * own_rows for cc in (1 - c, c) for yy in chips]
            this = jnp.concatenate([left[r : r + own_rows] for r in order], axis=0)
            picked = this if picked is None else jnp.where(win == y * 2 + c, this, picked)
        left = picked
        lre = left[:, :F]
        lim = left[:, F:]
        rre = right_ref[0, w, :, :F].astype(jnp.float32)
        rim = right_ref[0, w, :, F:].astype(jnp.float32)
        turned = []
        for l1 in range(sub):
            if l1 == 0:
                turned.append(right_ref[0, w])
                continue
            c = cf_ref[l1 : l1 + 1, :]
            s = sf_ref[l1 : l1 + 1, :]
            turned.append(jnp.concatenate([rre * c + rim * s, rim * c - rre * s], axis=1).astype(jnp.bfloat16))
        right_all = jnp.concatenate(turned, axis=0)
        lefts = []
        for l2 in range(LAGS // sub):
            if l2 * sub == LAGS // 2:
                lefts.append(left.astype(jnp.bfloat16))
            else:
                c = cc_ref[l2 : l2 + 1, :]
                s = sc_ref[l2 : l2 + 1, :]
                lefts.append(jnp.concatenate([lre * c - lim * s, lre * s + lim * c], axis=1).astype(jnp.bfloat16))
        res = lax.dot_general(
            jnp.concatenate(lefts, axis=0), right_all, (((1,), (1,)), ((), ())), preferred_element_type=jnp.float32
        )
        acc = res if acc is None else acc + res
    half_rows = C // 2
    for l2 in range(LAGS // sub):
        for l1 in range(sub):
            for part in range(2):
                rows = l2 * C + part * half_rows
                block = acc[rows : rows + half_rows, l1 * C : (l1 + 1) * C].astype(keep_ref.dtype)
                if part:
                    keep_ref[l2 * sub + l1] = block
                else:
                    far_ref[l2 * sub + l1] = block[: half_rows - own_rows]
                    near_ref[l2 * sub + l1] = block[half_rows - own_rows :]


def tile_correlation(cc, sc, cf, sf, incoming, slots, sub, n_y, own_rows):
    window_count = incoming.shape[1]
    slot_count = slots.shape[0] // 2
    table_spec = pl.BlockSpec(cc.shape, lambda t, idx: (0, 0))
    left_spec = pl.BlockSpec((1, window_count, C, 2 * F), lambda t, idx: (idx[2 * t], 0, 0, 0))
    right_spec = pl.BlockSpec((1, window_count, C, 2 * F), lambda t, idx: (idx[2 * t + 1], 0, 0, 0))
    flops = 2 * slot_count * window_count * C * 2 * F * LAGS * C
    grid_spec = pltpu.PrefetchScalarGridSpec(
        num_scalar_prefetch=1,
        grid=(slot_count,),
        in_specs=[table_spec] * 4 + [left_spec, right_spec],
        out_specs=[
            pl.BlockSpec((LAGS, C // 2 - own_rows, C), lambda t, idx: (0, 0, t)),
            pl.BlockSpec((LAGS, own_rows, C), lambda t, idx: (0, 0, t)),
            pl.BlockSpec((LAGS, C // 2, C), lambda t, idx: (0, 0, t)),
        ],
    )
    return pl.pallas_call(
        functools.partial(correlation_kernel, sub, n_y, own_rows),
        grid_spec=grid_spec,
        out_shape=[
            jax.ShapeDtypeStruct((LAGS, C // 2 - own_rows, slot_count * C), jnp.bfloat16),
            jax.ShapeDtypeStruct((LAGS, own_rows, slot_count * C), jnp.bfloat16),
            jax.ShapeDtypeStruct((LAGS, C // 2, slot_count * C), jnp.bfloat16),
        ],
        cost_estimate=pl.CostEstimate(
            flops=flops, transcendentals=0, bytes_accessed=slot_count * (4 * window_count * C * F * 2 + 2 * C * LAGS * C)
        ),
    )(slots, cc, sc, cf, sf, incoming, incoming)


def block_choice(lists, group, b_dev):
    return jnp.sum(jnp.where((lists // b_dev) == group, lists % b_dev, 0), axis=1)


def pick_blocks(blocks, choice):
    pick = choice[:, None, None, None]
    out = jnp.broadcast_to(blocks[:, 0][None], choice.shape + blocks[:, 0].shape)
    for k in range(1, blocks.shape[1]):
        out = jnp.where(pick == k, blocks[:, k][None], out)
    return out


def exchange_by_halves(whitened, block_list, lists, groups, pair_here, b_dev):
    n_pair = lists.shape[0]
    half = n_pair // 2
    base = (pair_here // half) * half
    pos = pair_here % half
    across = [(p, p ^ half) for p in range(n_pair)]
    mirror_blocks = jnp.stack([lax.ppermute(block, "pair", across) for block in block_list], axis=1)
    own_choice = block_choice(lists, pair_here, b_dev)
    mirror_choice = block_choice(lists, pair_here ^ half, b_dev)
    arrived_own = []
    arrived_relay = []
    for d in range(half):
        dest = base + (pos + d) % half
        own = pick_blocks(whitened, jnp.take(own_choice, dest[None], mode="clip"))[0]
        relay = pick_blocks(mirror_blocks, jnp.take(mirror_choice, dest[None], mode="clip"))[0]
        if d:
            perm = [(p, (p // half) * half + (p % half + d) % half) for p in range(n_pair)]
            own = lax.ppermute(own, "pair", perm)
            relay = lax.ppermute(relay, "pair", perm)
        arrived_own.append(own)
        arrived_relay.append(relay)
    incoming = jnp.stack(arrived_own + arrived_relay)
    step = (pos - groups % half) % half
    slots = jnp.where(groups // half == pair_here // half, step, half + step)
    return incoming, slots


def body(strain, pair_list, tile_live):
    window_count, local_rows, sample_count = strain.shape
    slot_count = tile_live.shape[0]
    n_pair = lax.axis_size("pair")
    n_win = lax.axis_size("win")
    pair_here = lax.axis_index("pair")
    win_here = lax.axis_index("win")
    b_dev = local_rows // C

    table = dft_table(sample_count, F)
    block_list = [
        whiten_rows(strain[:, k * C : (k + 1) * C].reshape(window_count * C, sample_count), table, F).reshape(
            window_count, C, 2 * F
        )
        for k in range(b_dev)
    ]
    whitened = jnp.stack(block_list, axis=1)

    lists = pair_list.reshape(n_pair, 2 * slot_count)
    wanted = lax.dynamic_slice_in_dim(pair_list, pair_here * slot_count, slot_count, 0)
    groups = wanted.reshape(2 * slot_count) // b_dev
    if n_pair == 8:
        incoming, slots = exchange_by_halves(whitened, block_list, lists, groups, pair_here, b_dev)
    else:
        outgoing = pick_blocks(whitened, block_choice(lists, pair_here, b_dev))
        incoming = lax.all_to_all(outgoing, "pair", 0, 0, tiled=True)
        slots = groups
    slots = jnp.clip(slots, 0, n_pair - 1)

    sub = 4
    own_rows = C // n_win
    n_y = n_win // 2
    bins = lax.iota(jnp.int32, F) + 1
    fine_lag = lax.iota(jnp.int32, sub) * DECIM
    coarse_lag = (lax.iota(jnp.int32, LAGS // sub) * sub - LAGS // 2) * DECIM
    cf, sf = cos_sin(fine_lag[:, None] * bins[None, :], sample_count)
    cc, sc = cos_sin(coarse_lag[:, None] * bins[None, :], sample_count)
    corr = tile_correlation(cc, sc, cf, sf, incoming, slots, sub, n_y, own_rows)

    core = win_here % 2
    y_here = win_here // 2
    far, near, keep = corr
    core_pairs = [(w, w ^ 1) for w in range(n_win)]
    got_far = lax.ppermute(far, "win", core_pairs)
    pieces = []
    for shift in range(1, n_y):
        rows = slice((shift - 1) * own_rows, shift * own_rows)
        piece = keep[:, rows].astype(jnp.float32) + got_far[:, rows].astype(jnp.float32)
        perm = [(w, ((w // 2 + shift) % n_y) * 2 + w % 2) for w in range(n_win)]
        pieces.append(lax.ppermute(piece.astype(jnp.bfloat16), "win", perm))
    got_near = lax.ppermute(near, "win", core_pairs)
    total = keep[:, (n_y - 1) * own_rows :].astype(jnp.float32) + got_near.astype(jnp.float32)
    for piece in pieces:
        total = total + piece.astype(jnp.float32)
    total = jnp.transpose(total.reshape(LAGS, own_rows, slot_count, C), (1, 2, 0, 3))

    live_local = tile_live.astype(jnp.float32)
    return total * live_local[None, :, None, None] / math.sqrt(F * window_count * n_win)


def solution(mesh):
    in_specs = (P("win", "pair", None), P(), P("pair"))
    out_specs = P("win", "pair", None, None)
    return jax.shard_map(body, mesh=mesh, in_specs=in_specs, out_specs=out_specs, check_vma=False)
```

```python
import functools
import math

import jax
import jax.numpy as jnp
from jax import lax
from jax.experimental import pallas as pl
from jax.experimental.pallas import tpu as pltpu
from jax.sharding import PartitionSpec as P

C = 128
F = 384
LAGS = 16
DECIM = 32
SPLIT = 128


def cos_sin(product, sample_count):
    angle = 2.0 * math.pi / sample_count * (product % sample_count).astype(jnp.float32)
    return jnp.cos(angle), jnp.sin(angle)


def dft_table(sample_count, bin_count):
    bin_index = lax.iota(jnp.int32, bin_count) + 1
    coarse = lax.iota(jnp.int32, sample_count // SPLIT) * SPLIT
    ca, sa = cos_sin(coarse[:, None] * bin_index[None, :], sample_count)
    c1, s1 = cos_sin((lax.iota(jnp.int32, SPLIT // 16) * 16)[:, None] * bin_index[None, :], sample_count)
    c0, s0 = cos_sin(lax.iota(jnp.int32, 16)[:, None] * bin_index[None, :], sample_count)
    cb = (c1[:, None, :] * c0[None, :, :] - s1[:, None, :] * s0[None, :, :]).reshape(SPLIT, bin_count)
    sb = (s1[:, None, :] * c0[None, :, :] + c1[:, None, :] * s0[None, :, :]).reshape(SPLIT, bin_count)
    cos_t = ca[:, None, :] * cb[None, :, :] - sa[:, None, :] * sb[None, :, :]
    sin_t = sa[:, None, :] * cb[None, :, :] + ca[:, None, :] * sb[None, :, :]
    table = jnp.concatenate([cos_t, -sin_t], axis=2).astype(jnp.bfloat16)
    return table.reshape(sample_count, 2 * bin_count)


def whiten_rows(strain_rows, table, bin_count):
    spectrum = jnp.dot(strain_rows, table, preferred_element_type=jnp.float32)
    real_part = spectrum[:, :bin_count]
    imag_part = spectrum[:, bin_count:]
    amplitude = jnp.sqrt(real_part * real_part + imag_part * imag_part)
    level = 0.2 * jnp.mean(amplitude, axis=1, keepdims=True) + 1e-06
    divisor = jnp.maximum(amplitude, level)
    return jnp.concatenate([real_part / divisor, imag_part / divisor], axis=1).astype(jnp.bfloat16)


def correlation_kernel(sub, n_y, own_rows, index_ref, cc_ref, sc_ref, cf_ref, sf_ref, left_ref, right_ref, send_ref, keep_ref):
    window_count = left_ref.shape[1]
    partner = 1 - lax.axis_index("win") % 2
    orders = [[(y * 2 + c) * own_rows for c in (1 - first, first) for y in range(n_y)] for first in (1, 0)]
    acc = None
    for w in range(window_count):
        left = left_ref[0, w].astype(jnp.float32)
        by_order = [jnp.concatenate([left[r : r + own_rows] for r in order], axis=0) for order in orders]
        left = jnp.where(partner == 0, by_order[0], by_order[1])
        lre = left[:, :F]
        lim = left[:, F:]
        rre = right_ref[0, w, :, :F].astype(jnp.float32)
        rim = right_ref[0, w, :, F:].astype(jnp.float32)
        turned = []
        for l1 in range(sub):
            if l1 == 0:
                turned.append(right_ref[0, w])
                continue
            c = cf_ref[l1 : l1 + 1, :]
            s = sf_ref[l1 : l1 + 1, :]
            turned.append(jnp.concatenate([rre * c + rim * s, rim * c - rre * s], axis=1).astype(jnp.bfloat16))
        right_all = jnp.concatenate(turned, axis=0)
        lefts = []
        for l2 in range(LAGS // sub):
            if l2 * sub == LAGS // 2:
                lefts.append(left.astype(jnp.bfloat16))
            else:
                c = cc_ref[l2 : l2 + 1, :]
                s = sc_ref[l2 : l2 + 1, :]
                lefts.append(jnp.concatenate([lre * c - lim * s, lre * s + lim * c], axis=1).astype(jnp.bfloat16))
        res = lax.dot_general(
            jnp.concatenate(lefts, axis=0), right_all, (((1,), (1,)), ((), ())), preferred_element_type=jnp.float32
        )
        acc = res if acc is None else acc + res
    half_rows = C // 2
    for l2 in range(LAGS // sub):
        for l1 in range(sub):
            for part in range(2):
                rows = l2 * C + part * half_rows
                out_ref = (send_ref, keep_ref)[part]
                out_ref[l2 * sub + l1] = acc[rows : rows + half_rows, l1 * C : (l1 + 1) * C].astype(out_ref.dtype)


def tile_correlation(cc, sc, cf, sf, incoming, slots, sub, n_y, own_rows):
    window_count = incoming.shape[1]
    slot_count = slots.shape[0] // 2
    table_spec = pl.BlockSpec(cc.shape, lambda t, idx: (0, 0))
    left_spec = pl.BlockSpec((1, window_count, C, 2 * F), lambda t, idx: (idx[2 * t], 0, 0, 0))
    right_spec = pl.BlockSpec((1, window_count, C, 2 * F), lambda t, idx: (idx[2 * t + 1], 0, 0, 0))
    flops = 2 * slot_count * window_count * C * 2 * F * LAGS * C
    grid_spec = pltpu.PrefetchScalarGridSpec(
        num_scalar_prefetch=1,
        grid=(slot_count,),
        in_specs=[table_spec] * 4 + [left_spec, right_spec],
        out_specs=[pl.BlockSpec((LAGS, C // 2, C), lambda t, idx: (0, 0, t))] * 2,
    )
    return pl.pallas_call(
        functools.partial(correlation_kernel, sub, n_y, own_rows),
        grid_spec=grid_spec,
        out_shape=[jax.ShapeDtypeStruct((LAGS, C // 2, slot_count * C), jnp.bfloat16)] * 2,
        cost_estimate=pl.CostEstimate(
            flops=flops, transcendentals=0, bytes_accessed=slot_count * (4 * window_count * C * F * 2 + 2 * C * LAGS * C)
        ),
    )(slots, cc, sc, cf, sf, incoming, incoming)


def block_choice(lists, group, b_dev):
    return jnp.sum(jnp.where((lists // b_dev) == group, lists % b_dev, 0), axis=1)


def pick_blocks(blocks, choice):
    pick = choice[:, None, None, None]
    out = jnp.broadcast_to(blocks[:, 0][None], choice.shape + blocks[:, 0].shape)
    for k in range(1, blocks.shape[1]):
        out = jnp.where(pick == k, blocks[:, k][None], out)
    return out


def exchange_by_halves(whitened, block_list, lists, groups, pair_here, b_dev):
    n_pair = lists.shape[0]
    half = n_pair // 2
    base = (pair_here // half) * half
    pos = pair_here % half
    across = [(p, p ^ half) for p in range(n_pair)]
    mirror_blocks = jnp.stack([lax.ppermute(block, "pair", across) for block in block_list], axis=1)
    own_choice = block_choice(lists, pair_here, b_dev)
    mirror_choice = block_choice(lists, pair_here ^ half, b_dev)
    arrived_own = []
    arrived_relay = []
    for d in range(half):
        dest = base + (pos + d) % half
        own = pick_blocks(whitened, jnp.take(own_choice, dest[None], mode="clip"))[0]
        relay = pick_blocks(mirror_blocks, jnp.take(mirror_choice, dest[None], mode="clip"))[0]
        if d:
            perm = [(p, (p // half) * half + (p % half + d) % half) for p in range(n_pair)]
            own = lax.ppermute(own, "pair", perm)
            relay = lax.ppermute(relay, "pair", perm)
        arrived_own.append(own)
        arrived_relay.append(relay)
    incoming = jnp.stack(arrived_own + arrived_relay)
    step = (pos - groups % half) % half
    slots = jnp.where(groups // half == pair_here // half, step, half + step)
    return incoming, slots


def body(strain, pair_list, tile_live):
    window_count, local_rows, sample_count = strain.shape
    slot_count = tile_live.shape[0]
    n_pair = lax.axis_size("pair")
    n_win = lax.axis_size("win")
    pair_here = lax.axis_index("pair")
    win_here = lax.axis_index("win")
    b_dev = local_rows // C

    table = dft_table(sample_count, F)
    block_list = [
        whiten_rows(strain[:, k * C : (k + 1) * C].reshape(window_count * C, sample_count), table, F).reshape(
            window_count, C, 2 * F
        )
        for k in range(b_dev)
    ]
    whitened = jnp.stack(block_list, axis=1)

    lists = pair_list.reshape(n_pair, 2 * slot_count)
    wanted = lax.dynamic_slice_in_dim(pair_list, pair_here * slot_count, slot_count, 0)
    groups = wanted.reshape(2 * slot_count) // b_dev
    if n_pair == 8:
        incoming, slots = exchange_by_halves(whitened, block_list, lists, groups, pair_here, b_dev)
    else:
        outgoing = pick_blocks(whitened, block_choice(lists, pair_here, b_dev))
        incoming = lax.all_to_all(outgoing, "pair", 0, 0, tiled=True)
        slots = groups
    slots = jnp.clip(slots, 0, n_pair - 1)

    sub = 4
    own_rows = C // n_win
    n_y = n_win // 2
    bins = lax.iota(jnp.int32, F) + 1
    fine_lag = lax.iota(jnp.int32, sub) * DECIM
    coarse_lag = (lax.iota(jnp.int32, LAGS // sub) * sub - LAGS // 2) * DECIM
    cf, sf = cos_sin(fine_lag[:, None] * bins[None, :], sample_count)
    cc, sc = cos_sin(coarse_lag[:, None] * bins[None, :], sample_count)
    corr = tile_correlation(cc, sc, cf, sf, incoming, slots, sub, n_y, own_rows)

    core = win_here % 2
    y_here = win_here // 2
    send, keep = corr
    keep = keep.astype(jnp.float32)
    got = lax.ppermute(send, "win", [(w, w ^ 1) for w in range(n_win)])
    keep = keep.reshape(LAGS, n_y, own_rows, slot_count * C)
    got = got.reshape(LAGS, n_y, own_rows, slot_count * C)

    def chip_sum(y):
        pick = lambda a: jnp.take(a, y, axis=1, mode="clip")
        return pick(keep) + pick(got).astype(jnp.float32)

    pieces = []
    for shift in range(1, n_y):
        dest = (y_here + shift) % n_y
        perm = [(w, ((w // 2 + shift) % n_y) * 2 + w % 2) for w in range(n_win)]
        pieces.append(lax.ppermute(chip_sum(dest).astype(jnp.bfloat16), "win", perm))
    total = chip_sum(y_here)
    for piece in pieces:
        total = total + piece.astype(jnp.float32)
    total = jnp.transpose(total.reshape(LAGS, own_rows, slot_count, C), (1, 2, 0, 3))

    live_local = tile_live.astype(jnp.float32)
    return total * live_local[None, :, None, None] / math.sqrt(F * window_count * n_win)


def solution(mesh):
    in_specs = (P("win", "pair", None), P(), P("pair"))
    out_specs = P("win", "pair", None, None)
    return jax.shard_map(body, mesh=mesh, in_specs=in_specs, out_specs=out_specs, check_vma=False)
```

```python
import functools
import math

import jax
import jax.numpy as jnp
from jax import lax
from jax.experimental import pallas as pl
from jax.experimental.pallas import tpu as pltpu
from jax.sharding import PartitionSpec as P

C = 128
F = 384
LAGS = 16
DECIM = 32
SPLIT = 128


def cos_sin(product, sample_count):
    angle = 2.0 * math.pi / sample_count * (product % sample_count).astype(jnp.float32)
    return jnp.cos(angle), jnp.sin(angle)


def dft_table(sample_count, bin_count):
    bin_index = lax.iota(jnp.int32, bin_count) + 1
    coarse_count = sample_count // SPLIT
    step = max(g for g in range(1, 11) if coarse_count % g == 0)
    c3, s3 = cos_sin((lax.iota(jnp.int32, coarse_count // step) * step * SPLIT)[:, None] * bin_index[None, :], sample_count)
    c2, s2 = cos_sin((lax.iota(jnp.int32, step) * SPLIT)[:, None] * bin_index[None, :], sample_count)
    ca = (c3[:, None, :] * c2[None, :, :] - s3[:, None, :] * s2[None, :, :]).reshape(coarse_count, bin_count)
    sa = (s3[:, None, :] * c2[None, :, :] + c3[:, None, :] * s2[None, :, :]).reshape(coarse_count, bin_count)
    c1, s1 = cos_sin((lax.iota(jnp.int32, SPLIT // 16) * 16)[:, None] * bin_index[None, :], sample_count)
    c0, s0 = cos_sin(lax.iota(jnp.int32, 16)[:, None] * bin_index[None, :], sample_count)
    cb = (c1[:, None, :] * c0[None, :, :] - s1[:, None, :] * s0[None, :, :]).reshape(SPLIT, bin_count)
    sb = (s1[:, None, :] * c0[None, :, :] + c1[:, None, :] * s0[None, :, :]).reshape(SPLIT, bin_count)
    cos_t = ca[:, None, :] * cb[None, :, :] - sa[:, None, :] * sb[None, :, :]
    sin_t = sa[:, None, :] * cb[None, :, :] + ca[:, None, :] * sb[None, :, :]
    table = jnp.concatenate([cos_t, -sin_t], axis=2).astype(jnp.bfloat16)
    return table.reshape(sample_count, 2 * bin_count)


def whiten_rows(strain_rows, table, bin_count):
    spectrum = jnp.dot(strain_rows, table, preferred_element_type=jnp.float32)
    real_part = spectrum[:, :bin_count]
    imag_part = spectrum[:, bin_count:]
    amplitude = jnp.sqrt(real_part * real_part + imag_part * imag_part)
    level = 0.2 * jnp.mean(amplitude, axis=1, keepdims=True) + 1e-06
    divisor = jnp.maximum(amplitude, level)
    return jnp.concatenate([real_part / divisor, imag_part / divisor], axis=1).astype(jnp.bfloat16)


def correlation_kernel(sub, n_y, own_rows, index_ref, cc_ref, sc_ref, cf_ref, sf_ref, left_ref, right_ref, send_ref, keep_ref):
    window_count = left_ref.shape[1]
    partner = 1 - lax.axis_index("win") % 2
    orders = [[(y * 2 + c) * own_rows for c in (1 - first, first) for y in range(n_y)] for first in (1, 0)]
    acc = None
    for w in range(window_count):
        left = left_ref[0, w].astype(jnp.float32)
        by_order = [jnp.concatenate([left[r : r + own_rows] for r in order], axis=0) for order in orders]
        left = jnp.where(partner == 0, by_order[0], by_order[1])
        lre = left[:, :F]
        lim = left[:, F:]
        rre = right_ref[0, w, :, :F].astype(jnp.float32)
        rim = right_ref[0, w, :, F:].astype(jnp.float32)
        turned = []
        for l1 in range(sub):
            if l1 == 0:
                turned.append(right_ref[0, w])
                continue
            c = cf_ref[l1 : l1 + 1, :]
            s = sf_ref[l1 : l1 + 1, :]
            turned.append(jnp.concatenate([rre * c + rim * s, rim * c - rre * s], axis=1).astype(jnp.bfloat16))
        right_all = jnp.concatenate(turned, axis=0)
        lefts = []
        for l2 in range(LAGS // sub):
            if l2 * sub == LAGS // 2:
                lefts.append(left.astype(jnp.bfloat16))
            else:
                c = cc_ref[l2 : l2 + 1, :]
                s = sc_ref[l2 : l2 + 1, :]
                lefts.append(jnp.concatenate([lre * c - lim * s, lre * s + lim * c], axis=1).astype(jnp.bfloat16))
        res = lax.dot_general(
            jnp.concatenate(lefts, axis=0), right_all, (((1,), (1,)), ((), ())), preferred_element_type=jnp.float32
        )
        acc = res if acc is None else acc + res
    half_rows = C // 2
    for l2 in range(LAGS // sub):
        for l1 in range(sub):
            for part in range(2):
                rows = l2 * C + part * half_rows
                out_ref = (send_ref, keep_ref)[part]
                out_ref[l2 * sub + l1] = acc[rows : rows + half_rows, l1 * C : (l1 + 1) * C].astype(out_ref.dtype)


def tile_correlation(cc, sc, cf, sf, incoming, slots, sub, n_y, own_rows):
    window_count = incoming.shape[1]
    slot_count = slots.shape[0] // 2
    table_spec = pl.BlockSpec(cc.shape, lambda t, idx: (0, 0))
    left_spec = pl.BlockSpec((1, window_count, C, 2 * F), lambda t, idx: (idx[2 * t], 0, 0, 0))
    right_spec = pl.BlockSpec((1, window_count, C, 2 * F), lambda t, idx: (idx[2 * t + 1], 0, 0, 0))
    flops = 2 * slot_count * window_count * C * 2 * F * LAGS * C
    grid_spec = pltpu.PrefetchScalarGridSpec(
        num_scalar_prefetch=1,
        grid=(slot_count,),
        in_specs=[table_spec] * 4 + [left_spec, right_spec],
        out_specs=[pl.BlockSpec((LAGS, C // 2, C), lambda t, idx: (0, 0, t))] * 2,
    )
    return pl.pallas_call(
        functools.partial(correlation_kernel, sub, n_y, own_rows),
        grid_spec=grid_spec,
        out_shape=[jax.ShapeDtypeStruct((LAGS, C // 2, slot_count * C), jnp.bfloat16)] * 2,
        cost_estimate=pl.CostEstimate(
            flops=flops, transcendentals=0, bytes_accessed=slot_count * (4 * window_count * C * F * 2 + 2 * C * LAGS * C)
        ),
    )(slots, cc, sc, cf, sf, incoming, incoming)


def block_choice(lists, group, b_dev):
    return jnp.sum(jnp.where((lists // b_dev) == group, lists % b_dev, 0), axis=1)


def pick_blocks(blocks, choice):
    pick = choice[:, None, None, None]
    out = jnp.broadcast_to(blocks[:, 0][None], choice.shape + blocks[:, 0].shape)
    for k in range(1, blocks.shape[1]):
        out = jnp.where(pick == k, blocks[:, k][None], out)
    return out


def exchange_by_halves(whitened, block_list, lists, groups, pair_here, b_dev):
    n_pair = lists.shape[0]
    half = n_pair // 2
    base = (pair_here // half) * half
    pos = pair_here % half
    across = [(p, p ^ half) for p in range(n_pair)]
    mirror_blocks = jnp.stack([lax.ppermute(block, "pair", across) for block in block_list], axis=1)
    own_choice = block_choice(lists, pair_here, b_dev)
    mirror_choice = block_choice(lists, pair_here ^ half, b_dev)
    arrived_own = []
    arrived_relay = []
    for d in range(half):
        dest = base + (pos + d) % half
        own = pick_blocks(whitened, jnp.take(own_choice, dest[None], mode="clip"))[0]
        relay = pick_blocks(mirror_blocks, jnp.take(mirror_choice, dest[None], mode="clip"))[0]
        if d:
            perm = [(p, (p // half) * half + (p % half + d) % half) for p in range(n_pair)]
            own = lax.ppermute(own, "pair", perm)
            relay = lax.ppermute(relay, "pair", perm)
        arrived_own.append(own)
        arrived_relay.append(relay)
    incoming = jnp.stack(arrived_own + arrived_relay)
    step = (pos - groups % half) % half
    slots = jnp.where(groups // half == pair_here // half, step, half + step)
    return incoming, slots


def body(strain, pair_list, tile_live):
    window_count, local_rows, sample_count = strain.shape
    slot_count = tile_live.shape[0]
    n_pair = lax.axis_size("pair")
    n_win = lax.axis_size("win")
    pair_here = lax.axis_index("pair")
    win_here = lax.axis_index("win")
    b_dev = local_rows // C

    table = dft_table(sample_count, F)
    block_list = [
        whiten_rows(strain[:, k * C : (k + 1) * C].reshape(window_count * C, sample_count), table, F).reshape(
            window_count, C, 2 * F
        )
        for k in range(b_dev)
    ]
    whitened = jnp.stack(block_list, axis=1)

    lists = pair_list.reshape(n_pair, 2 * slot_count)
    wanted = lax.dynamic_slice_in_dim(pair_list, pair_here * slot_count, slot_count, 0)
    groups = wanted.reshape(2 * slot_count) // b_dev
    if n_pair == 8:
        incoming, slots = exchange_by_halves(whitened, block_list, lists, groups, pair_here, b_dev)
    else:
        outgoing = pick_blocks(whitened, block_choice(lists, pair_here, b_dev))
        incoming = lax.all_to_all(outgoing, "pair", 0, 0, tiled=True)
        slots = groups
    slots = jnp.clip(slots, 0, n_pair - 1)

    sub = 4
    own_rows = C // n_win
    n_y = n_win // 2
    bins = lax.iota(jnp.int32, F) + 1
    fine_lag = lax.iota(jnp.int32, sub) * DECIM
    coarse_lag = (lax.iota(jnp.int32, LAGS // sub) * sub - LAGS // 2) * DECIM
    cf, sf = cos_sin(fine_lag[:, None] * bins[None, :], sample_count)
    cc, sc = cos_sin(coarse_lag[:, None] * bins[None, :], sample_count)
    corr = tile_correlation(cc, sc, cf, sf, incoming, slots, sub, n_y, own_rows)

    core = win_here % 2
    y_here = win_here // 2
    send, keep = corr
    keep = keep.astype(jnp.float32)
    got = lax.ppermute(send, "win", [(w, w ^ 1) for w in range(n_win)])
    keep = keep.reshape(LAGS, n_y, own_rows, slot_count * C)
    got = got.reshape(LAGS, n_y, own_rows, slot_count * C)

    def chip_sum(y):
        pick = lambda a: jnp.take(a, y, axis=1, mode="clip")
        return pick(keep) + pick(got).astype(jnp.float32)

    pieces = []
    for shift in range(1, n_y):
        dest = (y_here + shift) % n_y
        perm = [(w, ((w // 2 + shift) % n_y) * 2 + w % 2) for w in range(n_win)]
        pieces.append(lax.ppermute(chip_sum(dest).astype(jnp.bfloat16), "win", perm))
    total = chip_sum(y_here)
    for piece in pieces:
        total = total + piece.astype(jnp.float32)
    total = jnp.transpose(total.reshape(LAGS, own_rows, slot_count, C), (1, 2, 0, 3))

    live_local = tile_live.astype(jnp.float32)
    return total * live_local[None, :, None, None] / math.sqrt(F * window_count * n_win)


def solution(mesh):
    in_specs = (P("win", "pair", None), P(), P("pair"))
    out_specs = P("win", "pair", None, None)
    return jax.shard_map(body, mesh=mesh, in_specs=in_specs, out_specs=out_specs, check_vma=False)
```
